128 devices in a mesh: ev: 32 (over z, x, core), node: 4 (over y).
Axes of the slice: x: 4, y: 4, z: 4, core: 2. Of those that a mesh axis runs over, the one named last changes fastest.
Arguments:
- src_owner: int32 [65536, 1], P(('ev', 'node')), may hold values from 0 to 127; in each aligned block of 512 rows (0 to 511, 512 to 1023, ...) at most 8 rows name the same one
- src_row: int32 [65536], P(('ev', 'node')), may hold values from 0 to 4095
- dst_owner: int32 [65536, 1], P(('ev', 'node')), may hold values from 0 to 127; in each aligned block of 512 rows (0 to 511, 512 to 1023, ...) at most 8 rows name the same one
- dst_row: int32 [65536], P(('ev', 'node')), may hold values from 0 to 4095
- event_time: int32 [65536], P(('ev', 'node')), may hold values from 4096 to 8191
- edge_feat: bfloat16 [65536, 256], P(('ev', 'node')), may hold values from -6 to 6
- memory: bfloat16 [524288, 256], P(('ev', 'node')), may hold values from -3 to 3
- last_update: int32 [524288], P(('ev', 'node')), may hold values from 0 to 4095
- time_freq: float32 [128], replicated, may hold values from 0.0001 to 1
- time_phase: float32 [128], replicated, may hold values from -3.140625 to 3.140625
- w_msg_in: bfloat16 [896, 512], replicated, may hold values from -0.1875 to 0.1875
- b_msg: float32 [512], replicated, may hold values from -3 to 3
- w_msg_out: bfloat16 [512, 256], replicated, may hold values from -0.25 to 0.25
- w_gru_in: bfloat16 [256, 768], replicated, may hold values from -0.375 to 0.375
- b_gru_in: float32 [768], replicated, may hold values from -3 to 3
- w_gru_hid: bfloat16 [256, 768], replicated, may hold values from -0.375 to 0.375
Outputs:
- new_memory: bfloat16 [524288, 256], P(('ev', 'node'))
The draws below stay inside these ranges and needn't reach their ends.
Inputs may be any that keep to these rules, and one draw needn't show every extreme that they name: `src_owner`: within the events of one device (aligned blocks of 512 rows) no owner is named by more than 8 events, a bound that some block reaches. `dst_owner`: within the events of one device (aligned blocks of 512 rows) no owner is named by more than 8 events, a bound that some block reaches. `event_time`: every event is later than the last update of either of its nodes.
All inputs are finite; a program needn't handle non-finite values.
Results may differ from the reference program's by a relative error of at most 0.0021.
Values may be sent and summed in bfloat16 or wider, within the bound.
No kernel may reach another device: no remote copies, remote signals or barrier semaphores. Data moves between devices by JAX's collectives and lax.ppermute only.
A program may use at most 64 MiB of HBM per device.

```python
import math
import jax
import jax.numpy as jnp
import numpy as np

M = 256
TD = 128
FE = 256
HID = 512
MSG = 256
TIME_SPAN = 4096
EV_DEV = 512
ROWS_DEV = 4096
EVENTS = 65536
NODES = 524288
CAP = 8
DEVICES = 128


def with_ends(drawn, stream_key, low, top_value):
    longest = drawn.shape.index(max(drawn.shape))
    spots = []
    for shift in (0, 1):
        where = [jax.random.randint(jax.random.fold_in(stream_key, axis), (), 0, length) for axis, length in enumerate(drawn.shape)]
        where[longest] = (where[longest] + shift) % drawn.shape[longest]
        spots.append(tuple(where))
    return drawn.at[spots[0]].set(low).at[spots[1]].set(top_value)


def block_scale(stream_key, extent, cuts, low, largest):
    level = 1.0
    for position, blocks in cuts:
        steps = jax.random.uniform(jax.random.fold_in(jax.random.fold_in(stream_key, 6), position), (blocks,), jnp.float32, low / len(cuts), largest / len(cuts))
        level = level * jnp.repeat(jnp.exp(steps), extent[position] // blocks).reshape((-1,) + (1,) * (len(extent) - 1 - position))
    return level


def shared_out(own_key, own, number, rows, amount, top, bound, skew):
    sequence = jax.random.permutation(own_key, amount)
    packed, common = shares(amount, rows * top, bound, skew, True), shares(amount, rows * top, bound, skew, False)
    places = jnp.arange(amount)

    def named(lengths, offset_by):
        used = int((lengths > 0).sum())
        fixed = max(1, used // 4)
        moved = fixed + (places - fixed + offset_by * (used - fixed)) % max(1, amount - fixed)
        return jnp.zeros((amount,), jnp.int32).at[sequence[jnp.where(places < fixed, places, moved)]].set(jnp.asarray(lengths, jnp.int32))

    lengths = jnp.where(number % 4 == 0, named(packed, number // 4), named(common, number - number // 4 - 1))
    mixed = jax.random.permutation(jax.random.fold_in(own, 3), amount)
    source_of, taker = mixed[0:amount // 2 * 2:2], mixed[1:amount // 2 * 2:2]
    margin = jnp.minimum(lengths[source_of] - 1, bound - lengths[taker]) // 2
    margin = jnp.where((source_of == sequence[0]) | (taker == sequence[0]) | (lengths[taker] == 0), 0, jnp.maximum(margin, 0))
    moved = jax.random.randint(jax.random.fold_in(own, 4), (amount // 2,), 0, 1 << 20) % (margin + 1)
    lengths = lengths.at[source_of].add(-moved).at[taker].add(moved)
    labels = jnp.searchsorted(jnp.cumsum(lengths), jnp.arange(rows * top), side="right").astype(jnp.int32)
    table = labels.reshape(top, rows).T
    table = table[jax.random.permutation(jax.random.fold_in(own, 1), rows)]
    offset_by = jax.random.randint(jax.random.fold_in(own, 2), (rows, 1), 0, top)
    return jnp.take_along_axis(table, (jnp.arange(top)[None, :] + offset_by) % top, axis=1)


def shares(count, total, reach, skew, full):
    loads = [(1 << 20) // math.isqrt(standing ** skew) + 1 for standing in range(1, count + 1)]
    largest = reach if full else min(reach, max(-(-total // count), total * loads[0] // sum(loads)))
    least = 1 if total - largest >= count - 1 else 0
    counts, spare = [largest] + [least] * (count - 1), total - largest - least * (count - 1)
    while spare > 0:
        movable = [i for i in range(1, count) if counts[i] < largest] or [i for i in range(1, count) if counts[i] < reach]
        mass, budget = sum([loads[i] for i in movable]), spare
        for i in movable:
            more = min(reach - counts[i], max(1, budget * loads[i] // mass), spare)
            counts[i] = counts[i] + more
            spare = spare - more
    return np.array(counts)


def bell_draw(stream_key, shape, scale, reach, cuts=(), held_as=jnp.bfloat16):
    values = jax.random.normal(stream_key, shape, jnp.float32) * scale
    if len(cuts) > 0:
        values = block_scale(stream_key, shape, cuts, -0.22, 0.18) * values
    return jnp.clip(values, min=-reach, max=reach).astype(held_as)


def setup_inputs(seed: int = 0) -> dict:
    seeds = jax.random.split(jax.random.key(seed), 17)
    src_owner_keys = jax.random.split(jax.random.fold_in(seeds[0], 1), EVENTS // EV_DEV)
    src_owner_turns = jax.random.permutation(jax.random.fold_in(seeds[0], 3), EVENTS // EV_DEV)
    src_owner = jax.vmap(lambda own, number: shared_out(jax.random.fold_in(seeds[0], 2), own, number, EV_DEV, DEVICES, 1, CAP, 2))(src_owner_keys, src_owner_turns).reshape((EVENTS, 1))
    src_row = with_ends(jax.random.randint(seeds[1], (EVENTS,), 0, ROWS_DEV), jax.random.fold_in(seeds[1], 1), 0, ROWS_DEV - 1).astype(jnp.int32)
    dst_owner_keys = jax.random.split(jax.random.fold_in(seeds[2], 1), EVENTS // EV_DEV)
    dst_owner_turns = jax.random.permutation(jax.random.fold_in(seeds[2], 3), EVENTS // EV_DEV)
    dst_owner = jax.vmap(lambda own, number: shared_out(jax.random.fold_in(seeds[2], 2), own, number, EV_DEV, DEVICES, 1, CAP, 2))(dst_owner_keys, dst_owner_turns).reshape((EVENTS, 1))
    dst_row = with_ends(jax.random.randint(seeds[3], (EVENTS,), 0, ROWS_DEV), jax.random.fold_in(seeds[3], 1), 0, ROWS_DEV - 1).astype(jnp.int32)
    event_time = with_ends(jax.random.randint(seeds[4], (EVENTS,), TIME_SPAN, 2 * TIME_SPAN), jax.random.fold_in(seeds[4], 1), TIME_SPAN, (2 * TIME_SPAN) - 1).astype(jnp.int32)
    edge_feat = bell_draw(seeds[5], (EVENTS, FE), 1.0, 6.0, ((0, 128),))
    memory = bell_draw(seeds[6], (NODES, M), 0.5, 3.0, ((0, 128),))
    last_update = with_ends(jax.random.randint(seeds[7], (NODES,), 0, TIME_SPAN), jax.random.fold_in(seeds[7], 1), 0, TIME_SPAN - 1).astype(jnp.int32)
    time_freq = jnp.clip(jnp.exp(jax.random.uniform(seeds[8], (TD,), jnp.float32, math.log(0.0001), math.log(1.0))), 0.0001, 1.0)
    time_phase = jnp.clip(jax.random.uniform(seeds[9], (TD,), jnp.float32, -3.140625, 3.140625), -3.140625, 3.140625)
    w_msg_in = bell_draw(seeds[10], (2 * M + TD + FE, HID), (2 * M + TD + FE) ** -0.5, 0.1875)
    b_msg = bell_draw(seeds[11], (HID,), 0.5, 3.0, (), jnp.float32)
    w_msg_out = bell_draw(seeds[12], (HID, MSG), HID ** -0.5, 0.25)
    w_gru_in = bell_draw(seeds[13], (MSG, 3 * M), MSG ** -0.5, 0.375)
    b_gru_in = bell_draw(seeds[14], (3 * M,), 0.5, 3.0, (), jnp.float32)
    w_gru_hid = bell_draw(seeds[15], (M, 3 * M), M ** -0.5, 0.375)
    return {"src_owner": src_owner, "src_row": src_row, "dst_owner": dst_owner, "dst_row": dst_row, "event_time": event_time, "edge_feat": edge_feat, "memory": memory, "last_update": last_update, "time_freq": time_freq, "time_phase": time_phase, "w_msg_in": w_msg_in, "b_msg": b_msg, "w_msg_out": w_msg_out, "w_gru_in": w_gru_in, "b_gru_in": b_gru_in, "w_gru_hid": w_gru_hid}


def encode(delta_int, time_freq, time_phase):
    delta = delta_int.astype(jnp.float32)
    return jnp.cos(delta[..., None] * time_freq + time_phase).astype(jnp.bfloat16)


def gru_update(mean_msg, state, w_gru_in, b_gru_in, w_gru_hid):
    width = state.shape[-1]
    input_part = jnp.dot(mean_msg, w_gru_in, preferred_element_type=jnp.float32) + b_gru_in
    state_part = jnp.dot(state, w_gru_hid, preferred_element_type=jnp.float32)
    reset = jax.nn.sigmoid(input_part[:, :width] + state_part[:, :width])
    update = jax.nn.sigmoid(input_part[:, width:2 * width] + state_part[:, width:2 * width])
    candid = jnp.tanh(input_part[:, 2 * width:] + reset * state_part[:, 2 * width:])
    return ((1.0 - update) * candid + update * state.astype(jnp.float32)).astype(jnp.bfloat16)


def message_net(inputs, w_msg_in, b_msg, w_msg_out):
    hidden = jax.nn.relu(jnp.dot(inputs, w_msg_in, preferred_element_type=jnp.float32) + b_msg).astype(jnp.bfloat16)
    return jnp.dot(hidden, w_msg_out, preferred_element_type=jnp.float32).astype(jnp.bfloat16)


def reference(src_owner, src_row, dst_owner, dst_row, event_time, edge_feat, memory, last_update, time_freq, time_phase, w_msg_in, b_msg, w_msg_out, w_gru_in, b_gru_in, w_gru_hid):
    src_node = (src_owner[:, 0] * ROWS_DEV + src_row).astype(jnp.int32)
    dst_node = (dst_owner[:, 0] * ROWS_DEV + dst_row).astype(jnp.int32)
    mem_src = memory[src_node]
    mem_dst = memory[dst_node]
    enc_src = encode(event_time - last_update[src_node], time_freq, time_phase)
    enc_dst = encode(event_time - last_update[dst_node], time_freq, time_phase)
    msg_src = message_net(jnp.concatenate([mem_src, mem_dst, enc_src, edge_feat], axis=1), w_msg_in, b_msg, w_msg_out)
    msg_dst = message_net(jnp.concatenate([mem_dst, mem_src, enc_dst, edge_feat], axis=1), w_msg_in, b_msg, w_msg_out)
    targets = jnp.concatenate([src_node, dst_node])
    messages = jnp.concatenate([msg_src, msg_dst], axis=0)
    total = jnp.zeros((NODES, messages.shape[1]), jnp.float32).at[targets].add(messages.astype(jnp.float32))
    count = jnp.zeros((NODES,), jnp.int32).at[targets].add(1)
    divisor = jnp.maximum(count[targets], 1).astype(jnp.float32)
    mean_msg = (total[targets] / divisor[:, None]).astype(jnp.bfloat16)
    new_state = gru_update(mean_msg, memory[targets], w_gru_in, b_gru_in, w_gru_hid)
    return memory.at[targets].set(new_state)
```

```python
import jax
import jax.numpy as jnp
from jax import lax
from jax.sharding import PartitionSpec as P


def encode(delta_int, time_freq, time_phase):
    delta = delta_int.astype(jnp.float32)
    return jnp.cos(delta[..., None] * time_freq + time_phase).astype(jnp.bfloat16)


def gru_update(mean_msg, state, w_gru_in, b_gru_in, w_gru_hid):
    width = state.shape[-1]
    input_part = jnp.dot(mean_msg, w_gru_in, preferred_element_type=jnp.float32) + b_gru_in
    state_part = jnp.dot(state, w_gru_hid, preferred_element_type=jnp.float32)
    reset = jax.nn.sigmoid(input_part[:, :width] + state_part[:, :width])
    update = jax.nn.sigmoid(input_part[:, width : 2 * width] + state_part[:, width : 2 * width])
    candid = jnp.tanh(input_part[:, 2 * width :] + reset * state_part[:, 2 * width :])
    return ((1.0 - update) * candid + update * state.astype(jnp.float32)).astype(jnp.bfloat16)


def slot_of(owner_ids, owner_count, capacity):
    events_here = owner_ids.shape[0]
    columns = jnp.arange(owner_count, dtype=jnp.int32)
    onehot = (owner_ids[:, None] == columns[None, :]).astype(jnp.bfloat16)
    order = jnp.arange(events_here, dtype=jnp.int32)
    lower = (order[None, :] < order[:, None]).astype(jnp.bfloat16)
    earlier = jnp.dot(lower, onehot, preferred_element_type=jnp.float32)
    position = jnp.sum(earlier * onehot.astype(jnp.float32), axis=1).astype(jnp.int32)
    return owner_ids * capacity + position


def owner_lookup(request_pair, memory, last_update, time_freq, time_phase):
    row_request = request_pair[0].reshape(-1)
    time_request = request_pair[1].reshape(-1)
    rows_count = memory.shape[0]
    row_range = jnp.arange(rows_count, dtype=jnp.int32)
    select = (row_request[:, None] == row_range[None, :]).astype(jnp.bfloat16)
    high = (last_update // 64).astype(jnp.bfloat16)
    low = (last_update % 64).astype(jnp.bfloat16)
    table = jnp.concatenate([memory, high[:, None], low[:, None]], axis=1)
    fetched = jnp.dot(select, table, preferred_element_type=jnp.float32)
    mem_rows = fetched[:, : memory.shape[1]].astype(jnp.bfloat16)
    stamp = (
        fetched[:, memory.shape[1]].astype(jnp.int32) * 64
        + fetched[:, memory.shape[1] + 1].astype(jnp.int32)
    )
    encoded = encode(time_request - stamp, time_freq, time_phase)
    served = jnp.concatenate([mem_rows, encoded], axis=-1)
    return served.reshape(request_pair.shape[1:] + (served.shape[-1],))


def local(
    src_owner,
    src_row,
    dst_owner,
    dst_row,
    event_time,
    edge_feat,
    memory,
    last_update,
    time_freq,
    time_phase,
    w_msg_in,
    b_msg,
    w_msg_out,
    w_gru_in,
    b_gru_in,
    w_gru_hid,
):
    devices_all = lax.axis_size(("ev", "node"))
    events_here = edge_feat.shape[0]
    capacity = max(2, 2 * events_here // devices_all)
    width = memory.shape[1]
    time_width = time_freq.shape[0]
    hidden_width = w_msg_out.shape[0]
    msg_width = w_msg_out.shape[1]
    rows_count = memory.shape[0]
    slot_total = devices_all * capacity
    slot_ids = jnp.stack(
        [
            slot_of(src_owner[:, 0], devices_all, capacity),
            slot_of(dst_owner[:, 0], devices_all, capacity),
        ]
    )
    slot_range = jnp.arange(slot_total, dtype=jnp.int32)
    placed = slot_ids[:, None, :] == slot_range[None, :, None]
    placement = placed.astype(jnp.bfloat16)
    filled = jnp.any(placed, axis=2)
    rows_pair = jnp.stack([src_row, dst_row])
    row_sum = jnp.sum(jnp.where(placed, rows_pair[:, None, :], 0), axis=2)
    time_sum = jnp.sum(jnp.where(placed, event_time[None, None, :], 0), axis=2)
    row_request = jnp.where(filled, row_sum, -1)
    time_request = jnp.where(filled, time_sum, 0)
    edge_part = (
        jnp.dot(edge_feat, w_msg_in[2 * width + time_width :], preferred_element_type=jnp.float32)
        + b_msg
    )
    request = jnp.stack([row_request, time_request]).reshape((2, 2, devices_all, capacity))
    received = lax.all_to_all(request, ("ev", "node"), split_axis=2, concat_axis=2, tiled=True)
    served = owner_lookup(received, memory, last_update, time_freq, time_phase)
    returned = lax.all_to_all(served, ("ev", "node"), split_axis=1, concat_axis=1, tiled=True)
    rows_held = received[0]
    fetched_flat = returned.reshape(2, slot_total, width + time_width)
    picked = jnp.einsum(
        "kse,ksc->kec", placement, fetched_flat, preferred_element_type=jnp.float32
    ).astype(jnp.bfloat16)
    picked_src = picked[0]
    picked_dst = picked[1]
    mem_stack = jnp.concatenate([picked_src[:, :width], picked_dst[:, :width]], axis=0)
    enc_stack = jnp.concatenate([picked_src[:, width:], picked_dst[:, width:]], axis=0)
    paired_weight = jnp.concatenate([w_msg_in[:width], w_msg_in[width : 2 * width]], axis=1)
    projected = jnp.dot(mem_stack, paired_weight, preferred_element_type=jnp.float32)
    time_term = jnp.dot(
        enc_stack, w_msg_in[2 * width : 2 * width + time_width], preferred_element_type=jnp.float32
    )
    self_term = projected[:, :hidden_width]
    other_term = projected[:, hidden_width:]
    crossed = jnp.concatenate([other_term[events_here:], other_term[:events_here]], axis=0)
    edge_both = jnp.concatenate([edge_part, edge_part], axis=0)
    hidden = jax.nn.relu(self_term + crossed + time_term + edge_both).astype(jnp.bfloat16)
    messages = jnp.dot(hidden, w_msg_out, preferred_element_type=jnp.float32).astype(jnp.bfloat16)
    outgoing = jnp.einsum(
        "kse,kec->ksc",
        placement,
        messages.reshape(2, events_here, msg_width),
        preferred_element_type=jnp.float32,
    ).astype(jnp.bfloat16)
    arrived = lax.all_to_all(
        outgoing.reshape(2, devices_all, capacity, msg_width),
        ("ev", "node"),
        split_axis=1,
        concat_axis=1,
        tiled=True,
    )
    row_flat = rows_held.reshape(-1)
    msg_flat = arrived.reshape(-1, msg_width)
    row_range = jnp.arange(rows_count, dtype=jnp.int32)
    hits = row_range[:, None] == row_flat[None, :]
    total = jnp.dot(hits.astype(jnp.bfloat16), msg_flat, preferred_element_type=jnp.float32)
    count = jnp.sum(hits.astype(jnp.float32), axis=1)
    divisor = jnp.maximum(count, 1.0)
    mean_msg = (total / divisor[:, None]).astype(jnp.bfloat16)
    new_state = gru_update(mean_msg, memory, w_gru_in, b_gru_in, w_gru_hid)
    return jnp.where((count > 0)[:, None], new_state, memory)


def solution(mesh):
    in_specs = (
        P(("ev", "node"), None),
        P(("ev", "node")),
        P(("ev", "node"), None),
        P(("ev", "node")),
        P(("ev", "node")),
        P(("ev", "node"), None),
        P(("ev", "node"), None),
        P(("ev", "node")),
        P(),
        P(),
        P(),
        P(),
        P(),
        P(),
        P(),
        P(),
    )
    out_specs = P(("ev", "node"), None)
    return jax.shard_map(local, mesh=mesh, in_specs=in_specs, out_specs=out_specs, check_vma=False)
```

```python
import jax
import jax.numpy as jnp
from jax import lax
from jax.experimental import pallas as pl
from jax.sharding import PartitionSpec as P


def encode(delta_int, time_freq, time_phase):
    delta = delta_int.astype(jnp.float32)
    return jnp.cos(delta[..., None] * time_freq + time_phase).astype(jnp.bfloat16)


def gru_update(mean_msg, state, w_gru_in, b_gru_in, w_gru_hid):
    width = state.shape[-1]
    input_part = jnp.dot(mean_msg, w_gru_in, preferred_element_type=jnp.float32) + b_gru_in
    state_part = jnp.dot(state, w_gru_hid, preferred_element_type=jnp.float32)
    reset = jax.nn.sigmoid(input_part[:, :width] + state_part[:, :width])
    update = jax.nn.sigmoid(input_part[:, width : 2 * width] + state_part[:, width : 2 * width])
    candid = jnp.tanh(input_part[:, 2 * width :] + reset * state_part[:, 2 * width :])
    return ((1.0 - update) * candid + update * state.astype(jnp.float32)).astype(jnp.bfloat16)


def update_kernel(rows_ref, msg_ref, mem_ref, win_ref, bin_ref, whid_ref, out_ref):
    block = out_ref.shape[0]
    slots = rows_ref.shape[1]
    width = mem_ref.shape[1]
    ids = pl.program_id(0) * block + lax.broadcasted_iota(jnp.int32, (block, slots), 0)
    hit = ids == rows_ref[...]
    total = jnp.dot(hit.astype(jnp.bfloat16), msg_ref[...], preferred_element_type=jnp.float32)
    count = jnp.sum(hit.astype(jnp.float32), axis=1, keepdims=True)
    mean_msg = (total / jnp.maximum(count, 1.0)).astype(jnp.bfloat16)
    state = mem_ref[...]
    input_part = jnp.dot(mean_msg, win_ref[...], preferred_element_type=jnp.float32) + bin_ref[...]
    state_part = jnp.dot(state, whid_ref[...], preferred_element_type=jnp.float32)
    reset = jax.nn.sigmoid(input_part[:, :width] + state_part[:, :width])
    update = jax.nn.sigmoid(input_part[:, width : 2 * width] + state_part[:, width : 2 * width])
    candid = jnp.tanh(input_part[:, 2 * width :] + reset * state_part[:, 2 * width :])
    fresh = (1.0 - update) * candid + update * state.astype(jnp.float32)
    out_ref[...] = jnp.where(count > 0, fresh, state.astype(jnp.float32)).astype(out_ref.dtype)


def owner_update(row_flat, msg_flat, memory, w_gru_in, b_gru_in, w_gru_hid):
    rows_count, width = memory.shape
    slots, msg_width = msg_flat.shape
    block = 512
    gates = w_gru_in.shape[1]
    return pl.pallas_call(
        update_kernel,
        grid=(rows_count // block,),
        in_specs=[
            pl.BlockSpec((1, slots), lambda i: (0, 0)),
            pl.BlockSpec((slots, msg_width), lambda i: (0, 0)),
            pl.BlockSpec((block, width), lambda i: (i, 0)),
            pl.BlockSpec((msg_width, gates), lambda i: (0, 0)),
            pl.BlockSpec((1, gates), lambda i: (0, 0)),
            pl.BlockSpec((width, gates), lambda i: (0, 0)),
        ],
        out_specs=pl.BlockSpec((block, width), lambda i: (i, 0)),
        out_shape=jax.ShapeDtypeStruct(memory.shape, memory.dtype),
    )(row_flat.reshape(1, slots), msg_flat, memory, w_gru_in, b_gru_in.reshape(1, gates), w_gru_hid)


def slot_of(owner_ids, owner_count, capacity):
    events_here = owner_ids.shape[0]
    columns = jnp.arange(owner_count, dtype=jnp.int32)
    onehot = (owner_ids[:, None] == columns[None, :]).astype(jnp.bfloat16)
    order = jnp.arange(events_here, dtype=jnp.int32)
    lower = (order[None, :] < order[:, None]).astype(jnp.bfloat16)
    earlier = jnp.dot(lower, onehot, preferred_element_type=jnp.float32)
    position = jnp.sum(earlier * onehot.astype(jnp.float32), axis=1).astype(jnp.int32)
    return owner_ids * capacity + position


def owner_lookup(request_pair, memory, last_update, time_freq, time_phase):
    row_request = request_pair[0].reshape(-1)
    time_request = request_pair[1].reshape(-1)
    rows_count = memory.shape[0]
    row_range = jnp.arange(rows_count, dtype=jnp.int32)
    select = (row_request[:, None] == row_range[None, :]).astype(jnp.bfloat16)
    high = (last_update // 64).astype(jnp.bfloat16)
    low = (last_update % 64).astype(jnp.bfloat16)
    table = jnp.concatenate([memory, high[:, None], low[:, None]], axis=1)
    fetched = jnp.dot(select, table, preferred_element_type=jnp.float32)
    mem_rows = fetched[:, : memory.shape[1]].astype(jnp.bfloat16)
    stamp = (
        fetched[:, memory.shape[1]].astype(jnp.int32) * 64
        + fetched[:, memory.shape[1] + 1].astype(jnp.int32)
    )
    encoded = encode(time_request - stamp, time_freq, time_phase)
    served = jnp.concatenate([mem_rows, encoded], axis=-1)
    return served.reshape(request_pair.shape[1:] + (served.shape[-1],))


def local(
    src_owner,
    src_row,
    dst_owner,
    dst_row,
    event_time,
    edge_feat,
    memory,
    last_update,
    time_freq,
    time_phase,
    w_msg_in,
    b_msg,
    w_msg_out,
    w_gru_in,
    b_gru_in,
    w_gru_hid,
):
    devices_all = lax.axis_size(("ev", "node"))
    events_here = edge_feat.shape[0]
    capacity = max(2, 2 * events_here // devices_all)
    width = memory.shape[1]
    time_width = time_freq.shape[0]
    hidden_width = w_msg_out.shape[0]
    msg_width = w_msg_out.shape[1]
    rows_count = memory.shape[0]
    slot_total = devices_all * capacity
    slot_ids = jnp.stack(
        [
            slot_of(src_owner[:, 0], devices_all, capacity),
            slot_of(dst_owner[:, 0], devices_all, capacity),
        ]
    )
    slot_range = jnp.arange(slot_total, dtype=jnp.int32)
    placed = slot_ids[:, None, :] == slot_range[None, :, None]
    placement = placed.astype(jnp.bfloat16)
    filled = jnp.any(placed, axis=2)
    rows_pair = jnp.stack([src_row, dst_row])
    row_sum = jnp.sum(jnp.where(placed, rows_pair[:, None, :], 0), axis=2)
    time_sum = jnp.sum(jnp.where(placed, event_time[None, None, :], 0), axis=2)
    row_request = jnp.where(filled, row_sum, -1)
    time_request = jnp.where(filled, time_sum, 0)
    edge_part = (
        jnp.dot(edge_feat, w_msg_in[2 * width + time_width :], preferred_element_type=jnp.float32)
        + b_msg
    )
    request = jnp.stack([row_request, time_request]).reshape((2, 2, devices_all, capacity))
    received = lax.all_to_all(request, ("ev", "node"), split_axis=2, concat_axis=2, tiled=True)
    served = owner_lookup(received, memory, last_update, time_freq, time_phase)
    returned = lax.all_to_all(served, ("ev", "node"), split_axis=1, concat_axis=1, tiled=True)
    rows_held = received[0]
    fetched_flat = returned.reshape(2, slot_total, width + time_width)
    picked = jnp.einsum(
        "kse,ksc->kec", placement, fetched_flat, preferred_element_type=jnp.float32
    ).astype(jnp.bfloat16)
    picked_src = picked[0]
    picked_dst = picked[1]
    mem_stack = jnp.concatenate([picked_src[:, :width], picked_dst[:, :width]], axis=0)
    enc_stack = jnp.concatenate([picked_src[:, width:], picked_dst[:, width:]], axis=0)
    paired_weight = jnp.concatenate([w_msg_in[:width], w_msg_in[width : 2 * width]], axis=1)
    projected = jnp.dot(mem_stack, paired_weight, preferred_element_type=jnp.float32)
    time_term = jnp.dot(
        enc_stack, w_msg_in[2 * width : 2 * width + time_width], preferred_element_type=jnp.float32
    )
    self_term = projected[:, :hidden_width]
    other_term = projected[:, hidden_width:]
    crossed = jnp.concatenate([other_term[events_here:], other_term[:events_here]], axis=0)
    edge_both = jnp.concatenate([edge_part, edge_part], axis=0)
    hidden = jax.nn.relu(self_term + crossed + time_term + edge_both).astype(jnp.bfloat16)
    messages = jnp.dot(hidden, w_msg_out, preferred_element_type=jnp.float32).astype(jnp.bfloat16)
    outgoing = jnp.einsum(
        "kse,kec->ksc",
        placement,
        messages.reshape(2, events_here, msg_width),
        preferred_element_type=jnp.float32,
    ).astype(jnp.bfloat16)
    arrived = lax.all_to_all(
        outgoing.reshape(2, devices_all, capacity, msg_width),
        ("ev", "node"),
        split_axis=1,
        concat_axis=1,
        tiled=True,
    )
    row_flat = rows_held.reshape(-1)
    msg_flat = arrived.reshape(-1, msg_width)
    return owner_update(row_flat, msg_flat, memory, w_gru_in, b_gru_in, w_gru_hid)


def solution(mesh):
    in_specs = (
        P(("ev", "node"), None),
        P(("ev", "node")),
        P(("ev", "node"), None),
        P(("ev", "node")),
        P(("ev", "node")),
        P(("ev", "node"), None),
        P(("ev", "node"), None),
        P(("ev", "node")),
        P(),
        P(),
        P(),
        P(),
        P(),
        P(),
        P(),
        P(),
    )
    out_specs = P(("ev", "node"), None)
    return jax.shard_map(local, mesh=mesh, in_specs=in_specs, out_specs=out_specs, check_vma=False)
```

```python
import jax
import jax.numpy as jnp
from jax import lax
from jax.experimental import pallas as pl
from jax.sharding import PartitionSpec as P


def encode(delta_int, time_freq, time_phase):
    delta = delta_int.astype(jnp.float32)
    return jnp.cos(delta[..., None] * time_freq + time_phase).astype(jnp.bfloat16)


def gru_update(mean_msg, state, w_gru_in, b_gru_in, w_gru_hid):
    width = state.shape[-1]
    input_part = jnp.dot(mean_msg, w_gru_in, preferred_element_type=jnp.float32) + b_gru_in
    state_part = jnp.dot(state, w_gru_hid, preferred_element_type=jnp.float32)
    reset = jax.nn.sigmoid(input_part[:, :width] + state_part[:, :width])
    update = jax.nn.sigmoid(input_part[:, width : 2 * width] + state_part[:, width : 2 * width])
    candid = jnp.tanh(input_part[:, 2 * width :] + reset * state_part[:, 2 * width :])
    return ((1.0 - update) * candid + update * state.astype(jnp.float32)).astype(jnp.bfloat16)


def gate(x):
    return 0.5 + 0.5 * jnp.tanh(0.5 * x)


def update_kernel(rows_ref, msg_ref, mem_ref, win_ref, bin_ref, whid_ref, out_ref):
    block = out_ref.shape[0]
    slots = rows_ref.shape[1]
    width = mem_ref.shape[1]
    ids = pl.program_id(0) * block + lax.broadcasted_iota(jnp.int32, (block, slots), 0)
    onehot = (ids == rows_ref[...]).astype(jnp.bfloat16)
    total = jnp.dot(onehot, msg_ref[...], preferred_element_type=jnp.float32)
    ones = jnp.ones((slots, 128), jnp.bfloat16)
    count = jnp.dot(onehot, ones, preferred_element_type=jnp.float32)[:, :1]
    mean_msg = (total / jnp.maximum(count, 1.0)).astype(jnp.bfloat16)
    state = mem_ref[...]
    input_part = jnp.dot(mean_msg, win_ref[...], preferred_element_type=jnp.float32) + bin_ref[...]
    state_part = jnp.dot(state, whid_ref[...], preferred_element_type=jnp.float32)
    reset = gate(input_part[:, :width] + state_part[:, :width])
    update = gate(input_part[:, width : 2 * width] + state_part[:, width : 2 * width])
    candid = jnp.tanh(input_part[:, 2 * width :] + reset * state_part[:, 2 * width :])
    fresh = (1.0 - update) * candid + update * state.astype(jnp.float32)
    out_ref[...] = jnp.where(count > 0, fresh, state.astype(jnp.float32)).astype(out_ref.dtype)


def owner_update(row_flat, msg_flat, memory, w_gru_in, b_gru_in, w_gru_hid):
    rows_count, width = memory.shape
    slots, msg_width = msg_flat.shape
    block = 1024
    gates = w_gru_in.shape[1]
    return pl.pallas_call(
        update_kernel,
        grid=(rows_count // block,),
        in_specs=[
            pl.BlockSpec((1, slots), lambda i: (0, 0)),
            pl.BlockSpec((slots, msg_width), lambda i: (0, 0)),
            pl.BlockSpec((block, width), lambda i: (i, 0)),
            pl.BlockSpec((msg_width, gates), lambda i: (0, 0)),
            pl.BlockSpec((1, gates), lambda i: (0, 0)),
            pl.BlockSpec((width, gates), lambda i: (0, 0)),
        ],
        out_specs=pl.BlockSpec((block, width), lambda i: (i, 0)),
        out_shape=jax.ShapeDtypeStruct(memory.shape, memory.dtype),
    )(row_flat.reshape(1, slots), msg_flat, memory, w_gru_in, b_gru_in.reshape(1, gates), w_gru_hid)


def slot_of(owner_ids, owner_count, capacity):
    events_here = owner_ids.shape[0]
    columns = jnp.arange(owner_count, dtype=jnp.int32)
    onehot = (owner_ids[:, None] == columns[None, :]).astype(jnp.bfloat16)
    order = jnp.arange(events_here, dtype=jnp.int32)
    lower = (order[None, :] < order[:, None]).astype(jnp.bfloat16)
    earlier = jnp.dot(lower, onehot, preferred_element_type=jnp.float32)
    position = jnp.sum(earlier * onehot.astype(jnp.float32), axis=1).astype(jnp.int32)
    return owner_ids * capacity + position


def owner_lookup(request_pair, memory, last_update, time_freq, time_phase):
    row_request = request_pair[0].reshape(-1)
    time_request = request_pair[1].reshape(-1)
    rows_count = memory.shape[0]
    row_range = jnp.arange(rows_count, dtype=jnp.int32)
    select = (row_request[:, None] == row_range[None, :]).astype(jnp.bfloat16)
    high = (last_update // 64).astype(jnp.bfloat16)
    low = (last_update % 64).astype(jnp.bfloat16)
    table = jnp.concatenate([memory, high[:, None], low[:, None]], axis=1)
    fetched = jnp.dot(select, table, preferred_element_type=jnp.float32)
    mem_rows = fetched[:, : memory.shape[1]].astype(jnp.bfloat16)
    stamp = (
        fetched[:, memory.shape[1]].astype(jnp.int32) * 64
        + fetched[:, memory.shape[1] + 1].astype(jnp.int32)
    )
    encoded = encode(time_request - stamp, time_freq, time_phase)
    served = jnp.concatenate([mem_rows, encoded], axis=-1)
    return served.reshape(request_pair.shape[1:] + (served.shape[-1],))


def local(
    src_owner,
    src_row,
    dst_owner,
    dst_row,
    event_time,
    edge_feat,
    memory,
    last_update,
    time_freq,
    time_phase,
    w_msg_in,
    b_msg,
    w_msg_out,
    w_gru_in,
    b_gru_in,
    w_gru_hid,
):
    devices_all = lax.axis_size(("ev", "node"))
    events_here = edge_feat.shape[0]
    capacity = max(2, 2 * events_here // devices_all)
    width = memory.shape[1]
    time_width = time_freq.shape[0]
    hidden_width = w_msg_out.shape[0]
    msg_width = w_msg_out.shape[1]
    rows_count = memory.shape[0]
    slot_total = devices_all * capacity
    slot_ids = jnp.stack(
        [
            slot_of(src_owner[:, 0], devices_all, capacity),
            slot_of(dst_owner[:, 0], devices_all, capacity),
        ]
    )
    slot_range = jnp.arange(slot_total, dtype=jnp.int32)
    placed = slot_ids[:, None, :] == slot_range[None, :, None]
    placement = placed.astype(jnp.bfloat16)
    filled = jnp.any(placed, axis=2)
    rows_pair = jnp.stack([src_row, dst_row])
    row_sum = jnp.sum(jnp.where(placed, rows_pair[:, None, :], 0), axis=2)
    time_sum = jnp.sum(jnp.where(placed, event_time[None, None, :], 0), axis=2)
    row_request = jnp.where(filled, row_sum, -1)
    time_request = jnp.where(filled, time_sum, 0)
    edge_part = (
        jnp.dot(edge_feat, w_msg_in[2 * width + time_width :], preferred_element_type=jnp.float32)
        + b_msg
    )
    request = jnp.stack([row_request, time_request]).reshape((2, 2, devices_all, capacity))
    received = lax.all_to_all(request, ("ev", "node"), split_axis=2, concat_axis=2, tiled=True)
    served = owner_lookup(received, memory, last_update, time_freq, time_phase)
    returned = lax.all_to_all(served, ("ev", "node"), split_axis=1, concat_axis=1, tiled=True)
    rows_held = received[0]
    fetched_flat = returned.reshape(2, slot_total, width + time_width)
    picked = jnp.einsum(
        "kse,ksc->kec", placement, fetched_flat, preferred_element_type=jnp.float32
    ).astype(jnp.bfloat16)
    picked_src = picked[0]
    picked_dst = picked[1]
    mem_stack = jnp.concatenate([picked_src[:, :width], picked_dst[:, :width]], axis=0)
    enc_stack = jnp.concatenate([picked_src[:, width:], picked_dst[:, width:]], axis=0)
    paired_weight = jnp.concatenate([w_msg_in[:width], w_msg_in[width : 2 * width]], axis=1)
    projected = jnp.dot(mem_stack, paired_weight, preferred_element_type=jnp.float32)
    time_term = jnp.dot(
        enc_stack, w_msg_in[2 * width : 2 * width + time_width], preferred_element_type=jnp.float32
    )
    self_term = projected[:, :hidden_width]
    other_term = projected[:, hidden_width:]
    crossed = jnp.concatenate([other_term[events_here:], other_term[:events_here]], axis=0)
    edge_both = jnp.concatenate([edge_part, edge_part], axis=0)
    hidden = jax.nn.relu(self_term + crossed + time_term + edge_both).astype(jnp.bfloat16)
    messages = jnp.dot(hidden, w_msg_out, preferred_element_type=jnp.float32).astype(jnp.bfloat16)
    outgoing = jnp.einsum(
        "kse,kec->ksc",
        placement,
        messages.reshape(2, events_here, msg_width),
        preferred_element_type=jnp.float32,
    ).astype(jnp.bfloat16)
    arrived = lax.all_to_all(
        outgoing.reshape(2, devices_all, capacity, msg_width),
        ("ev", "node"),
        split_axis=1,
        concat_axis=1,
        tiled=True,
    )
    row_flat = rows_held.reshape(-1)
    msg_flat = arrived.reshape(-1, msg_width)
    return owner_update(row_flat, msg_flat, memory, w_gru_in, b_gru_in, w_gru_hid)


def solution(mesh):
    in_specs = (
        P(("ev", "node"), None),
        P(("ev", "node")),
        P(("ev", "node"), None),
        P(("ev", "node")),
        P(("ev", "node")),
        P(("ev", "node"), None),
        P(("ev", "node"), None),
        P(("ev", "node")),
        P(),
        P(),
        P(),
        P(),
        P(),
        P(),
        P(),
        P(),
    )
    out_specs = P(("ev", "node"), None)
    return jax.shard_map(local, mesh=mesh, in_specs=in_specs, out_specs=out_specs, check_vma=False)
```

```python
import jax
import jax.numpy as jnp
from jax import lax
from jax.experimental import pallas as pl
from jax.sharding import PartitionSpec as P


def encode(delta_int, time_freq, time_phase):
    delta = delta_int.astype(jnp.float32)
    return jnp.cos(delta[..., None] * time_freq + time_phase).astype(jnp.bfloat16)


def gru_update(mean_msg, state, w_gru_in, b_gru_in, w_gru_hid):
    width = state.shape[-1]
    input_part = jnp.dot(mean_msg, w_gru_in, preferred_element_type=jnp.float32) + b_gru_in
    state_part = jnp.dot(state, w_gru_hid, preferred_element_type=jnp.float32)
    reset = jax.nn.sigmoid(input_part[:, :width] + state_part[:, :width])
    update = jax.nn.sigmoid(input_part[:, width : 2 * width] + state_part[:, width : 2 * width])
    candid = jnp.tanh(input_part[:, 2 * width :] + reset * state_part[:, 2 * width :])
    return ((1.0 - update) * candid + update * state.astype(jnp.float32)).astype(jnp.bfloat16)


def gate(x):
    return 0.5 + 0.5 * jnp.tanh(0.5 * x)


def update_kernel(rows_ref, msg_ref, mem_ref, win_ref, bin_ref, whid_ref, out_ref):
    block = out_ref.shape[0]
    slots = rows_ref.shape[1]
    width = mem_ref.shape[1]
    ids = pl.program_id(0) * block + lax.broadcasted_iota(jnp.int32, (block, slots), 0)
    onehot = (ids == rows_ref[...]).astype(jnp.bfloat16)
    total = jnp.dot(onehot, msg_ref[...], preferred_element_type=jnp.float32)
    ones = jnp.ones((slots, 128), jnp.bfloat16)
    count = jnp.dot(onehot, ones, preferred_element_type=jnp.float32)[:, :1]
    mean_msg = (total / jnp.maximum(count, 1.0)).astype(jnp.bfloat16)
    state = mem_ref[...]
    input_part = jnp.dot(mean_msg, win_ref[...], preferred_element_type=jnp.float32) + bin_ref[...]
    state_part = jnp.dot(state, whid_ref[...], preferred_element_type=jnp.float32)
    reset = gate(input_part[:, :width] + state_part[:, :width])
    update = gate(input_part[:, width : 2 * width] + state_part[:, width : 2 * width])
    candid = jnp.tanh(input_part[:, 2 * width :] + reset * state_part[:, 2 * width :])
    fresh = (1.0 - update) * candid + update * state.astype(jnp.float32)
    out_ref[...] = jnp.where(count > 0, fresh, state.astype(jnp.float32)).astype(out_ref.dtype)


def owner_update(row_flat, msg_flat, memory, w_gru_in, b_gru_in, w_gru_hid):
    rows_count, width = memory.shape
    slots, msg_width = msg_flat.shape
    block = 1024
    gates = w_gru_in.shape[1]
    return pl.pallas_call(
        update_kernel,
        grid=(rows_count // block,),
        in_specs=[
            pl.BlockSpec((1, slots), lambda i: (0, 0)),
            pl.BlockSpec((slots, msg_width), lambda i: (0, 0)),
            pl.BlockSpec((block, width), lambda i: (i, 0)),
            pl.BlockSpec((msg_width, gates), lambda i: (0, 0)),
            pl.BlockSpec((1, gates), lambda i: (0, 0)),
            pl.BlockSpec((width, gates), lambda i: (0, 0)),
        ],
        out_specs=pl.BlockSpec((block, width), lambda i: (i, 0)),
        out_shape=jax.ShapeDtypeStruct(memory.shape, memory.dtype),
    )(row_flat.reshape(1, slots), msg_flat, memory, w_gru_in, b_gru_in.reshape(1, gates), w_gru_hid)


def message_kernel(col_ref, row_ref, fetched_ref, edge_ref, w_in_ref, w_out_ref, out_ref):
    events = edge_ref.shape[0]
    slot_total = fetched_ref.shape[1]
    width = out_ref.shape[2]
    time_width = fetched_ref.shape[2] - width
    lane_ids = lax.broadcasted_iota(jnp.int32, (events, slot_total), 1)
    picked = []
    for side in range(2):
        pick = (lane_ids == col_ref[:, side : side + 1]).astype(jnp.bfloat16)
        rows = jnp.dot(pick, fetched_ref[side], preferred_element_type=jnp.float32)
        picked.append(rows.astype(jnp.bfloat16))
    mem_src, enc_src = picked[0][:, :width], picked[0][:, width:]
    mem_dst, enc_dst = picked[1][:, :width], picked[1][:, width:]
    w_self = w_in_ref[:width]
    w_other = w_in_ref[width : 2 * width]
    w_time = w_in_ref[2 * width : 2 * width + time_width]
    edge = edge_ref[...]

    def message(own, other, enc):
        hidden = (
            jnp.dot(own, w_self, preferred_element_type=jnp.float32)
            + jnp.dot(other, w_other, preferred_element_type=jnp.float32)
            + jnp.dot(enc, w_time, preferred_element_type=jnp.float32)
            + edge
        )
        hidden = jnp.maximum(hidden, 0.0).astype(jnp.bfloat16)
        return jnp.dot(hidden, w_out_ref[...], preferred_element_type=jnp.float32).astype(jnp.bfloat16)

    sent = (message(mem_src, mem_dst, enc_src), message(mem_dst, mem_src, enc_dst))
    sub_ids = lax.broadcasted_iota(jnp.int32, (slot_total, events), 0)
    for side in range(2):
        place = (sub_ids == row_ref[side : side + 1, :]).astype(jnp.bfloat16)
        out_ref[side] = jnp.dot(place, sent[side], preferred_element_type=jnp.float32).astype(out_ref.dtype)


def event_messages(slot_ids, fetched, edge_part, w_msg_in, w_msg_out):
    sides, slot_total, fetched_width = fetched.shape
    events, hidden_width = edge_part.shape
    msg_width = w_msg_out.shape[1]
    return pl.pallas_call(
        message_kernel,
        out_shape=jax.ShapeDtypeStruct((sides, slot_total, msg_width), jnp.bfloat16),
    )(slot_ids.T, slot_ids, fetched, edge_part, w_msg_in, w_msg_out)


def slot_of(owner_ids, owner_count, capacity):
    events_here = owner_ids.shape[0]
    columns = jnp.arange(owner_count, dtype=jnp.int32)
    onehot = (owner_ids[:, None] == columns[None, :]).astype(jnp.bfloat16)
    order = jnp.arange(events_here, dtype=jnp.int32)
    lower = (order[None, :] < order[:, None]).astype(jnp.bfloat16)
    earlier = jnp.dot(lower, onehot, preferred_element_type=jnp.float32)
    position = jnp.sum(earlier * onehot.astype(jnp.float32), axis=1).astype(jnp.int32)
    return owner_ids * capacity + position


def owner_lookup(request_pair, memory, last_update, time_freq, time_phase):
    row_request = request_pair[0].reshape(-1)
    time_request = request_pair[1].reshape(-1)
    rows_count = memory.shape[0]
    row_range = jnp.arange(rows_count, dtype=jnp.int32)
    select = (row_request[:, None] == row_range[None, :]).astype(jnp.bfloat16)
    high = (last_update // 64).astype(jnp.bfloat16)
    low = (last_update % 64).astype(jnp.bfloat16)
    table = jnp.concatenate([memory, high[:, None], low[:, None]], axis=1)
    fetched = jnp.dot(select, table, preferred_element_type=jnp.float32)
    mem_rows = fetched[:, : memory.shape[1]].astype(jnp.bfloat16)
    stamp = (
        fetched[:, memory.shape[1]].astype(jnp.int32) * 64
        + fetched[:, memory.shape[1] + 1].astype(jnp.int32)
    )
    encoded = encode(time_request - stamp, time_freq, time_phase)
    served = jnp.concatenate([mem_rows, encoded], axis=-1)
    return served.reshape(request_pair.shape[1:] + (served.shape[-1],))


def local(
    src_owner,
    src_row,
    dst_owner,
    dst_row,
    event_time,
    edge_feat,
    memory,
    last_update,
    time_freq,
    time_phase,
    w_msg_in,
    b_msg,
    w_msg_out,
    w_gru_in,
    b_gru_in,
    w_gru_hid,
):
    devices_all = lax.axis_size(("ev", "node"))
    events_here = edge_feat.shape[0]
    capacity = max(2, 2 * events_here // devices_all)
    width = memory.shape[1]
    time_width = time_freq.shape[0]
    hidden_width = w_msg_out.shape[0]
    msg_width = w_msg_out.shape[1]
    rows_count = memory.shape[0]
    slot_total = devices_all * capacity
    slot_ids = jnp.stack(
        [
            slot_of(src_owner[:, 0], devices_all, capacity),
            slot_of(dst_owner[:, 0], devices_all, capacity),
        ]
    )
    slot_range = jnp.arange(slot_total, dtype=jnp.int32)
    placed = slot_ids[:, None, :] == slot_range[None, :, None]
    placement = placed.astype(jnp.bfloat16)
    filled = jnp.any(placed, axis=2)
    rows_pair = jnp.stack([src_row, dst_row])
    row_sum = jnp.sum(jnp.where(placed, rows_pair[:, None, :], 0), axis=2)
    time_sum = jnp.sum(jnp.where(placed, event_time[None, None, :], 0), axis=2)
    row_request = jnp.where(filled, row_sum, -1)
    time_request = jnp.where(filled, time_sum, 0)
    edge_part = (
        jnp.dot(edge_feat, w_msg_in[2 * width + time_width :], preferred_element_type=jnp.float32)
        + b_msg
    )
    request = jnp.stack([row_request, time_request]).reshape((2, 2, devices_all, capacity))
    received = lax.all_to_all(request, ("ev", "node"), split_axis=2, concat_axis=2, tiled=True)
    served = owner_lookup(received, memory, last_update, time_freq, time_phase)
    returned = lax.all_to_all(served, ("ev", "node"), split_axis=1, concat_axis=1, tiled=True)
    rows_held = received[0]
    fetched_flat = returned.reshape(2, slot_total, width + time_width)
    outgoing = event_messages(slot_ids, fetched_flat, edge_part, w_msg_in, w_msg_out)
    arrived = lax.all_to_all(
        outgoing.reshape(2, devices_all, capacity, msg_width),
        ("ev", "node"),
        split_axis=1,
        concat_axis=1,
        tiled=True,
    )
    row_flat = rows_held.reshape(-1)
    msg_flat = arrived.reshape(-1, msg_width)
    return owner_update(row_flat, msg_flat, memory, w_gru_in, b_gru_in, w_gru_hid)


def solution(mesh):
    in_specs = (
        P(("ev", "node"), None),
        P(("ev", "node")),
        P(("ev", "node"), None),
        P(("ev", "node")),
        P(("ev", "node")),
        P(("ev", "node"), None),
        P(("ev", "node"), None),
        P(("ev", "node")),
        P(),
        P(),
        P(),
        P(),
        P(),
        P(),
        P(),
        P(),
    )
    out_specs = P(("ev", "node"), None)
    return jax.shard_map(local, mesh=mesh, in_specs=in_specs, out_specs=out_specs, check_vma=False)
```

```python
import jax
import jax.numpy as jnp
from jax import lax
from jax.experimental import pallas as pl
from jax.sharding import PartitionSpec as P


def encode(delta_int, time_freq, time_phase):
    delta = delta_int.astype(jnp.float32)
    return jnp.cos(delta[..., None] * time_freq + time_phase).astype(jnp.bfloat16)


def gru_update(mean_msg, state, w_gru_in, b_gru_in, w_gru_hid):
    width = state.shape[-1]
    input_part = jnp.dot(mean_msg, w_gru_in, preferred_element_type=jnp.float32) + b_gru_in
    state_part = jnp.dot(state, w_gru_hid, preferred_element_type=jnp.float32)
    reset = jax.nn.sigmoid(input_part[:, :width] + state_part[:, :width])
    update = jax.nn.sigmoid(input_part[:, width : 2 * width] + state_part[:, width : 2 * width])
    candid = jnp.tanh(input_part[:, 2 * width :] + reset * state_part[:, 2 * width :])
    return ((1.0 - update) * candid + update * state.astype(jnp.float32)).astype(jnp.bfloat16)


def gate(x):
    return 0.5 + 0.5 * jnp.tanh(0.5 * x)


def update_kernel(rows_ref, msg_ref, mem_ref, win_ref, bin_ref, whid_ref, out_ref):
    block = out_ref.shape[0]
    slots = rows_ref.shape[1]
    width = mem_ref.shape[1]
    ids = pl.program_id(0) * block + lax.broadcasted_iota(jnp.int32, (block, slots), 0)
    onehot = (ids == rows_ref[...]).astype(jnp.bfloat16)
    total = jnp.dot(onehot, msg_ref[...], preferred_element_type=jnp.float32)
    ones = jnp.ones((slots, 128), jnp.bfloat16)
    count = jnp.dot(onehot, ones, preferred_element_type=jnp.float32)[:, :1]
    mean_msg = (total / jnp.maximum(count, 1.0)).astype(jnp.bfloat16)
    state = mem_ref[...]
    input_part = jnp.dot(mean_msg, win_ref[...], preferred_element_type=jnp.float32) + bin_ref[...]
    state_part = jnp.dot(state, whid_ref[...], preferred_element_type=jnp.float32)
    reset = gate(input_part[:, :width] + state_part[:, :width])
    update = gate(input_part[:, width : 2 * width] + state_part[:, width : 2 * width])
    candid = jnp.tanh(input_part[:, 2 * width :] + reset * state_part[:, 2 * width :])
    fresh = (1.0 - update) * candid + update * state.astype(jnp.float32)
    out_ref[...] = jnp.where(count > 0, fresh, state.astype(jnp.float32)).astype(out_ref.dtype)


def owner_update(row_flat, msg_flat, memory, w_gru_in, b_gru_in, w_gru_hid):
    rows_count, width = memory.shape
    slots, msg_width = msg_flat.shape
    block = 1024
    gates = w_gru_in.shape[1]
    return pl.pallas_call(
        update_kernel,
        grid=(rows_count // block,),
        in_specs=[
            pl.BlockSpec((1, slots), lambda i: (0, 0)),
            pl.BlockSpec((slots, msg_width), lambda i: (0, 0)),
            pl.BlockSpec((block, width), lambda i: (i, 0)),
            pl.BlockSpec((msg_width, gates), lambda i: (0, 0)),
            pl.BlockSpec((1, gates), lambda i: (0, 0)),
            pl.BlockSpec((width, gates), lambda i: (0, 0)),
        ],
        out_specs=pl.BlockSpec((block, width), lambda i: (i, 0)),
        out_shape=jax.ShapeDtypeStruct(memory.shape, memory.dtype),
    )(row_flat.reshape(1, slots), msg_flat, memory, w_gru_in, b_gru_in.reshape(1, gates), w_gru_hid)


def message_kernel(col_ref, row_ref, fetched_ref, edge_ref, w_in_ref, w_out_ref, out_ref):
    events = edge_ref.shape[0]
    slot_total = fetched_ref.shape[0]
    width = out_ref.shape[1]
    time_width = fetched_ref.shape[1] - width
    lane_ids = lax.broadcasted_iota(jnp.int32, (events, slot_total), 1)
    picked = []
    for side in range(2):
        pick = (lane_ids == col_ref[:, side : side + 1]).astype(jnp.bfloat16)
        rows = jnp.dot(pick, fetched_ref[...], preferred_element_type=jnp.float32)
        picked.append(rows.astype(jnp.bfloat16))
    mem_src, enc_src = picked[0][:, :width], picked[0][:, width:]
    mem_dst, enc_dst = picked[1][:, :width], picked[1][:, width:]
    w_self = w_in_ref[:width]
    w_other = w_in_ref[width : 2 * width]
    w_time = w_in_ref[2 * width : 2 * width + time_width]
    edge = edge_ref[...]

    def message(own, other, enc):
        hidden = (
            jnp.dot(own, w_self, preferred_element_type=jnp.float32)
            + jnp.dot(other, w_other, preferred_element_type=jnp.float32)
            + jnp.dot(enc, w_time, preferred_element_type=jnp.float32)
            + edge
        )
        hidden = jnp.maximum(hidden, 0.0).astype(jnp.bfloat16)
        return jnp.dot(hidden, w_out_ref[...], preferred_element_type=jnp.float32).astype(jnp.bfloat16)

    sent = (message(mem_src, mem_dst, enc_src), message(mem_dst, mem_src, enc_dst))
    sub_ids = lax.broadcasted_iota(jnp.int32, (slot_total, events), 0)
    placed = [(sub_ids == row_ref[side : side + 1, :]).astype(jnp.bfloat16) for side in range(2)]
    out = jnp.dot(placed[0], sent[0], preferred_element_type=jnp.float32)
    out = out + jnp.dot(placed[1], sent[1], preferred_element_type=jnp.float32)
    out_ref[...] = out.astype(out_ref.dtype)


def event_messages(slot_ids, fetched, edge_part, w_msg_in, w_msg_out):
    slot_total = fetched.shape[0]
    msg_width = w_msg_out.shape[1]
    return pl.pallas_call(
        message_kernel,
        out_shape=jax.ShapeDtypeStruct((slot_total, msg_width), jnp.bfloat16),
    )(slot_ids.T, slot_ids, fetched, edge_part, w_msg_in, w_msg_out)


def slot_of(owner_ids, owner_count, capacity):
    events_here = owner_ids.shape[0]
    columns = jnp.arange(owner_count, dtype=jnp.int32)
    onehot = (owner_ids[:, None] == columns[None, :]).astype(jnp.bfloat16)
    order = jnp.arange(events_here, dtype=jnp.int32)
    lower = (order[None, :] < order[:, None]).astype(jnp.bfloat16)
    earlier = jnp.dot(lower, onehot, preferred_element_type=jnp.float32)
    position = jnp.sum(earlier * onehot.astype(jnp.float32), axis=1).astype(jnp.int32)
    return owner_ids * capacity + position


def owner_lookup(row_request, time_request, memory, last_update, time_freq, time_phase):
    rows_count, width = memory.shape
    row_range = jnp.arange(rows_count, dtype=jnp.int32)
    select = (row_request[:, None] == row_range[None, :]).astype(jnp.bfloat16)
    high = (last_update // 64).astype(jnp.bfloat16)
    low = (last_update % 64).astype(jnp.bfloat16)
    table = jnp.concatenate([memory, high[:, None], low[:, None]], axis=1)
    fetched = jnp.dot(select, table, preferred_element_type=jnp.float32)
    mem_rows = fetched[:, :width].astype(jnp.bfloat16)
    stamp = fetched[:, width].astype(jnp.int32) * 64 + fetched[:, width + 1].astype(jnp.int32)
    encoded = encode(time_request - stamp, time_freq, time_phase)
    return jnp.concatenate([mem_rows, encoded], axis=-1)


def local(
    src_owner,
    src_row,
    dst_owner,
    dst_row,
    event_time,
    edge_feat,
    memory,
    last_update,
    time_freq,
    time_phase,
    w_msg_in,
    b_msg,
    w_msg_out,
    w_gru_in,
    b_gru_in,
    w_gru_hid,
):
    devices_all = lax.axis_size(("ev", "node"))
    events_here = edge_feat.shape[0]
    capacity = max(2, 2 * events_here // devices_all)
    chunk = 2 * capacity
    width = memory.shape[1]
    time_width = time_freq.shape[0]
    slot_total = devices_all * chunk
    slot_ids = jnp.stack(
        [
            slot_of(src_owner[:, 0], devices_all, chunk),
            slot_of(dst_owner[:, 0], devices_all, chunk) + capacity,
        ]
    )
    slot_all = slot_ids.reshape(-1)
    rows_all = jnp.concatenate([src_row, dst_row])
    times_all = jnp.concatenate([event_time, event_time])
    digits = jnp.stack(
        [rows_all // 64, rows_all % 64, times_all // 64, times_all % 64, jnp.ones_like(rows_all)],
        axis=1,
    ).astype(jnp.bfloat16)
    slot_range = jnp.arange(slot_total, dtype=jnp.int32)
    placed = (slot_range[:, None] == slot_all[None, :]).astype(jnp.bfloat16)
    gathered = jnp.dot(placed, digits, preferred_element_type=jnp.float32).astype(jnp.int32)
    filled = gathered[:, 4] > 0
    row_request = jnp.where(filled, gathered[:, 0] * 64 + gathered[:, 1], -1)
    time_request = gathered[:, 2] * 64 + gathered[:, 3]
    request = jnp.stack([row_request, time_request]).reshape(2, devices_all, chunk)
    request = request.transpose(1, 0, 2)
    edge_part = (
        jnp.dot(edge_feat, w_msg_in[2 * width + time_width :], preferred_element_type=jnp.float32)
        + b_msg
    )
    received = lax.all_to_all(request, ("ev", "node"), split_axis=0, concat_axis=0, tiled=True)
    rows_held = received[:, 0, :].reshape(-1)
    times_held = received[:, 1, :].reshape(-1)
    served = owner_lookup(rows_held, times_held, memory, last_update, time_freq, time_phase)
    returned = lax.all_to_all(served, ("ev", "node"), split_axis=0, concat_axis=0, tiled=True)
    outgoing = event_messages(slot_ids, returned, edge_part, w_msg_in, w_msg_out)
    arrived = lax.all_to_all(outgoing, ("ev", "node"), split_axis=0, concat_axis=0, tiled=True)
    return owner_update(rows_held, arrived, memory, w_gru_in, b_gru_in, w_gru_hid)


def solution(mesh):
    in_specs = (
        P(("ev", "node"), None),
        P(("ev", "node")),
        P(("ev", "node"), None),
        P(("ev", "node")),
        P(("ev", "node")),
        P(("ev", "node"), None),
        P(("ev", "node"), None),
        P(("ev", "node")),
        P(),
        P(),
        P(),
        P(),
        P(),
        P(),
        P(),
        P(),
    )
    out_specs = P(("ev", "node"), None)
    return jax.shard_map(local, mesh=mesh, in_specs=in_specs, out_specs=out_specs, check_vma=False)
```

```python
import jax
import jax.numpy as jnp
from jax import lax
from jax.experimental import pallas as pl
from jax.sharding import PartitionSpec as P


def encode(delta_int, time_freq, time_phase):
    delta = delta_int.astype(jnp.float32)
    return jnp.cos(delta[..., None] * time_freq + time_phase).astype(jnp.bfloat16)


def gru_update(mean_msg, state, w_gru_in, b_gru_in, w_gru_hid):
    width = state.shape[-1]
    input_part = jnp.dot(mean_msg, w_gru_in, preferred_element_type=jnp.float32) + b_gru_in
    state_part = jnp.dot(state, w_gru_hid, preferred_element_type=jnp.float32)
    reset = jax.nn.sigmoid(input_part[:, :width] + state_part[:, :width])
    update = jax.nn.sigmoid(input_part[:, width : 2 * width] + state_part[:, width : 2 * width])
    candid = jnp.tanh(input_part[:, 2 * width :] + reset * state_part[:, 2 * width :])
    return ((1.0 - update) * candid + update * state.astype(jnp.float32)).astype(jnp.bfloat16)


def gate(x):
    return 0.5 + 0.5 * jnp.tanh(0.5 * x)


def onehot_kernel(rows_ref, onehot_ref, count_ref):
    block, slots = onehot_ref.shape
    ids = pl.program_id(0) * block + lax.broadcasted_iota(jnp.int32, (block, slots), 0)
    hit = ids == rows_ref[...]
    onehot_ref[...] = hit.astype(onehot_ref.dtype)
    count_ref[...] = jnp.sum(hit.astype(jnp.float32), axis=1, keepdims=True)


def update_kernel(onehot_ref, count_ref, msg_ref, mem_ref, win_ref, bin_ref, whid_ref, out_ref):
    width = mem_ref.shape[1]
    total = jnp.dot(onehot_ref[...], msg_ref[...], preferred_element_type=jnp.float32)
    count = count_ref[...]
    mean_msg = (total / jnp.maximum(count, 1.0)).astype(jnp.bfloat16)
    state = mem_ref[...]
    input_part = jnp.dot(mean_msg, win_ref[...], preferred_element_type=jnp.float32) + bin_ref[...]
    state_part = jnp.dot(state, whid_ref[...], preferred_element_type=jnp.float32)
    reset = gate(input_part[:, :width] + state_part[:, :width])
    update = gate(input_part[:, width : 2 * width] + state_part[:, width : 2 * width])
    candid = jnp.tanh(input_part[:, 2 * width :] + reset * state_part[:, 2 * width :])
    fresh = (1.0 - update) * candid + update * state.astype(jnp.float32)
    out_ref[...] = jnp.where(count > 0, fresh, state.astype(jnp.float32)).astype(out_ref.dtype)


def row_onehot(row_flat, rows_count):
    slots = row_flat.shape[0]
    block = 512
    return pl.pallas_call(
        onehot_kernel,
        grid=(rows_count // block,),
        in_specs=[pl.BlockSpec((1, slots), lambda i: (0, 0))],
        out_specs=[
            pl.BlockSpec((block, slots), lambda i: (i, 0)),
            pl.BlockSpec((block, 1), lambda i: (i, 0)),
        ],
        out_shape=[
            jax.ShapeDtypeStruct((rows_count, slots), jnp.bfloat16),
            jax.ShapeDtypeStruct((rows_count, 1), jnp.float32),
        ],
        cost_estimate=pl.CostEstimate(
            flops=4 * rows_count * slots, transcendentals=0, bytes_accessed=2 * rows_count * slots
        ),
    )(row_flat.reshape(1, slots))


def owner_update(onehot, count, msg_flat, memory, w_gru_in, b_gru_in, w_gru_hid):
    rows_count, width = memory.shape
    slots, msg_width = msg_flat.shape
    block = 1024
    gates = w_gru_in.shape[1]
    return pl.pallas_call(
        update_kernel,
        grid=(rows_count // block,),
        in_specs=[
            pl.BlockSpec((block, slots), lambda i: (i, 0)),
            pl.BlockSpec((block, 1), lambda i: (i, 0)),
            pl.BlockSpec((slots, msg_width), lambda i: (0, 0)),
            pl.BlockSpec((block, width), lambda i: (i, 0)),
            pl.BlockSpec((msg_width, gates), lambda i: (0, 0)),
            pl.BlockSpec((1, gates), lambda i: (0, 0)),
            pl.BlockSpec((width, gates), lambda i: (0, 0)),
        ],
        out_specs=pl.BlockSpec((block, width), lambda i: (i, 0)),
        out_shape=jax.ShapeDtypeStruct(memory.shape, memory.dtype),
    )(onehot, count, msg_flat, memory, w_gru_in, b_gru_in.reshape(1, gates), w_gru_hid)


def message_kernel(col_ref, row_ref, fetched_ref, edge_ref, w_in_ref, w_out_ref, out_ref):
    events = edge_ref.shape[0]
    slot_total = fetched_ref.shape[0]
    width = out_ref.shape[1]
    time_width = fetched_ref.shape[1] - width
    lane_ids = lax.broadcasted_iota(jnp.int32, (events, slot_total), 1)
    picked = []
    for side in range(2):
        pick = (lane_ids == col_ref[:, side : side + 1]).astype(jnp.bfloat16)
        rows = jnp.dot(pick, fetched_ref[...], preferred_element_type=jnp.float32)
        picked.append(rows.astype(jnp.bfloat16))
    mem_src, enc_src = picked[0][:, :width], picked[0][:, width:]
    mem_dst, enc_dst = picked[1][:, :width], picked[1][:, width:]
    w_self = w_in_ref[:width]
    w_other = w_in_ref[width : 2 * width]
    w_time = w_in_ref[2 * width : 2 * width + time_width]
    edge = edge_ref[...]

    def message(own, other, enc):
        hidden = (
            jnp.dot(own, w_self, preferred_element_type=jnp.float32)
            + jnp.dot(other, w_other, preferred_element_type=jnp.float32)
            + jnp.dot(enc, w_time, preferred_element_type=jnp.float32)
            + edge
        )
        hidden = jnp.maximum(hidden, 0.0).astype(jnp.bfloat16)
        return jnp.dot(hidden, w_out_ref[...], preferred_element_type=jnp.float32).astype(jnp.bfloat16)

    sent = (message(mem_src, mem_dst, enc_src), message(mem_dst, mem_src, enc_dst))
    sub_ids = lax.broadcasted_iota(jnp.int32, (slot_total, events), 0)
    placed = [(sub_ids == row_ref[side : side + 1, :]).astype(jnp.bfloat16) for side in range(2)]
    out = jnp.dot(placed[0], sent[0], preferred_element_type=jnp.float32)
    out = out + jnp.dot(placed[1], sent[1], preferred_element_type=jnp.float32)
    out_ref[...] = out.astype(out_ref.dtype)


def event_messages(slot_ids, fetched, edge_part, w_msg_in, w_msg_out):
    slot_total = fetched.shape[0]
    msg_width = w_msg_out.shape[1]
    return pl.pallas_call(
        message_kernel,
        out_shape=jax.ShapeDtypeStruct((slot_total, msg_width), jnp.bfloat16),
    )(slot_ids.T, slot_ids, fetched, edge_part, w_msg_in, w_msg_out)


def slot_of(owner_ids, owner_count, capacity):
    events_here = owner_ids.shape[0]
    columns = jnp.arange(owner_count, dtype=jnp.int32)
    onehot = (owner_ids[:, None] == columns[None, :]).astype(jnp.bfloat16)
    order = jnp.arange(events_here, dtype=jnp.int32)
    lower = (order[None, :] < order[:, None]).astype(jnp.bfloat16)
    earlier = jnp.dot(lower, onehot, preferred_element_type=jnp.float32)
    position = jnp.sum(earlier * onehot.astype(jnp.float32), axis=1).astype(jnp.int32)
    return owner_ids * capacity + position


def owner_lookup(row_request, time_request, memory, last_update, time_freq, time_phase):
    rows_count, width = memory.shape
    row_range = jnp.arange(rows_count, dtype=jnp.int32)
    select = (row_request[:, None] == row_range[None, :]).astype(jnp.bfloat16)
    high = (last_update // 64).astype(jnp.bfloat16)
    low = (last_update % 64).astype(jnp.bfloat16)
    table = jnp.concatenate([memory, high[:, None], low[:, None]], axis=1)
    fetched = jnp.dot(select, table, preferred_element_type=jnp.float32)
    mem_rows = fetched[:, :width].astype(jnp.bfloat16)
    stamp = fetched[:, width].astype(jnp.int32) * 64 + fetched[:, width + 1].astype(jnp.int32)
    encoded = encode(time_request - stamp, time_freq, time_phase)
    return jnp.concatenate([mem_rows, encoded], axis=-1)


def local(
    src_owner,
    src_row,
    dst_owner,
    dst_row,
    event_time,
    edge_feat,
    memory,
    last_update,
    time_freq,
    time_phase,
    w_msg_in,
    b_msg,
    w_msg_out,
    w_gru_in,
    b_gru_in,
    w_gru_hid,
):
    devices_all = lax.axis_size(("ev", "node"))
    events_here = edge_feat.shape[0]
    capacity = max(2, 2 * events_here // devices_all)
    chunk = 2 * capacity
    width = memory.shape[1]
    time_width = time_freq.shape[0]
    slot_total = devices_all * chunk
    slot_ids = jnp.stack(
        [
            slot_of(src_owner[:, 0], devices_all, chunk),
            slot_of(dst_owner[:, 0], devices_all, chunk) + capacity,
        ]
    )
    slot_all = slot_ids.reshape(-1)
    rows_all = jnp.concatenate([src_row, dst_row])
    times_all = jnp.concatenate([event_time, event_time])
    digits = jnp.stack(
        [rows_all // 64, rows_all % 64, times_all // 64, times_all % 64, jnp.ones_like(rows_all)],
        axis=1,
    ).astype(jnp.bfloat16)
    slot_range = jnp.arange(slot_total, dtype=jnp.int32)
    placed = (slot_range[:, None] == slot_all[None, :]).astype(jnp.bfloat16)
    gathered = jnp.dot(placed, digits, preferred_element_type=jnp.float32).astype(jnp.int32)
    filled = gathered[:, 4] > 0
    row_request = jnp.where(filled, gathered[:, 0] * 64 + gathered[:, 1], -1)
    time_request = gathered[:, 2] * 64 + gathered[:, 3]
    request = jnp.stack([row_request, time_request]).reshape(2, devices_all, chunk)
    request = request.transpose(1, 0, 2)
    edge_part = (
        jnp.dot(edge_feat, w_msg_in[2 * width + time_width :], preferred_element_type=jnp.float32)
        + b_msg
    )
    received = lax.all_to_all(request, ("ev", "node"), split_axis=0, concat_axis=0, tiled=True)
    rows_held = received[:, 0, :].reshape(-1)
    times_held = received[:, 1, :].reshape(-1)
    served = owner_lookup(rows_held, times_held, memory, last_update, time_freq, time_phase)
    returned = lax.all_to_all(served, ("ev", "node"), split_axis=0, concat_axis=0, tiled=True)
    onehot, count = row_onehot(rows_held, memory.shape[0])
    outgoing = event_messages(slot_ids, returned, edge_part, w_msg_in, w_msg_out)
    arrived = lax.all_to_all(outgoing, ("ev", "node"), split_axis=0, concat_axis=0, tiled=True)
    return owner_update(onehot, count, arrived, memory, w_gru_in, b_gru_in, w_gru_hid)


def solution(mesh):
    in_specs = (
        P(("ev", "node"), None),
        P(("ev", "node")),
        P(("ev", "node"), None),
        P(("ev", "node")),
        P(("ev", "node")),
        P(("ev", "node"), None),
        P(("ev", "node"), None),
        P(("ev", "node")),
        P(),
        P(),
        P(),
        P(),
        P(),
        P(),
        P(),
        P(),
    )
    out_specs = P(("ev", "node"), None)
    return jax.shard_map(local, mesh=mesh, in_specs=in_specs, out_specs=out_specs, check_vma=False)
```

```python
import jax
import jax.numpy as jnp
from jax import lax
from jax.experimental import pallas as pl
from jax.sharding import PartitionSpec as P


def encode(delta_int, time_freq, time_phase):
    delta = delta_int.astype(jnp.float32)
    return jnp.cos(delta[..., None] * time_freq + time_phase).astype(jnp.bfloat16)


def gru_update(mean_msg, state, w_gru_in, b_gru_in, w_gru_hid):
    width = state.shape[-1]
    input_part = jnp.dot(mean_msg, w_gru_in, preferred_element_type=jnp.float32) + b_gru_in
    state_part = jnp.dot(state, w_gru_hid, preferred_element_type=jnp.float32)
    reset = jax.nn.sigmoid(input_part[:, :width] + state_part[:, :width])
    update = jax.nn.sigmoid(input_part[:, width : 2 * width] + state_part[:, width : 2 * width])
    candid = jnp.tanh(input_part[:, 2 * width :] + reset * state_part[:, 2 * width :])
    return ((1.0 - update) * candid + update * state.astype(jnp.float32)).astype(jnp.bfloat16)


def gate(x):
    return 0.5 + 0.5 * jnp.tanh(0.5 * x)


def update_kernel(rows_ref, msg_ref, mem_ref, win_ref, bin_ref, whid_ref, out_ref):
    block = out_ref.shape[0]
    slots = rows_ref.shape[1]
    width = mem_ref.shape[1]
    ids = pl.program_id(0) * block + lax.broadcasted_iota(jnp.int32, (block, slots), 0)
    onehot = (ids == rows_ref[...]).astype(jnp.bfloat16)
    total = jnp.dot(onehot, msg_ref[...], preferred_element_type=jnp.float32)
    ones = jnp.ones((slots, 128), jnp.bfloat16)
    count = jnp.dot(onehot, ones, preferred_element_type=jnp.float32)[:, :1]
    mean_msg = (total / jnp.maximum(count, 1.0)).astype(jnp.bfloat16)
    state = mem_ref[...]
    input_part = jnp.dot(mean_msg, win_ref[...], preferred_element_type=jnp.float32) + bin_ref[...]
    state_part = jnp.dot(state, whid_ref[...], preferred_element_type=jnp.float32)
    reset = gate(input_part[:, :width] + state_part[:, :width])
    update = gate(input_part[:, width : 2 * width] + state_part[:, width : 2 * width])
    candid = jnp.tanh(input_part[:, 2 * width :] + reset * state_part[:, 2 * width :])
    fresh = (1.0 - update) * candid + update * state.astype(jnp.float32)
    out_ref[...] = jnp.where(count > 0, fresh, state.astype(jnp.float32)).astype(out_ref.dtype)


def owner_update(row_flat, msg_flat, memory, w_gru_in, b_gru_in, w_gru_hid):
    rows_count, width = memory.shape
    slots, msg_width = msg_flat.shape
    block = 1024
    gates = w_gru_in.shape[1]
    return pl.pallas_call(
        update_kernel,
        grid=(rows_count // block,),
        in_specs=[
            pl.BlockSpec((1, slots), lambda i: (0, 0)),
            pl.BlockSpec((slots, msg_width), lambda i: (0, 0)),
            pl.BlockSpec((block, width), lambda i: (i, 0)),
            pl.BlockSpec((msg_width, gates), lambda i: (0, 0)),
            pl.BlockSpec((1, gates), lambda i: (0, 0)),
            pl.BlockSpec((width, gates), lambda i: (0, 0)),
        ],
        out_specs=pl.BlockSpec((block, width), lambda i: (i, 0)),
        out_shape=jax.ShapeDtypeStruct(memory.shape, memory.dtype),
    )(row_flat.reshape(1, slots), msg_flat, memory, w_gru_in, b_gru_in.reshape(1, gates), w_gru_hid)


def message_kernel(col_ref, row_ref, fetched_ref, edge_ref, w_in_ref, w_out_ref, out_ref):
    events = edge_ref.shape[0]
    slot_total = fetched_ref.shape[0]
    width = out_ref.shape[1]
    time_width = fetched_ref.shape[1] - width
    lane_ids = lax.broadcasted_iota(jnp.int32, (events, slot_total), 1)
    picked = []
    for side in range(2):
        pick = (lane_ids == col_ref[:, side : side + 1]).astype(jnp.bfloat16)
        rows = jnp.dot(pick, fetched_ref[...], preferred_element_type=jnp.float32)
        picked.append(rows.astype(jnp.bfloat16))
    mem_src, enc_src = picked[0][:, :width], picked[0][:, width:]
    mem_dst, enc_dst = picked[1][:, :width], picked[1][:, width:]
    w_self = w_in_ref[:width]
    w_other = w_in_ref[width : 2 * width]
    w_time = w_in_ref[2 * width : 2 * width + time_width]
    edge = edge_ref[...]

    def message(own, other, enc):
        hidden = (
            jnp.dot(own, w_self, preferred_element_type=jnp.float32)
            + jnp.dot(other, w_other, preferred_element_type=jnp.float32)
            + jnp.dot(enc, w_time, preferred_element_type=jnp.float32)
            + edge
        )
        hidden = jnp.maximum(hidden, 0.0).astype(jnp.bfloat16)
        return jnp.dot(hidden, w_out_ref[...], preferred_element_type=jnp.float32).astype(jnp.bfloat16)

    sent = (message(mem_src, mem_dst, enc_src), message(mem_dst, mem_src, enc_dst))
    sub_ids = lax.broadcasted_iota(jnp.int32, (slot_total, events), 0)
    placed = [(sub_ids == row_ref[side : side + 1, :]).astype(jnp.bfloat16) for side in range(2)]
    out = jnp.dot(placed[0], sent[0], preferred_element_type=jnp.float32)
    out = out + jnp.dot(placed[1], sent[1], preferred_element_type=jnp.float32)
    out_ref[...] = out.astype(out_ref.dtype)


def event_messages(slot_ids, fetched, edge_part, w_msg_in, w_msg_out):
    slot_total = fetched.shape[0]
    msg_width = w_msg_out.shape[1]
    return pl.pallas_call(
        message_kernel,
        out_shape=jax.ShapeDtypeStruct((slot_total, msg_width), jnp.bfloat16),
    )(slot_ids.T, slot_ids, fetched, edge_part, w_msg_in, w_msg_out)


def slot_of(owner_ids, owner_count, capacity):
    events_here = owner_ids.shape[0]
    columns = jnp.arange(owner_count, dtype=jnp.int32)
    onehot = (owner_ids[:, None] == columns[None, :]).astype(jnp.bfloat16)
    order = jnp.arange(events_here, dtype=jnp.int32)
    lower = (order[None, :] < order[:, None]).astype(jnp.bfloat16)
    earlier = jnp.dot(lower, onehot, preferred_element_type=jnp.float32)
    position = jnp.sum(earlier * onehot.astype(jnp.float32), axis=1).astype(jnp.int32)
    return owner_ids * capacity + position


def lookup_kernel(rows_ref, times_ref, mem_ref, digits_ref, freq_ref, phase_ref, out_ref):
    block = out_ref.shape[0]
    rows_count, width = mem_ref.shape
    lanes = lax.broadcasted_iota(jnp.int32, (block, rows_count), 1)
    select = (lanes == rows_ref[...]).astype(jnp.bfloat16)
    mem_rows = jnp.dot(select, mem_ref[...], preferred_element_type=jnp.float32)
    parts = jnp.dot(select, digits_ref[...], preferred_element_type=jnp.float32)
    stamp = parts[:, 0:1].astype(jnp.int32) * 64 + parts[:, 1:2].astype(jnp.int32)
    delta = (times_ref[...] - stamp).astype(jnp.float32)
    encoded = jnp.cos(delta * freq_ref[...] + phase_ref[...])
    out_ref[:, :width] = mem_rows.astype(out_ref.dtype)
    out_ref[:, width:] = encoded.astype(out_ref.dtype)


def owner_lookup(row_request, time_request, memory, last_update, time_freq, time_phase):
    rows_count, width = memory.shape
    slots = row_request.shape[0]
    time_width = time_freq.shape[0]
    digit_cols = jnp.arange(time_width, dtype=jnp.int32)
    digits = jnp.where(
        digit_cols[None, :] == 0,
        last_update[:, None] // 64,
        jnp.where(digit_cols[None, :] == 1, last_update[:, None] % 64, 0),
    ).astype(jnp.bfloat16)
    block = 512
    return pl.pallas_call(
        lookup_kernel,
        grid=(slots // block,),
        in_specs=[
            pl.BlockSpec((block, 1), lambda i: (i, 0)),
            pl.BlockSpec((block, 1), lambda i: (i, 0)),
            pl.BlockSpec((rows_count, width), lambda i: (0, 0)),
            pl.BlockSpec((rows_count, time_width), lambda i: (0, 0)),
            pl.BlockSpec((1, time_width), lambda i: (0, 0)),
            pl.BlockSpec((1, time_width), lambda i: (0, 0)),
        ],
        out_specs=pl.BlockSpec((block, width + time_width), lambda i: (i, 0)),
        out_shape=jax.ShapeDtypeStruct((slots, width + time_width), memory.dtype),
    )(
        row_request.reshape(slots, 1),
        time_request.reshape(slots, 1),
        memory,
        digits,
        time_freq.reshape(1, time_width),
        time_phase.reshape(1, time_width),
    )


def local(
    src_owner,
    src_row,
    dst_owner,
    dst_row,
    event_time,
    edge_feat,
    memory,
    last_update,
    time_freq,
    time_phase,
    w_msg_in,
    b_msg,
    w_msg_out,
    w_gru_in,
    b_gru_in,
    w_gru_hid,
):
    devices_all = lax.axis_size(("ev", "node"))
    events_here = edge_feat.shape[0]
    capacity = max(2, 2 * events_here // devices_all)
    chunk = 2 * capacity
    width = memory.shape[1]
    time_width = time_freq.shape[0]
    slot_total = devices_all * chunk
    slot_ids = jnp.stack(
        [
            slot_of(src_owner[:, 0], devices_all, chunk),
            slot_of(dst_owner[:, 0], devices_all, chunk) + capacity,
        ]
    )
    slot_all = slot_ids.reshape(-1)
    rows_all = jnp.concatenate([src_row, dst_row])
    times_all = jnp.concatenate([event_time, event_time])
    digits = jnp.stack(
        [rows_all // 64, rows_all % 64, times_all // 64, times_all % 64, jnp.ones_like(rows_all)],
        axis=1,
    ).astype(jnp.bfloat16)
    slot_range = jnp.arange(slot_total, dtype=jnp.int32)
    placed = (slot_range[:, None] == slot_all[None, :]).astype(jnp.bfloat16)
    gathered = jnp.dot(placed, digits, preferred_element_type=jnp.float32).astype(jnp.int32)
    filled = gathered[:, 4] > 0
    row_request = jnp.where(filled, gathered[:, 0] * 64 + gathered[:, 1], -1)
    time_request = gathered[:, 2] * 64 + gathered[:, 3]
    request = jnp.stack([row_request, time_request]).reshape(2, devices_all, chunk)
    request = request.transpose(1, 0, 2)
    edge_part = (
        jnp.dot(edge_feat, w_msg_in[2 * width + time_width :], preferred_element_type=jnp.float32)
        + b_msg
    )
    received = lax.all_to_all(request, ("ev", "node"), split_axis=0, concat_axis=0, tiled=True)
    rows_held = received[:, 0, :].reshape(-1)
    times_held = received[:, 1, :].reshape(-1)
    served = owner_lookup(rows_held, times_held, memory, last_update, time_freq, time_phase)
    returned = lax.all_to_all(served, ("ev", "node"), split_axis=0, concat_axis=0, tiled=True)
    outgoing = event_messages(slot_ids, returned, edge_part, w_msg_in, w_msg_out)
    arrived = lax.all_to_all(outgoing, ("ev", "node"), split_axis=0, concat_axis=0, tiled=True)
    return owner_update(rows_held, arrived, memory, w_gru_in, b_gru_in, w_gru_hid)


def solution(mesh):
    in_specs = (
        P(("ev", "node"), None),
        P(("ev", "node")),
        P(("ev", "node"), None),
        P(("ev", "node")),
        P(("ev", "node")),
        P(("ev", "node"), None),
        P(("ev", "node"), None),
        P(("ev", "node")),
        P(),
        P(),
        P(),
        P(),
        P(),
        P(),
        P(),
        P(),
    )
    out_specs = P(("ev", "node"), None)
    return jax.shard_map(local, mesh=mesh, in_specs=in_specs, out_specs=out_specs, check_vma=False)
```

```python
import jax
import jax.numpy as jnp
from jax import lax
from jax.experimental import pallas as pl
from jax.sharding import PartitionSpec as P


def encode(delta_int, time_freq, time_phase):
    delta = delta_int.astype(jnp.float32)
    return jnp.cos(delta[..., None] * time_freq + time_phase).astype(jnp.bfloat16)


def gru_update(mean_msg, state, w_gru_in, b_gru_in, w_gru_hid):
    width = state.shape[-1]
    input_part = jnp.dot(mean_msg, w_gru_in, preferred_element_type=jnp.float32) + b_gru_in
    state_part = jnp.dot(state, w_gru_hid, preferred_element_type=jnp.float32)
    reset = jax.nn.sigmoid(input_part[:, :width] + state_part[:, :width])
    update = jax.nn.sigmoid(input_part[:, width : 2 * width] + state_part[:, width : 2 * width])
    candid = jnp.tanh(input_part[:, 2 * width :] + reset * state_part[:, 2 * width :])
    return ((1.0 - update) * candid + update * state.astype(jnp.float32)).astype(jnp.bfloat16)


def gate(x):
    return 0.5 + 0.5 * jnp.tanh(0.5 * x)


def update_kernel(rows_ref, msg_ref, mem_ref, win_ref, bin_ref, whid_ref, out_ref):
    block = out_ref.shape[0]
    slots = rows_ref.shape[1]
    width = mem_ref.shape[1]
    ids = pl.program_id(0) * block + lax.broadcasted_iota(jnp.int32, (block, slots), 0)
    onehot = (ids == rows_ref[...]).astype(jnp.bfloat16)
    total = jnp.dot(onehot, msg_ref[...], preferred_element_type=jnp.float32)
    ones = jnp.ones((slots, 128), jnp.bfloat16)
    count = jnp.dot(onehot, ones, preferred_element_type=jnp.float32)[:, :1]
    mean_msg = (total / jnp.maximum(count, 1.0)).astype(jnp.bfloat16)
    state = mem_ref[...]
    input_part = jnp.dot(mean_msg, win_ref[...], preferred_element_type=jnp.float32) + bin_ref[...]
    state_part = jnp.dot(state, whid_ref[...], preferred_element_type=jnp.float32)
    reset = gate(input_part[:, :width] + state_part[:, :width])
    update = gate(input_part[:, width : 2 * width] + state_part[:, width : 2 * width])
    candid = jnp.tanh(input_part[:, 2 * width :] + reset * state_part[:, 2 * width :])
    fresh = (1.0 - update) * candid + update * state.astype(jnp.float32)
    out_ref[...] = jnp.where(count > 0, fresh, state.astype(jnp.float32)).astype(out_ref.dtype)


def owner_update(row_flat, msg_flat, memory, w_gru_in, b_gru_in, w_gru_hid):
    rows_count, width = memory.shape
    slots, msg_width = msg_flat.shape
    block = 1024
    gates = w_gru_in.shape[1]
    return pl.pallas_call(
        update_kernel,
        grid=(rows_count // block,),
        in_specs=[
            pl.BlockSpec((1, slots), lambda i: (0, 0)),
            pl.BlockSpec((slots, msg_width), lambda i: (0, 0)),
            pl.BlockSpec((block, width), lambda i: (i, 0)),
            pl.BlockSpec((msg_width, gates), lambda i: (0, 0)),
            pl.BlockSpec((1, gates), lambda i: (0, 0)),
            pl.BlockSpec((width, gates), lambda i: (0, 0)),
        ],
        out_specs=pl.BlockSpec((block, width), lambda i: (i, 0)),
        out_shape=jax.ShapeDtypeStruct(memory.shape, memory.dtype),
    )(row_flat.reshape(1, slots), msg_flat, memory, w_gru_in, b_gru_in.reshape(1, gates), w_gru_hid)


def message_kernel(col_ref, row_ref, fetched_ref, edge_ref, w_in_ref, w_out_ref, out_ref):
    events = edge_ref.shape[0]
    slot_total = fetched_ref.shape[0]
    width = out_ref.shape[1]
    time_width = fetched_ref.shape[1] - width
    lane_ids = lax.broadcasted_iota(jnp.int32, (events, slot_total), 1)
    picked = []
    for side in range(2):
        pick = (lane_ids == col_ref[:, side : side + 1]).astype(jnp.bfloat16)
        rows = jnp.dot(pick, fetched_ref[...], preferred_element_type=jnp.float32)
        picked.append(rows.astype(jnp.bfloat16))
    mem_src, enc_src = picked[0][:, :width], picked[0][:, width:]
    mem_dst, enc_dst = picked[1][:, :width], picked[1][:, width:]
    w_self = w_in_ref[:width]
    w_other = w_in_ref[width : 2 * width]
    w_time = w_in_ref[2 * width : 2 * width + time_width]
    edge = edge_ref[...]

    def message(own, other, enc):
        hidden = (
            jnp.dot(own, w_self, preferred_element_type=jnp.float32)
            + jnp.dot(other, w_other, preferred_element_type=jnp.float32)
            + jnp.dot(enc, w_time, preferred_element_type=jnp.float32)
            + edge
        )
        hidden = jnp.maximum(hidden, 0.0).astype(jnp.bfloat16)
        return jnp.dot(hidden, w_out_ref[...], preferred_element_type=jnp.float32).astype(jnp.bfloat16)

    sent = (message(mem_src, mem_dst, enc_src), message(mem_dst, mem_src, enc_dst))
    sub_ids = lax.broadcasted_iota(jnp.int32, (slot_total, events), 0)
    placed = [(sub_ids == row_ref[side : side + 1, :]).astype(jnp.bfloat16) for side in range(2)]
    out = jnp.dot(placed[0], sent[0], preferred_element_type=jnp.float32)
    out = out + jnp.dot(placed[1], sent[1], preferred_element_type=jnp.float32)
    out_ref[...] = out.astype(out_ref.dtype)


def event_messages(slot_ids, slot_cols, fetched, edge_part, w_msg_in, w_msg_out):
    slot_total = fetched.shape[0]
    msg_width = w_msg_out.shape[1]
    return pl.pallas_call(
        message_kernel,
        out_shape=jax.ShapeDtypeStruct((slot_total, msg_width), jnp.bfloat16),
    )(slot_cols, slot_ids, fetched, edge_part, w_msg_in, w_msg_out)


def prologue_kernel(owner_ref, rows_ref, time_ref, slot_ref, slot_t_ref, request_ref):
    events = owner_ref.shape[1]
    owners = 128
    capacity = 8
    slot_total = request_ref.shape[1]
    chunk = slot_total // owners
    upper = (
        lax.broadcasted_iota(jnp.int32, (events, events), 0)
        < lax.broadcasted_iota(jnp.int32, (events, events), 1)
    ).astype(jnp.bfloat16)
    owner_ids = lax.broadcasted_iota(jnp.int32, (owners, events), 0)
    slots = []
    for side in range(2):
        owner_row = owner_ref[side : side + 1, :]
        onehot = owner_ids == owner_row
        earlier = jnp.dot(onehot.astype(jnp.bfloat16), upper, preferred_element_type=jnp.float32)
        position = jnp.sum(jnp.where(onehot, earlier, 0.0), axis=0, keepdims=True)
        slots.append(owner_row * chunk + side * capacity + position.astype(jnp.int32))
    slot_all = jnp.concatenate(slots, axis=1)
    rows_all = jnp.concatenate([rows_ref[0:1, :], rows_ref[1:2, :]], axis=1)
    times_all = jnp.concatenate([time_ref[...], time_ref[...]], axis=1)
    zero = jnp.zeros_like(rows_all)
    digits = jnp.concatenate(
        [rows_all // 64, rows_all % 64, times_all // 64, times_all % 64, zero + 1, zero, zero, zero],
        axis=0,
    ).astype(jnp.float32)
    stacked = jnp.concatenate([slot_all] + [jnp.zeros_like(slot_all)] * 7, axis=0)
    columns = jnp.transpose(stacked)
    slot_col = columns[:, 0:1]
    lanes = lax.broadcasted_iota(jnp.int32, (2 * events, slot_total), 1)
    placed = (lanes == slot_col).astype(jnp.bfloat16)
    got = jnp.dot(digits.astype(jnp.bfloat16), placed, preferred_element_type=jnp.float32)
    got = got.astype(jnp.int32)
    row_request = jnp.where(got[4:5] > 0, got[0:1] * 64 + got[1:2], -1)
    time_request = got[2:3] * 64 + got[3:4]
    request_ref[...] = jnp.concatenate([row_request, time_request], axis=0)
    slot_ref[...] = jnp.concatenate(slots, axis=0)
    slot_t_ref[...] = jnp.concatenate([columns[:events, 0:1], columns[events:, 0:1]], axis=1)


def build_requests(src_owner, src_row, dst_owner, dst_row, event_time, slot_total):
    events = src_row.shape[0]
    owner_pair = jnp.concatenate([src_owner, dst_owner], axis=1).T
    rows_pair = jnp.stack([src_row, dst_row])
    return pl.pallas_call(
        prologue_kernel,
        out_shape=[
            jax.ShapeDtypeStruct((2, events), jnp.int32),
            jax.ShapeDtypeStruct((events, 2), jnp.int32),
            jax.ShapeDtypeStruct((2, slot_total), jnp.int32),
        ],
    )(owner_pair, rows_pair, event_time.reshape(1, events))


def slot_of(owner_ids, owner_count, capacity):
    events_here = owner_ids.shape[0]
    columns = jnp.arange(owner_count, dtype=jnp.int32)
    onehot = (owner_ids[:, None] == columns[None, :]).astype(jnp.bfloat16)
    order = jnp.arange(events_here, dtype=jnp.int32)
    lower = (order[None, :] < order[:, None]).astype(jnp.bfloat16)
    earlier = jnp.dot(lower, onehot, preferred_element_type=jnp.float32)
    position = jnp.sum(earlier * onehot.astype(jnp.float32), axis=1).astype(jnp.int32)
    return owner_ids * capacity + position


def owner_lookup(row_request, time_request, memory, last_update, time_freq, time_phase):
    rows_count, width = memory.shape
    row_range = jnp.arange(rows_count, dtype=jnp.int32)
    select = (row_request[:, None] == row_range[None, :]).astype(jnp.bfloat16)
    high = (last_update // 64).astype(jnp.bfloat16)
    low = (last_update % 64).astype(jnp.bfloat16)
    table = jnp.concatenate([memory, high[:, None], low[:, None]], axis=1)
    fetched = jnp.dot(select, table, preferred_element_type=jnp.float32)
    mem_rows = fetched[:, :width].astype(jnp.bfloat16)
    stamp = fetched[:, width].astype(jnp.int32) * 64 + fetched[:, width + 1].astype(jnp.int32)
    encoded = encode(time_request - stamp, time_freq, time_phase)
    return jnp.concatenate([mem_rows, encoded], axis=-1)


def local(
    src_owner,
    src_row,
    dst_owner,
    dst_row,
    event_time,
    edge_feat,
    memory,
    last_update,
    time_freq,
    time_phase,
    w_msg_in,
    b_msg,
    w_msg_out,
    w_gru_in,
    b_gru_in,
    w_gru_hid,
):
    devices_all = lax.axis_size(("ev", "node"))
    events_here = edge_feat.shape[0]
    capacity = max(2, 2 * events_here // devices_all)
    chunk = 2 * capacity
    width = memory.shape[1]
    time_width = time_freq.shape[0]
    slot_total = devices_all * chunk
    slot_ids, slot_cols, request = build_requests(
        src_owner, src_row, dst_owner, dst_row, event_time, slot_total
    )
    request = request.reshape(2, devices_all, chunk).transpose(1, 0, 2)
    edge_part = (
        jnp.dot(edge_feat, w_msg_in[2 * width + time_width :], preferred_element_type=jnp.float32)
        + b_msg
    )
    received = lax.all_to_all(request, ("ev", "node"), split_axis=0, concat_axis=0, tiled=True)
    rows_held = received[:, 0, :].reshape(-1)
    times_held = received[:, 1, :].reshape(-1)
    served = owner_lookup(rows_held, times_held, memory, last_update, time_freq, time_phase)
    returned = lax.all_to_all(served, ("ev", "node"), split_axis=0, concat_axis=0, tiled=True)
    outgoing = event_messages(slot_ids, slot_cols, returned, edge_part, w_msg_in, w_msg_out)
    arrived = lax.all_to_all(outgoing, ("ev", "node"), split_axis=0, concat_axis=0, tiled=True)
    return owner_update(rows_held, arrived, memory, w_gru_in, b_gru_in, w_gru_hid)


def solution(mesh):
    in_specs = (
        P(("ev", "node"), None),
        P(("ev", "node")),
        P(("ev", "node"), None),
        P(("ev", "node")),
        P(("ev", "node")),
        P(("ev", "node"), None),
        P(("ev", "node"), None),
        P(("ev", "node")),
        P(),
        P(),
        P(),
        P(),
        P(),
        P(),
        P(),
        P(),
    )
    out_specs = P(("ev", "node"), None)
    return jax.shard_map(local, mesh=mesh, in_specs=in_specs, out_specs=out_specs, check_vma=False)
```

```python
import jax
import jax.numpy as jnp
from jax import lax
from jax.experimental import pallas as pl
from jax.sharding import PartitionSpec as P


def encode(delta_int, time_freq, time_phase):
    delta = delta_int.astype(jnp.float32)
    return jnp.cos(delta[..., None] * time_freq + time_phase).astype(jnp.bfloat16)


def gru_update(mean_msg, state, w_gru_in, b_gru_in, w_gru_hid):
    width = state.shape[-1]
    input_part = jnp.dot(mean_msg, w_gru_in, preferred_element_type=jnp.float32) + b_gru_in
    state_part = jnp.dot(state, w_gru_hid, preferred_element_type=jnp.float32)
    reset = jax.nn.sigmoid(input_part[:, :width] + state_part[:, :width])
    update = jax.nn.sigmoid(input_part[:, width : 2 * width] + state_part[:, width : 2 * width])
    candid = jnp.tanh(input_part[:, 2 * width :] + reset * state_part[:, 2 * width :])
    return ((1.0 - update) * candid + update * state.astype(jnp.float32)).astype(jnp.bfloat16)


def gate(x):
    return 0.5 + 0.5 * jnp.tanh(0.5 * x)


def update_kernel(rows_ref, msg_ref, mem_ref, win_ref, bin_ref, whid_ref, out_ref):
    block = out_ref.shape[0]
    slots = rows_ref.shape[1]
    width = mem_ref.shape[1]
    ids = pl.program_id(0) * block + lax.broadcasted_iota(jnp.int32, (block, slots), 0)
    onehot = (ids == rows_ref[...]).astype(jnp.bfloat16)
    total = jnp.dot(onehot, msg_ref[...], preferred_element_type=jnp.float32)
    ones = jnp.ones((slots, 128), jnp.bfloat16)
    count = jnp.dot(onehot, ones, preferred_element_type=jnp.float32)[:, :1]
    mean_msg = (total / jnp.maximum(count, 1.0)).astype(jnp.bfloat16)
    state = mem_ref[...]
    input_part = jnp.dot(mean_msg, win_ref[...], preferred_element_type=jnp.float32) + bin_ref[...]
    state_part = jnp.dot(state, whid_ref[...], preferred_element_type=jnp.float32)
    reset = gate(input_part[:, :width] + state_part[:, :width])
    update = gate(input_part[:, width : 2 * width] + state_part[:, width : 2 * width])
    candid = jnp.tanh(input_part[:, 2 * width :] + reset * state_part[:, 2 * width :])
    fresh = (1.0 - update) * candid + update * state.astype(jnp.float32)
    out_ref[...] = jnp.where(count > 0, fresh, state.astype(jnp.float32)).astype(out_ref.dtype)


def owner_update(row_flat, msg_flat, memory, w_gru_in, b_gru_in, w_gru_hid):
    rows_count, width = memory.shape
    slots, msg_width = msg_flat.shape
    block = 1024
    gates = w_gru_in.shape[1]
    return pl.pallas_call(
        update_kernel,
        grid=(rows_count // block,),
        in_specs=[
            pl.BlockSpec((1, slots), lambda i: (0, 0)),
            pl.BlockSpec((slots, msg_width), lambda i: (0, 0)),
            pl.BlockSpec((block, width), lambda i: (i, 0)),
            pl.BlockSpec((msg_width, gates), lambda i: (0, 0)),
            pl.BlockSpec((1, gates), lambda i: (0, 0)),
            pl.BlockSpec((width, gates), lambda i: (0, 0)),
        ],
        out_specs=pl.BlockSpec((block, width), lambda i: (i, 0)),
        out_shape=jax.ShapeDtypeStruct(memory.shape, memory.dtype),
    )(row_flat.reshape(1, slots), msg_flat, memory, w_gru_in, b_gru_in.reshape(1, gates), w_gru_hid)


def message_kernel(col_ref, row_ref, fetched_ref, edge_ref, w_in_ref, w_out_ref, out_ref):
    events = edge_ref.shape[0]
    slot_total = fetched_ref.shape[0]
    width = out_ref.shape[1]
    time_width = fetched_ref.shape[1] - width
    lane_ids = lax.broadcasted_iota(jnp.int32, (events, slot_total), 1)
    picked = []
    for side in range(2):
        pick = (lane_ids == col_ref[:, side : side + 1]).astype(jnp.bfloat16)
        rows = jnp.dot(pick, fetched_ref[...], preferred_element_type=jnp.float32)
        picked.append(rows.astype(jnp.bfloat16))
    mem_src, enc_src = picked[0][:, :width], picked[0][:, width:]
    mem_dst, enc_dst = picked[1][:, :width], picked[1][:, width:]
    w_self = w_in_ref[:width]
    w_other = w_in_ref[width : 2 * width]
    w_time = w_in_ref[2 * width : 2 * width + time_width]
    edge = edge_ref[...]

    def message(own, other, enc):
        hidden = (
            jnp.dot(own, w_self, preferred_element_type=jnp.float32)
            + jnp.dot(other, w_other, preferred_element_type=jnp.float32)
            + jnp.dot(enc, w_time, preferred_element_type=jnp.float32)
            + edge
        )
        hidden = jnp.maximum(hidden, 0.0).astype(jnp.bfloat16)
        return jnp.dot(hidden, w_out_ref[...], preferred_element_type=jnp.float32).astype(jnp.bfloat16)

    sent = (message(mem_src, mem_dst, enc_src), message(mem_dst, mem_src, enc_dst))
    sub_ids = lax.broadcasted_iota(jnp.int32, (slot_total, events), 0)
    placed = [(sub_ids == row_ref[side : side + 1, :]).astype(jnp.bfloat16) for side in range(2)]
    out = jnp.dot(placed[0], sent[0], preferred_element_type=jnp.float32)
    out = out + jnp.dot(placed[1], sent[1], preferred_element_type=jnp.float32)
    out_ref[...] = out.astype(out_ref.dtype)


def event_messages(slot_ids, slot_cols, fetched, edge_part, w_msg_in, w_msg_out):
    slot_total = fetched.shape[0]
    msg_width = w_msg_out.shape[1]
    return pl.pallas_call(
        message_kernel,
        out_shape=jax.ShapeDtypeStruct((slot_total, msg_width), jnp.bfloat16),
    )(slot_cols, slot_ids, fetched, edge_part, w_msg_in, w_msg_out)


def prologue_kernel(
    src_owner_ref, dst_owner_ref, src_row_ref, dst_row_ref, time_ref, slot_ref, slot_t_ref, request_ref
):
    events = src_owner_ref.shape[0]
    slot_total = request_ref.shape[1]
    capacity = 8
    owners = slot_total // (2 * capacity)
    chunk = 2 * capacity
    lower = (
        lax.broadcasted_iota(jnp.int32, (events, events), 0)
        > lax.broadcasted_iota(jnp.int32, (events, events), 1)
    ).astype(jnp.bfloat16)
    owner_ids = lax.broadcasted_iota(jnp.int32, (events, owners), 1)
    columns = []
    for side, owner_ref in enumerate((src_owner_ref, dst_owner_ref)):
        owner_col = owner_ref[...]
        onehot = owner_ids == owner_col
        earlier = jnp.dot(lower, onehot.astype(jnp.bfloat16), preferred_element_type=jnp.float32)
        position = jnp.sum(jnp.where(onehot, earlier, 0.0), axis=1, keepdims=True)
        columns.append(owner_col * chunk + side * capacity + position.astype(jnp.int32))
    slot_t_ref[...] = jnp.concatenate(columns, axis=1)
    padded = jnp.concatenate(columns + [jnp.zeros_like(columns[0])] * 6, axis=1)
    slot_ref[...] = jnp.transpose(padded)[0:2, :]
    slot_col = jnp.concatenate(columns, axis=0)
    rows_all = jnp.concatenate([src_row_ref[...], dst_row_ref[...]], axis=1)
    times_all = jnp.concatenate([time_ref[...], time_ref[...]], axis=1)
    zero = jnp.zeros_like(rows_all)
    digits = jnp.concatenate(
        [rows_all // 64, rows_all % 64, times_all // 64, times_all % 64, zero + 1, zero, zero, zero],
        axis=0,
    ).astype(jnp.float32)
    lanes = lax.broadcasted_iota(jnp.int32, (2 * events, slot_total), 1)
    placed = (lanes == slot_col).astype(jnp.bfloat16)
    got = jnp.dot(digits.astype(jnp.bfloat16), placed, preferred_element_type=jnp.float32)
    got = got.astype(jnp.int32)
    row_request = jnp.where(got[4:5] > 0, got[0:1] * 64 + got[1:2], -1)
    time_request = got[2:3] * 64 + got[3:4]
    request_ref[...] = jnp.concatenate([row_request, time_request], axis=0)


def build_requests(src_owner, src_row, dst_owner, dst_row, event_time, slot_total):
    events = src_row.shape[0]
    return pl.pallas_call(
        prologue_kernel,
        out_shape=[
            jax.ShapeDtypeStruct((2, events), jnp.int32),
            jax.ShapeDtypeStruct((events, 2), jnp.int32),
            jax.ShapeDtypeStruct((2, slot_total), jnp.int32),
        ],
    )(
        src_owner,
        dst_owner,
        src_row.reshape(1, events),
        dst_row.reshape(1, events),
        event_time.reshape(1, events),
    )


def slot_of(owner_ids, owner_count, capacity):
    events_here = owner_ids.shape[0]
    columns = jnp.arange(owner_count, dtype=jnp.int32)
    onehot = (owner_ids[:, None] == columns[None, :]).astype(jnp.bfloat16)
    order = jnp.arange(events_here, dtype=jnp.int32)
    lower = (order[None, :] < order[:, None]).astype(jnp.bfloat16)
    earlier = jnp.dot(lower, onehot, preferred_element_type=jnp.float32)
    position = jnp.sum(earlier * onehot.astype(jnp.float32), axis=1).astype(jnp.int32)
    return owner_ids * capacity + position


def owner_lookup(row_request, time_request, memory, last_update, time_freq, time_phase):
    rows_count, width = memory.shape
    row_range = jnp.arange(rows_count, dtype=jnp.int32)
    select = (row_request[:, None] == row_range[None, :]).astype(jnp.bfloat16)
    high = (last_update // 64).astype(jnp.bfloat16)
    low = (last_update % 64).astype(jnp.bfloat16)
    table = jnp.concatenate([memory, high[:, None], low[:, None]], axis=1)
    fetched = jnp.dot(select, table, preferred_element_type=jnp.float32)
    mem_rows = fetched[:, :width].astype(jnp.bfloat16)
    stamp = fetched[:, width].astype(jnp.int32) * 64 + fetched[:, width + 1].astype(jnp.int32)
    encoded = encode(time_request - stamp, time_freq, time_phase)
    return jnp.concatenate([mem_rows, encoded], axis=-1)


def local(
    src_owner,
    src_row,
    dst_owner,
    dst_row,
    event_time,
    edge_feat,
    memory,
    last_update,
    time_freq,
    time_phase,
    w_msg_in,
    b_msg,
    w_msg_out,
    w_gru_in,
    b_gru_in,
    w_gru_hid,
):
    devices_all = lax.axis_size(("ev", "node"))
    events_here = edge_feat.shape[0]
    capacity = max(2, 2 * events_here // devices_all)
    chunk = 2 * capacity
    width = memory.shape[1]
    time_width = time_freq.shape[0]
    slot_total = devices_all * chunk
    slot_ids, slot_cols, request = build_requests(
        src_owner, src_row, dst_owner, dst_row, event_time, slot_total
    )
    request = request.reshape(2, devices_all, chunk).transpose(1, 0, 2)
    edge_part = (
        jnp.dot(edge_feat, w_msg_in[2 * width + time_width :], preferred_element_type=jnp.float32)
        + b_msg
    )
    received = lax.all_to_all(request, ("ev", "node"), split_axis=0, concat_axis=0, tiled=True)
    rows_held = received[:, 0, :].reshape(-1)
    times_held = received[:, 1, :].reshape(-1)
    served = owner_lookup(rows_held, times_held, memory, last_update, time_freq, time_phase)
    returned = lax.all_to_all(served, ("ev", "node"), split_axis=0, concat_axis=0, tiled=True)
    outgoing = event_messages(slot_ids, slot_cols, returned, edge_part, w_msg_in, w_msg_out)
    arrived = lax.all_to_all(outgoing, ("ev", "node"), split_axis=0, concat_axis=0, tiled=True)
    return owner_update(rows_held, arrived, memory, w_gru_in, b_gru_in, w_gru_hid)


def solution(mesh):
    in_specs = (
        P(("ev", "node"), None),
        P(("ev", "node")),
        P(("ev", "node"), None),
        P(("ev", "node")),
        P(("ev", "node")),
        P(("ev", "node"), None),
        P(("ev", "node"), None),
        P(("ev", "node")),
        P(),
        P(),
        P(),
        P(),
        P(),
        P(),
        P(),
        P(),
    )
    out_specs = P(("ev", "node"), None)
    return jax.shard_map(local, mesh=mesh, in_specs=in_specs, out_specs=out_specs, check_vma=False)
```

```python
import jax
import jax.numpy as jnp
from jax import lax
from jax.experimental import pallas as pl
from jax.sharding import PartitionSpec as P


def encode(delta_int, time_freq, time_phase):
    delta = delta_int.astype(jnp.float32)
    return jnp.cos(delta[..., None] * time_freq + time_phase).astype(jnp.bfloat16)


def gru_update(mean_msg, state, w_gru_in, b_gru_in, w_gru_hid):
    width = state.shape[-1]
    input_part = jnp.dot(mean_msg, w_gru_in, preferred_element_type=jnp.float32) + b_gru_in
    state_part = jnp.dot(state, w_gru_hid, preferred_element_type=jnp.float32)
    reset = jax.nn.sigmoid(input_part[:, :width] + state_part[:, :width])
    update = jax.nn.sigmoid(input_part[:, width : 2 * width] + state_part[:, width : 2 * width])
    candid = jnp.tanh(input_part[:, 2 * width :] + reset * state_part[:, 2 * width :])
    return ((1.0 - update) * candid + update * state.astype(jnp.float32)).astype(jnp.bfloat16)


def gate(x):
    return 0.5 + 0.5 * jnp.tanh(0.5 * x)


def update_kernel(rows_ref, msg_ref, mem_ref, win_ref, bin_ref, whid_ref, out_ref):
    block = out_ref.shape[0]
    slots = rows_ref.shape[1]
    width = mem_ref.shape[1]
    ids = pl.program_id(0) * block + lax.broadcasted_iota(jnp.int32, (block, slots), 0)
    onehot = (ids == rows_ref[...]).astype(jnp.bfloat16)
    total = jnp.dot(onehot, msg_ref[...], preferred_element_type=jnp.float32)
    ones = jnp.ones((slots, 128), jnp.bfloat16)
    count = jnp.dot(onehot, ones, preferred_element_type=jnp.float32)[:, :1]
    mean_msg = (total / jnp.maximum(count, 1.0)).astype(jnp.bfloat16)
    state = mem_ref[...]
    input_part = jnp.dot(mean_msg, win_ref[...], preferred_element_type=jnp.float32) + bin_ref[...]
    state_part = jnp.dot(state, whid_ref[...], preferred_element_type=jnp.float32)
    reset = gate(input_part[:, :width] + state_part[:, :width])
    update = gate(input_part[:, width : 2 * width] + state_part[:, width : 2 * width])
    candid = jnp.tanh(input_part[:, 2 * width :] + reset * state_part[:, 2 * width :])
    fresh = (1.0 - update) * candid + update * state.astype(jnp.float32)
    out_ref[...] = jnp.where(count > 0, fresh, state.astype(jnp.float32)).astype(out_ref.dtype)


def owner_update(row_flat, msg_flat, memory, w_gru_in, b_gru_in, w_gru_hid):
    rows_count, width = memory.shape
    slots, msg_width = msg_flat.shape
    block = 1024
    gates = w_gru_in.shape[1]
    return pl.pallas_call(
        update_kernel,
        grid=(rows_count // block,),
        in_specs=[
            pl.BlockSpec((1, slots), lambda i: (0, 0)),
            pl.BlockSpec((slots, msg_width), lambda i: (0, 0)),
            pl.BlockSpec((block, width), lambda i: (i, 0)),
            pl.BlockSpec((msg_width, gates), lambda i: (0, 0)),
            pl.BlockSpec((1, gates), lambda i: (0, 0)),
            pl.BlockSpec((width, gates), lambda i: (0, 0)),
        ],
        out_specs=pl.BlockSpec((block, width), lambda i: (i, 0)),
        out_shape=jax.ShapeDtypeStruct(memory.shape, memory.dtype),
    )(row_flat.reshape(1, slots), msg_flat, memory, w_gru_in, b_gru_in.reshape(1, gates), w_gru_hid)


def message_kernel(col_ref, row_ref, fetched_ref, edge_ref, w_in_ref, w_out_ref, out_ref):
    events = edge_ref.shape[0]
    slot_total = fetched_ref.shape[0]
    width = out_ref.shape[1]
    time_width = fetched_ref.shape[1] - width
    lane_ids = lax.broadcasted_iota(jnp.int32, (events, slot_total), 1)
    picked = []
    for side in range(2):
        pick = (lane_ids == col_ref[:, side : side + 1]).astype(jnp.bfloat16)
        rows = jnp.dot(pick, fetched_ref[...], preferred_element_type=jnp.float32)
        picked.append(rows.astype(jnp.bfloat16))
    mem_src, enc_src = picked[0][:, :width], picked[0][:, width:]
    mem_dst, enc_dst = picked[1][:, :width], picked[1][:, width:]
    w_self = w_in_ref[:width]
    w_other = w_in_ref[width : 2 * width]
    w_time = w_in_ref[2 * width : 2 * width + time_width]
    edge = edge_ref[...]

    def message(own, other, enc):
        hidden = (
            jnp.dot(own, w_self, preferred_element_type=jnp.float32)
            + jnp.dot(other, w_other, preferred_element_type=jnp.float32)
            + jnp.dot(enc, w_time, preferred_element_type=jnp.float32)
            + edge
        )
        hidden = jnp.maximum(hidden, 0.0).astype(jnp.bfloat16)
        return jnp.dot(hidden, w_out_ref[...], preferred_element_type=jnp.float32).astype(jnp.bfloat16)

    sent = (message(mem_src, mem_dst, enc_src), message(mem_dst, mem_src, enc_dst))
    sub_ids = lax.broadcasted_iota(jnp.int32, (slot_total, events), 0)
    placed = [(sub_ids == row_ref[side : side + 1, :]).astype(jnp.bfloat16) for side in range(2)]
    out = jnp.dot(placed[0], sent[0], preferred_element_type=jnp.float32)
    out = out + jnp.dot(placed[1], sent[1], preferred_element_type=jnp.float32)
    out_ref[...] = out.astype(out_ref.dtype)


def event_messages(slot_ids, slot_cols, fetched, edge_part, w_msg_in, w_msg_out):
    slot_total = fetched.shape[0]
    msg_width = w_msg_out.shape[1]
    return pl.pallas_call(
        message_kernel,
        out_shape=jax.ShapeDtypeStruct((slot_total, msg_width), jnp.bfloat16),
    )(slot_cols, slot_ids, fetched, edge_part, w_msg_in, w_msg_out)


def prologue_kernel(owner_ref, src_row_ref, dst_row_ref, time_ref, slot_ref, slot_t_ref, request_ref):
    events = owner_ref.shape[1]
    owners = 128
    capacity = 8
    slot_total = request_ref.shape[1]
    chunk = slot_total // owners
    upper = (
        lax.broadcasted_iota(jnp.int32, (events, events), 0)
        < lax.broadcasted_iota(jnp.int32, (events, events), 1)
    ).astype(jnp.bfloat16)
    owner_ids = lax.broadcasted_iota(jnp.int32, (owners, events), 0)
    slots = []
    for side in range(2):
        owner_row = owner_ref[side : side + 1, :]
        onehot = owner_ids == owner_row
        earlier = jnp.dot(onehot.astype(jnp.bfloat16), upper, preferred_element_type=jnp.float32)
        position = jnp.sum(jnp.where(onehot, earlier, 0.0), axis=0, keepdims=True)
        slots.append(owner_row * chunk + side * capacity + position.astype(jnp.int32))
    slot_all = jnp.concatenate(slots, axis=1)
    rows_all = jnp.concatenate([src_row_ref[...], dst_row_ref[...]], axis=1)
    times_all = jnp.concatenate([time_ref[...], time_ref[...]], axis=1)
    zero = jnp.zeros_like(rows_all)
    digits = jnp.concatenate(
        [rows_all // 64, rows_all % 64, times_all // 64, times_all % 64, zero + 1, zero, zero, zero],
        axis=0,
    ).astype(jnp.float32)
    stacked = jnp.concatenate([slot_all] + [jnp.zeros_like(slot_all)] * 7, axis=0)
    columns = jnp.transpose(stacked)
    slot_col = columns[:, 0:1]
    lanes = lax.broadcasted_iota(jnp.int32, (2 * events, slot_total), 1)
    placed = (lanes == slot_col).astype(jnp.bfloat16)
    got = jnp.dot(digits.astype(jnp.bfloat16), placed, preferred_element_type=jnp.float32)
    got = got.astype(jnp.int32)
    row_request = jnp.where(got[4:5] > 0, got[0:1] * 64 + got[1:2], -1)
    time_request = got[2:3] * 64 + got[3:4]
    request_ref[...] = jnp.concatenate([row_request, time_request], axis=0)
    slot_ref[...] = jnp.concatenate(slots, axis=0)
    slot_t_ref[...] = jnp.concatenate([columns[:events, 0:1], columns[events:, 0:1]], axis=1)


def build_requests(src_owner, src_row, dst_owner, dst_row, event_time, slot_total):
    events = src_row.shape[0]
    owner_pair = jnp.concatenate([src_owner, dst_owner], axis=1).T
    return pl.pallas_call(
        prologue_kernel,
        out_shape=[
            jax.ShapeDtypeStruct((2, events), jnp.int32),
            jax.ShapeDtypeStruct((events, 2), jnp.int32),
            jax.ShapeDtypeStruct((2, slot_total), jnp.int32),
        ],
    )(owner_pair, src_row.reshape(1, events), dst_row.reshape(1, events), event_time.reshape(1, events))


def slot_of(owner_ids, owner_count, capacity):
    events_here = owner_ids.shape[0]
    columns = jnp.arange(owner_count, dtype=jnp.int32)
    onehot = (owner_ids[:, None] == columns[None, :]).astype(jnp.bfloat16)
    order = jnp.arange(events_here, dtype=jnp.int32)
    lower = (order[None, :] < order[:, None]).astype(jnp.bfloat16)
    earlier = jnp.dot(lower, onehot, preferred_element_type=jnp.float32)
    position = jnp.sum(earlier * onehot.astype(jnp.float32), axis=1).astype(jnp.int32)
    return owner_ids * capacity + position


def owner_lookup(row_request, time_request, memory, last_update, time_freq, time_phase):
    rows_count, width = memory.shape
    row_range = jnp.arange(rows_count, dtype=jnp.int32)
    select = (row_request[:, None] == row_range[None, :]).astype(jnp.bfloat16)
    high = (last_update // 64).astype(jnp.bfloat16)
    low = (last_update % 64).astype(jnp.bfloat16)
    table = jnp.concatenate([memory, high[:, None], low[:, None]], axis=1)
    fetched = jnp.dot(select, table, preferred_element_type=jnp.float32)
    mem_rows = fetched[:, :width].astype(jnp.bfloat16)
    stamp = fetched[:, width].astype(jnp.int32) * 64 + fetched[:, width + 1].astype(jnp.int32)
    encoded = encode(time_request - stamp, time_freq, time_phase)
    return jnp.concatenate([mem_rows, encoded], axis=-1)


def local(
    src_owner,
    src_row,
    dst_owner,
    dst_row,
    event_time,
    edge_feat,
    memory,
    last_update,
    time_freq,
    time_phase,
    w_msg_in,
    b_msg,
    w_msg_out,
    w_gru_in,
    b_gru_in,
    w_gru_hid,
):
    devices_all = lax.axis_size(("ev", "node"))
    events_here = edge_feat.shape[0]
    capacity = max(2, 2 * events_here // devices_all)
    chunk = 2 * capacity
    width = memory.shape[1]
    time_width = time_freq.shape[0]
    slot_total = devices_all * chunk
    slot_ids, slot_cols, request = build_requests(
        src_owner, src_row, dst_owner, dst_row, event_time, slot_total
    )
    request = request.reshape(2, devices_all, chunk)
    edge_part = (
        jnp.dot(edge_feat, w_msg_in[2 * width + time_width :], preferred_element_type=jnp.float32)
        + b_msg
    )
    received = lax.all_to_all(request, ("ev", "node"), split_axis=1, concat_axis=1, tiled=True)
    rows_held = received[0].reshape(-1)
    times_held = received[1].reshape(-1)
    served = owner_lookup(rows_held, times_held, memory, last_update, time_freq, time_phase)
    returned = lax.all_to_all(served, ("ev", "node"), split_axis=0, concat_axis=0, tiled=True)
    outgoing = event_messages(slot_ids, slot_cols, returned, edge_part, w_msg_in, w_msg_out)
    arrived = lax.all_to_all(outgoing, ("ev", "node"), split_axis=0, concat_axis=0, tiled=True)
    return owner_update(rows_held, arrived, memory, w_gru_in, b_gru_in, w_gru_hid)


def solution(mesh):
    in_specs = (
        P(("ev", "node"), None),
        P(("ev", "node")),
        P(("ev", "node"), None),
        P(("ev", "node")),
        P(("ev", "node")),
        P(("ev", "node"), None),
        P(("ev", "node"), None),
        P(("ev", "node")),
        P(),
        P(),
        P(),
        P(),
        P(),
        P(),
        P(),
        P(),
    )
    out_specs = P(("ev", "node"), None)
    return jax.shard_map(local, mesh=mesh, in_specs=in_specs, out_specs=out_specs, check_vma=False)
```

```python
import jax
import jax.numpy as jnp
from jax import lax
from jax.experimental import pallas as pl
from jax.sharding import PartitionSpec as P


def encode(delta_int, time_freq, time_phase):
    delta = delta_int.astype(jnp.float32)
    return jnp.cos(delta[..., None] * time_freq + time_phase).astype(jnp.bfloat16)


def gru_update(mean_msg, state, w_gru_in, b_gru_in, w_gru_hid):
    width = state.shape[-1]
    input_part = jnp.dot(mean_msg, w_gru_in, preferred_element_type=jnp.float32) + b_gru_in
    state_part = jnp.dot(state, w_gru_hid, preferred_element_type=jnp.float32)
    reset = jax.nn.sigmoid(input_part[:, :width] + state_part[:, :width])
    update = jax.nn.sigmoid(input_part[:, width : 2 * width] + state_part[:, width : 2 * width])
    candid = jnp.tanh(input_part[:, 2 * width :] + reset * state_part[:, 2 * width :])
    return ((1.0 - update) * candid + update * state.astype(jnp.float32)).astype(jnp.bfloat16)


def gate(x):
    return 0.5 + 0.5 * jnp.tanh(0.5 * x)


def update_kernel(rows_ref, msg_ref, mem_ref, win_ref, bin_ref, whid_ref, out_ref):
    block = out_ref.shape[0]
    slots = rows_ref.shape[1]
    width = mem_ref.shape[1]
    ids = pl.program_id(0) * block + lax.broadcasted_iota(jnp.int32, (block, slots), 0)
    onehot = (ids == rows_ref[...]).astype(jnp.bfloat16)
    total = jnp.dot(onehot, msg_ref[...], preferred_element_type=jnp.float32)
    ones = jnp.ones((slots, 128), jnp.bfloat16)
    count = jnp.dot(onehot, ones, preferred_element_type=jnp.float32)[:, :1]
    mean_msg = (total / jnp.maximum(count, 1.0)).astype(jnp.bfloat16)
    state = mem_ref[...]
    input_part = jnp.dot(mean_msg, win_ref[...], preferred_element_type=jnp.float32) + bin_ref[...]
    state_part = jnp.dot(state, whid_ref[...], preferred_element_type=jnp.float32)
    reset = gate(input_part[:, :width] + state_part[:, :width])
    update = gate(input_part[:, width : 2 * width] + state_part[:, width : 2 * width])
    candid = jnp.tanh(input_part[:, 2 * width :] + reset * state_part[:, 2 * width :])
    fresh = (1.0 - update) * candid + update * state.astype(jnp.float32)
    out_ref[...] = jnp.where(count > 0, fresh, state.astype(jnp.float32)).astype(out_ref.dtype)


def owner_update(row_flat, msg_flat, memory, w_gru_in, b_gru_in, w_gru_hid):
    rows_count, width = memory.shape
    slots, msg_width = msg_flat.shape
    block = 1024
    gates = w_gru_in.shape[1]
    return pl.pallas_call(
        update_kernel,
        grid=(rows_count // block,),
        in_specs=[
            pl.BlockSpec((1, slots), lambda i: (0, 0)),
            pl.BlockSpec((slots, msg_width), lambda i: (0, 0)),
            pl.BlockSpec((block, width), lambda i: (i, 0)),
            pl.BlockSpec((msg_width, gates), lambda i: (0, 0)),
            pl.BlockSpec((1, gates), lambda i: (0, 0)),
            pl.BlockSpec((width, gates), lambda i: (0, 0)),
        ],
        out_specs=pl.BlockSpec((block, width), lambda i: (i, 0)),
        out_shape=jax.ShapeDtypeStruct(memory.shape, memory.dtype),
    )(row_flat.reshape(1, slots), msg_flat, memory, w_gru_in, b_gru_in.reshape(1, gates), w_gru_hid)


def message_kernel(
    col_ref, row_ref, fetched_ref, edge_ref, time_ref, freq_ref, phase_ref, w_in_ref, w_out_ref, out_ref
):
    events = edge_ref.shape[0]
    slot_total = fetched_ref.shape[0]
    width = out_ref.shape[1]
    time_width = fetched_ref.shape[1] - width
    lane_ids = lax.broadcasted_iota(jnp.int32, (events, slot_total), 1)
    picked = []
    for side in range(2):
        pick = (lane_ids == col_ref[:, side : side + 1]).astype(jnp.bfloat16)
        rows = jnp.dot(pick, fetched_ref[...], preferred_element_type=jnp.float32)
        stamp = rows[:, width : width + 1].astype(jnp.int32) * 64
        stamp = stamp + rows[:, width + 1 : width + 2].astype(jnp.int32)
        delta = (time_ref[...] - stamp).astype(jnp.float32)
        encoded = jnp.cos(delta * freq_ref[...] + phase_ref[...]).astype(jnp.bfloat16)
        picked.append((rows[:, :width].astype(jnp.bfloat16), encoded))
    mem_src, enc_src = picked[0]
    mem_dst, enc_dst = picked[1]
    w_self = w_in_ref[:width]
    w_other = w_in_ref[width : 2 * width]
    w_time = w_in_ref[2 * width : 2 * width + time_width]
    edge = edge_ref[...]

    def message(own, other, enc):
        hidden = (
            jnp.dot(own, w_self, preferred_element_type=jnp.float32)
            + jnp.dot(other, w_other, preferred_element_type=jnp.float32)
            + jnp.dot(enc, w_time, preferred_element_type=jnp.float32)
            + edge
        )
        hidden = jnp.maximum(hidden, 0.0).astype(jnp.bfloat16)
        return jnp.dot(hidden, w_out_ref[...], preferred_element_type=jnp.float32).astype(jnp.bfloat16)

    sent = (message(mem_src, mem_dst, enc_src), message(mem_dst, mem_src, enc_dst))
    sub_ids = lax.broadcasted_iota(jnp.int32, (slot_total, events), 0)
    placed = [(sub_ids == row_ref[side : side + 1, :]).astype(jnp.bfloat16) for side in range(2)]
    out = jnp.dot(placed[0], sent[0], preferred_element_type=jnp.float32)
    out = out + jnp.dot(placed[1], sent[1], preferred_element_type=jnp.float32)
    out_ref[...] = out.astype(out_ref.dtype)


def event_messages(
    slot_ids, slot_cols, fetched, edge_part, event_time, time_freq, time_phase, w_msg_in, w_msg_out
):
    slot_total = fetched.shape[0]
    msg_width = w_msg_out.shape[1]
    return pl.pallas_call(
        message_kernel,
        out_shape=jax.ShapeDtypeStruct((slot_total, msg_width), jnp.bfloat16),
    )(
        slot_cols,
        slot_ids,
        fetched,
        edge_part,
        event_time.reshape(-1, 1),
        time_freq.reshape(1, -1),
        time_phase.reshape(1, -1),
        w_msg_in,
        w_msg_out,
    )


def prologue_kernel(owner_ref, src_row_ref, dst_row_ref, time_ref, slot_ref, slot_t_ref, request_ref):
    events = owner_ref.shape[1]
    owners = 128
    capacity = 8
    slot_total = request_ref.shape[1]
    chunk = slot_total // owners
    upper = (
        lax.broadcasted_iota(jnp.int32, (events, events), 0)
        < lax.broadcasted_iota(jnp.int32, (events, events), 1)
    ).astype(jnp.bfloat16)
    owner_ids = lax.broadcasted_iota(jnp.int32, (owners, events), 0)
    slots = []
    for side in range(2):
        owner_row = owner_ref[side : side + 1, :]
        onehot = owner_ids == owner_row
        earlier = jnp.dot(onehot.astype(jnp.bfloat16), upper, preferred_element_type=jnp.float32)
        position = jnp.sum(jnp.where(onehot, earlier, 0.0), axis=0, keepdims=True)
        slots.append(owner_row * chunk + side * capacity + position.astype(jnp.int32))
    slot_all = jnp.concatenate(slots, axis=1)
    rows_all = jnp.concatenate([src_row_ref[...], dst_row_ref[...]], axis=1)
    times_all = jnp.concatenate([time_ref[...], time_ref[...]], axis=1)
    zero = jnp.zeros_like(rows_all)
    digits = jnp.concatenate(
        [rows_all // 64, rows_all % 64, times_all // 64, times_all % 64, zero + 1, zero, zero, zero],
        axis=0,
    ).astype(jnp.float32)
    stacked = jnp.concatenate([slot_all] + [jnp.zeros_like(slot_all)] * 7, axis=0)
    columns = jnp.transpose(stacked)
    slot_col = columns[:, 0:1]
    lanes = lax.broadcasted_iota(jnp.int32, (2 * events, slot_total), 1)
    placed = (lanes == slot_col).astype(jnp.bfloat16)
    got = jnp.dot(digits.astype(jnp.bfloat16), placed, preferred_element_type=jnp.float32)
    got = got.astype(jnp.int32)
    row_request = jnp.where(got[4:5] > 0, got[0:1] * 64 + got[1:2], -1)
    time_request = got[2:3] * 64 + got[3:4]
    request_ref[...] = jnp.concatenate([row_request, time_request], axis=0)
    slot_ref[...] = jnp.concatenate(slots, axis=0)
    slot_t_ref[...] = jnp.concatenate([columns[:events, 0:1], columns[events:, 0:1]], axis=1)


def build_requests(src_owner, src_row, dst_owner, dst_row, event_time, slot_total):
    events = src_row.shape[0]
    owner_pair = jnp.concatenate([src_owner, dst_owner], axis=1).T
    return pl.pallas_call(
        prologue_kernel,
        out_shape=[
            jax.ShapeDtypeStruct((2, events), jnp.int32),
            jax.ShapeDtypeStruct((events, 2), jnp.int32),
            jax.ShapeDtypeStruct((2, slot_total), jnp.int32),
        ],
    )(owner_pair, src_row.reshape(1, events), dst_row.reshape(1, events), event_time.reshape(1, events))


def slot_of(owner_ids, owner_count, capacity):
    events_here = owner_ids.shape[0]
    columns = jnp.arange(owner_count, dtype=jnp.int32)
    onehot = (owner_ids[:, None] == columns[None, :]).astype(jnp.bfloat16)
    order = jnp.arange(events_here, dtype=jnp.int32)
    lower = (order[None, :] < order[:, None]).astype(jnp.bfloat16)
    earlier = jnp.dot(lower, onehot, preferred_element_type=jnp.float32)
    position = jnp.sum(earlier * onehot.astype(jnp.float32), axis=1).astype(jnp.int32)
    return owner_ids * capacity + position


def owner_lookup(row_request, memory, last_update, time_width):
    rows_count, width = memory.shape
    row_range = jnp.arange(rows_count, dtype=jnp.int32)
    select = (row_request[:, None] == row_range[None, :]).astype(jnp.bfloat16)
    digit_cols = jnp.arange(time_width, dtype=jnp.int32)
    digits = jnp.where(
        digit_cols[None, :] == 0,
        last_update[:, None] // 64,
        jnp.where(digit_cols[None, :] == 1, last_update[:, None] % 64, 0),
    ).astype(jnp.bfloat16)
    table = jnp.concatenate([memory, digits], axis=1)
    return jnp.dot(select, table, preferred_element_type=jnp.float32).astype(jnp.bfloat16)


def local(
    src_owner,
    src_row,
    dst_owner,
    dst_row,
    event_time,
    edge_feat,
    memory,
    last_update,
    time_freq,
    time_phase,
    w_msg_in,
    b_msg,
    w_msg_out,
    w_gru_in,
    b_gru_in,
    w_gru_hid,
):
    devices_all = lax.axis_size(("ev", "node"))
    events_here = edge_feat.shape[0]
    capacity = max(2, 2 * events_here // devices_all)
    chunk = 2 * capacity
    width = memory.shape[1]
    time_width = time_freq.shape[0]
    slot_total = devices_all * chunk
    slot_ids, slot_cols, request = build_requests(
        src_owner, src_row, dst_owner, dst_row, event_time, slot_total
    )
    request = request.reshape(2, devices_all, chunk)
    edge_part = (
        jnp.dot(edge_feat, w_msg_in[2 * width + time_width :], preferred_element_type=jnp.float32)
        + b_msg
    )
    received = lax.all_to_all(request, ("ev", "node"), split_axis=1, concat_axis=1, tiled=True)
    rows_held = received[0].reshape(-1)
    served = owner_lookup(rows_held, memory, last_update, time_width)
    returned = lax.all_to_all(served, ("ev", "node"), split_axis=0, concat_axis=0, tiled=True)
    outgoing = event_messages(
        slot_ids, slot_cols, returned, edge_part, event_time, time_freq, time_phase, w_msg_in, w_msg_out
    )
    arrived = lax.all_to_all(outgoing, ("ev", "node"), split_axis=0, concat_axis=0, tiled=True)
    return owner_update(rows_held, arrived, memory, w_gru_in, b_gru_in, w_gru_hid)


def solution(mesh):
    in_specs = (
        P(("ev", "node"), None),
        P(("ev", "node")),
        P(("ev", "node"), None),
        P(("ev", "node")),
        P(("ev", "node")),
        P(("ev", "node"), None),
        P(("ev", "node"), None),
        P(("ev", "node")),
        P(),
        P(),
        P(),
        P(),
        P(),
        P(),
        P(),
        P(),
    )
    out_specs = P(("ev", "node"), None)
    return jax.shard_map(local, mesh=mesh, in_specs=in_specs, out_specs=out_specs, check_vma=False)
```

```python
import jax
import jax.numpy as jnp
from jax import lax
from jax.experimental import pallas as pl
from jax.sharding import PartitionSpec as P


def encode(delta_int, time_freq, time_phase):
    delta = delta_int.astype(jnp.float32)
    return jnp.cos(delta[..., None] * time_freq + time_phase).astype(jnp.bfloat16)


def gru_update(mean_msg, state, w_gru_in, b_gru_in, w_gru_hid):
    width = state.shape[-1]
    input_part = jnp.dot(mean_msg, w_gru_in, preferred_element_type=jnp.float32) + b_gru_in
    state_part = jnp.dot(state, w_gru_hid, preferred_element_type=jnp.float32)
    reset = jax.nn.sigmoid(input_part[:, :width] + state_part[:, :width])
    update = jax.nn.sigmoid(input_part[:, width : 2 * width] + state_part[:, width : 2 * width])
    candid = jnp.tanh(input_part[:, 2 * width :] + reset * state_part[:, 2 * width :])
    return ((1.0 - update) * candid + update * state.astype(jnp.float32)).astype(jnp.bfloat16)


def gate(x):
    return 0.5 + 0.5 * jnp.tanh(0.5 * x)


def update_kernel(rows_ref, msg_ref, mem_ref, win_ref, bin_ref, whid_ref, out_ref):
    block = out_ref.shape[0]
    slots = rows_ref.shape[1]
    width = mem_ref.shape[1]
    ids = pl.program_id(0) * block + lax.broadcasted_iota(jnp.int32, (block, slots), 0)
    onehot = (ids == rows_ref[...]).astype(jnp.bfloat16)
    total = jnp.dot(onehot, msg_ref[...], preferred_element_type=jnp.float32)
    ones = jnp.ones((slots, 128), jnp.bfloat16)
    count = jnp.dot(onehot, ones, preferred_element_type=jnp.float32)[:, :1]
    mean_msg = (total / jnp.maximum(count, 1.0)).astype(jnp.bfloat16)
    state = mem_ref[...]
    input_part = jnp.dot(mean_msg, win_ref[...], preferred_element_type=jnp.float32) + bin_ref[...]
    state_part = jnp.dot(state, whid_ref[...], preferred_element_type=jnp.float32)
    reset = gate(input_part[:, :width] + state_part[:, :width])
    update = gate(input_part[:, width : 2 * width] + state_part[:, width : 2 * width])
    candid = jnp.tanh(input_part[:, 2 * width :] + reset * state_part[:, 2 * width :])
    fresh = (1.0 - update) * candid + update * state.astype(jnp.float32)
    out_ref[...] = jnp.where(count > 0, fresh, state.astype(jnp.float32)).astype(out_ref.dtype)


def owner_update(row_flat, msg_flat, memory, w_gru_in, b_gru_in, w_gru_hid):
    rows_count, width = memory.shape
    slots, msg_width = msg_flat.shape
    block = 1024
    gates = w_gru_in.shape[1]
    return pl.pallas_call(
        update_kernel,
        grid=(rows_count // block,),
        in_specs=[
            pl.BlockSpec((1, slots), lambda i: (0, 0)),
            pl.BlockSpec((slots, msg_width), lambda i: (0, 0)),
            pl.BlockSpec((block, width), lambda i: (i, 0)),
            pl.BlockSpec((msg_width, gates), lambda i: (0, 0)),
            pl.BlockSpec((1, gates), lambda i: (0, 0)),
            pl.BlockSpec((width, gates), lambda i: (0, 0)),
        ],
        out_specs=pl.BlockSpec((block, width), lambda i: (i, 0)),
        out_shape=jax.ShapeDtypeStruct(memory.shape, memory.dtype),
    )(row_flat.reshape(1, slots), msg_flat, memory, w_gru_in, b_gru_in.reshape(1, gates), w_gru_hid)


def message_kernel(
    col_ref, row_ref, fetched_ref, edge_ref, time_ref, freq_ref, phase_ref, w_in_ref, w_out_ref, out_ref
):
    events = edge_ref.shape[0]
    slot_total = fetched_ref.shape[0]
    width = out_ref.shape[1]
    time_width = fetched_ref.shape[1] - width
    lane_ids = lax.broadcasted_iota(jnp.int32, (events, slot_total), 1)
    picked = []
    for side in range(2):
        pick = (lane_ids == col_ref[:, side : side + 1]).astype(jnp.bfloat16)
        rows = jnp.dot(pick, fetched_ref[...], preferred_element_type=jnp.float32)
        stamp = rows[:, width : width + 1].astype(jnp.int32) * 64
        stamp = stamp + rows[:, width + 1 : width + 2].astype(jnp.int32)
        delta = (time_ref[...] - stamp).astype(jnp.float32)
        encoded = jnp.cos(delta * freq_ref[...] + phase_ref[...]).astype(jnp.bfloat16)
        picked.append((rows[:, :width].astype(jnp.bfloat16), encoded))
    mem_src, enc_src = picked[0]
    mem_dst, enc_dst = picked[1]
    w_self = w_in_ref[:width]
    w_other = w_in_ref[width : 2 * width]
    w_time = w_in_ref[2 * width : 2 * width + time_width]
    edge = edge_ref[...]

    def message(own, other, enc):
        hidden = (
            jnp.dot(own, w_self, preferred_element_type=jnp.float32)
            + jnp.dot(other, w_other, preferred_element_type=jnp.float32)
            + jnp.dot(enc, w_time, preferred_element_type=jnp.float32)
            + edge
        )
        hidden = jnp.maximum(hidden, 0.0).astype(jnp.bfloat16)
        return jnp.dot(hidden, w_out_ref[...], preferred_element_type=jnp.float32).astype(jnp.bfloat16)

    sent = (message(mem_src, mem_dst, enc_src), message(mem_dst, mem_src, enc_dst))
    sub_ids = lax.broadcasted_iota(jnp.int32, (slot_total, events), 0)
    placed = [(sub_ids == row_ref[side : side + 1, :]).astype(jnp.bfloat16) for side in range(2)]
    out = jnp.dot(placed[0], sent[0], preferred_element_type=jnp.float32)
    out = out + jnp.dot(placed[1], sent[1], preferred_element_type=jnp.float32)
    out_ref[...] = out.astype(out_ref.dtype)


def event_messages(
    slot_ids, slot_cols, fetched, edge_part, event_time, time_freq, time_phase, w_msg_in, w_msg_out
):
    slot_total = fetched.shape[0]
    msg_width = w_msg_out.shape[1]
    return pl.pallas_call(
        message_kernel,
        out_shape=jax.ShapeDtypeStruct((slot_total, msg_width), jnp.bfloat16),
    )(
        slot_cols,
        slot_ids,
        fetched,
        edge_part,
        event_time.reshape(-1, 1),
        time_freq.reshape(1, -1),
        time_phase.reshape(1, -1),
        w_msg_in,
        w_msg_out,
    )


def prologue_kernel(owner_ref, src_row_ref, dst_row_ref, time_ref, slot_ref, slot_t_ref, request_ref):
    events = owner_ref.shape[1]
    owners = 128
    capacity = 8
    slot_total = request_ref.shape[1]
    chunk = slot_total // owners
    upper = (
        lax.broadcasted_iota(jnp.int32, (events, events), 0)
        < lax.broadcasted_iota(jnp.int32, (events, events), 1)
    ).astype(jnp.bfloat16)
    owner_ids = lax.broadcasted_iota(jnp.int32, (owners, events), 0)
    slots = []
    for side in range(2):
        owner_row = owner_ref[side : side + 1, :]
        onehot = owner_ids == owner_row
        earlier = jnp.dot(onehot.astype(jnp.bfloat16), upper, preferred_element_type=jnp.float32)
        position = jnp.sum(jnp.where(onehot, earlier, 0.0), axis=0, keepdims=True)
        slots.append(owner_row * chunk + side * capacity + position.astype(jnp.int32))
    slot_all = jnp.concatenate(slots, axis=1)
    rows_all = jnp.concatenate([src_row_ref[...], dst_row_ref[...]], axis=1)
    times_all = jnp.concatenate([time_ref[...], time_ref[...]], axis=1)
    zero = jnp.zeros_like(rows_all)
    digits = jnp.concatenate(
        [rows_all // 64, rows_all % 64, times_all // 64, times_all % 64, zero + 1, zero, zero, zero],
        axis=0,
    ).astype(jnp.float32)
    stacked = jnp.concatenate([slot_all] + [jnp.zeros_like(slot_all)] * 7, axis=0)
    columns = jnp.transpose(stacked)
    slot_col = columns[:, 0:1]
    lanes = lax.broadcasted_iota(jnp.int32, (2 * events, slot_total), 1)
    placed = (lanes == slot_col).astype(jnp.bfloat16)
    got = jnp.dot(digits.astype(jnp.bfloat16), placed, preferred_element_type=jnp.float32)
    got = got.astype(jnp.int32)
    row_request = jnp.where(got[4:5] > 0, got[0:1] * 64 + got[1:2], -1)
    request_ref[...] = row_request
    slot_ref[...] = jnp.concatenate(slots, axis=0)
    slot_t_ref[...] = jnp.concatenate([columns[:events, 0:1], columns[events:, 0:1]], axis=1)


def build_requests(src_owner, src_row, dst_owner, dst_row, event_time, slot_total):
    events = src_row.shape[0]
    owner_pair = jnp.concatenate([src_owner, dst_owner], axis=1).T
    return pl.pallas_call(
        prologue_kernel,
        out_shape=[
            jax.ShapeDtypeStruct((2, events), jnp.int32),
            jax.ShapeDtypeStruct((events, 2), jnp.int32),
            jax.ShapeDtypeStruct((1, slot_total), jnp.int32),
        ],
    )(owner_pair, src_row.reshape(1, events), dst_row.reshape(1, events), event_time.reshape(1, events))


def slot_of(owner_ids, owner_count, capacity):
    events_here = owner_ids.shape[0]
    columns = jnp.arange(owner_count, dtype=jnp.int32)
    onehot = (owner_ids[:, None] == columns[None, :]).astype(jnp.bfloat16)
    order = jnp.arange(events_here, dtype=jnp.int32)
    lower = (order[None, :] < order[:, None]).astype(jnp.bfloat16)
    earlier = jnp.dot(lower, onehot, preferred_element_type=jnp.float32)
    position = jnp.sum(earlier * onehot.astype(jnp.float32), axis=1).astype(jnp.int32)
    return owner_ids * capacity + position


def owner_lookup(row_request, memory, last_update, time_width):
    rows_count, width = memory.shape
    row_range = jnp.arange(rows_count, dtype=jnp.int32)
    select = (row_request[:, None] == row_range[None, :]).astype(jnp.bfloat16)
    digit_cols = jnp.arange(time_width, dtype=jnp.int32)
    digits = jnp.where(
        digit_cols[None, :] == 0,
        last_update[:, None] // 64,
        jnp.where(digit_cols[None, :] == 1, last_update[:, None] % 64, 0),
    ).astype(jnp.bfloat16)
    table = jnp.concatenate([memory, digits], axis=1)
    return jnp.dot(select, table, preferred_element_type=jnp.float32).astype(jnp.bfloat16)


def local(
    src_owner,
    src_row,
    dst_owner,
    dst_row,
    event_time,
    edge_feat,
    memory,
    last_update,
    time_freq,
    time_phase,
    w_msg_in,
    b_msg,
    w_msg_out,
    w_gru_in,
    b_gru_in,
    w_gru_hid,
):
    devices_all = lax.axis_size(("ev", "node"))
    events_here = edge_feat.shape[0]
    capacity = max(2, 2 * events_here // devices_all)
    chunk = 2 * capacity
    width = memory.shape[1]
    time_width = time_freq.shape[0]
    slot_total = devices_all * chunk
    slot_ids, slot_cols, request = build_requests(
        src_owner, src_row, dst_owner, dst_row, event_time, slot_total
    )
    request = request.reshape(slot_total)
    edge_part = (
        jnp.dot(edge_feat, w_msg_in[2 * width + time_width :], preferred_element_type=jnp.float32)
        + b_msg
    )
    rows_held = lax.all_to_all(request, ("ev", "node"), split_axis=0, concat_axis=0, tiled=True)
    served = owner_lookup(rows_held, memory, last_update, time_width)
    returned = lax.all_to_all(served, ("ev", "node"), split_axis=0, concat_axis=0, tiled=True)
    outgoing = event_messages(
        slot_ids, slot_cols, returned, edge_part, event_time, time_freq, time_phase, w_msg_in, w_msg_out
    )
    arrived = lax.all_to_all(outgoing, ("ev", "node"), split_axis=0, concat_axis=0, tiled=True)
    return owner_update(rows_held, arrived, memory, w_gru_in, b_gru_in, w_gru_hid)


def solution(mesh):
    in_specs = (
        P(("ev", "node"), None),
        P(("ev", "node")),
        P(("ev", "node"), None),
        P(("ev", "node")),
        P(("ev", "node")),
        P(("ev", "node"), None),
        P(("ev", "node"), None),
        P(("ev", "node")),
        P(),
        P(),
        P(),
        P(),
        P(),
        P(),
        P(),
        P(),
    )
    out_specs = P(("ev", "node"), None)
    return jax.shard_map(local, mesh=mesh, in_specs=in_specs, out_specs=out_specs, check_vma=False)
```

```python
import jax
import jax.numpy as jnp
from jax import lax
from jax.experimental import pallas as pl
from jax.sharding import PartitionSpec as P


def encode(delta_int, time_freq, time_phase):
    delta = delta_int.astype(jnp.float32)
    return jnp.cos(delta[..., None] * time_freq + time_phase).astype(jnp.bfloat16)


def gru_update(mean_msg, state, w_gru_in, b_gru_in, w_gru_hid):
    width = state.shape[-1]
    input_part = jnp.dot(mean_msg, w_gru_in, preferred_element_type=jnp.float32) + b_gru_in
    state_part = jnp.dot(state, w_gru_hid, preferred_element_type=jnp.float32)
    reset = jax.nn.sigmoid(input_part[:, :width] + state_part[:, :width])
    update = jax.nn.sigmoid(input_part[:, width : 2 * width] + state_part[:, width : 2 * width])
    candid = jnp.tanh(input_part[:, 2 * width :] + reset * state_part[:, 2 * width :])
    return ((1.0 - update) * candid + update * state.astype(jnp.float32)).astype(jnp.bfloat16)


def gate(x):
    return 0.5 + 0.5 * jnp.tanh(0.5 * x)


def update_kernel(rows_ref, count_ref, msg_ref, mem_ref, win_ref, bin_ref, whid_ref, out_ref):
    block = out_ref.shape[0]
    slots = rows_ref.shape[1]
    width = mem_ref.shape[1]
    ids = pl.program_id(0) * block + lax.broadcasted_iota(jnp.int32, (block, slots), 0)
    onehot = (ids == rows_ref[...]).astype(jnp.bfloat16)
    total = jnp.dot(onehot, msg_ref[...], preferred_element_type=jnp.float32)
    count = count_ref[...]
    mean_msg = (total / jnp.maximum(count, 1.0)).astype(jnp.bfloat16)
    state = mem_ref[...]
    input_part = jnp.dot(mean_msg, win_ref[...], preferred_element_type=jnp.float32) + bin_ref[...]
    state_part = jnp.dot(state, whid_ref[...], preferred_element_type=jnp.float32)
    reset = gate(input_part[:, :width] + state_part[:, :width])
    update = gate(input_part[:, width : 2 * width] + state_part[:, width : 2 * width])
    candid = jnp.tanh(input_part[:, 2 * width :] + reset * state_part[:, 2 * width :])
    fresh = (1.0 - update) * candid + update * state.astype(jnp.float32)
    out_ref[...] = jnp.where(count > 0, fresh, state.astype(jnp.float32)).astype(out_ref.dtype)


def owner_update(row_flat, msg_flat, memory, w_gru_in, b_gru_in, w_gru_hid):
    rows_count, width = memory.shape
    slots, msg_width = msg_flat.shape
    block = 1024
    gates = w_gru_in.shape[1]
    row_range = jnp.arange(rows_count, dtype=jnp.int32)
    hits = row_range[:, None] == row_flat[None, :]
    count = jnp.sum(hits.astype(jnp.float32), axis=1, keepdims=True)
    return pl.pallas_call(
        update_kernel,
        grid=(rows_count // block,),
        in_specs=[
            pl.BlockSpec((1, slots), lambda i: (0, 0)),
            pl.BlockSpec((block, 1), lambda i: (i, 0)),
            pl.BlockSpec((slots, msg_width), lambda i: (0, 0)),
            pl.BlockSpec((block, width), lambda i: (i, 0)),
            pl.BlockSpec((msg_width, gates), lambda i: (0, 0)),
            pl.BlockSpec((1, gates), lambda i: (0, 0)),
            pl.BlockSpec((width, gates), lambda i: (0, 0)),
        ],
        out_specs=pl.BlockSpec((block, width), lambda i: (i, 0)),
        out_shape=jax.ShapeDtypeStruct(memory.shape, memory.dtype),
    )(row_flat.reshape(1, slots), count, msg_flat, memory, w_gru_in, b_gru_in.reshape(1, gates), w_gru_hid)


def message_kernel(
    col_ref, row_ref, fetched_ref, edge_ref, time_ref, freq_ref, phase_ref, w_in_ref, w_out_ref, out_ref
):
    events = edge_ref.shape[0]
    slot_total = fetched_ref.shape[0]
    width = out_ref.shape[1]
    time_width = fetched_ref.shape[1] - width
    lane_ids = lax.broadcasted_iota(jnp.int32, (events, slot_total), 1)
    picked = []
    for side in range(2):
        pick = (lane_ids == col_ref[:, side : side + 1]).astype(jnp.bfloat16)
        rows = jnp.dot(pick, fetched_ref[...], preferred_element_type=jnp.float32)
        stamp = rows[:, width : width + 1].astype(jnp.int32) * 64
        stamp = stamp + rows[:, width + 1 : width + 2].astype(jnp.int32)
        delta = (time_ref[...] - stamp).astype(jnp.float32)
        encoded = jnp.cos(delta * freq_ref[...] + phase_ref[...]).astype(jnp.bfloat16)
        picked.append((rows[:, :width].astype(jnp.bfloat16), encoded))
    mem_src, enc_src = picked[0]
    mem_dst, enc_dst = picked[1]
    w_self = w_in_ref[:width]
    w_other = w_in_ref[width : 2 * width]
    w_time = w_in_ref[2 * width : 2 * width + time_width]
    edge = edge_ref[...]

    def message(own, other, enc):
        hidden = (
            jnp.dot(own, w_self, preferred_element_type=jnp.float32)
            + jnp.dot(other, w_other, preferred_element_type=jnp.float32)
            + jnp.dot(enc, w_time, preferred_element_type=jnp.float32)
            + edge
        )
        hidden = jnp.maximum(hidden, 0.0).astype(jnp.bfloat16)
        return jnp.dot(hidden, w_out_ref[...], preferred_element_type=jnp.float32).astype(jnp.bfloat16)

    sent = (message(mem_src, mem_dst, enc_src), message(mem_dst, mem_src, enc_dst))
    sub_ids = lax.broadcasted_iota(jnp.int32, (slot_total, events), 0)
    placed = [(sub_ids == row_ref[side : side + 1, :]).astype(jnp.bfloat16) for side in range(2)]
    out = jnp.dot(placed[0], sent[0], preferred_element_type=jnp.float32)
    out = out + jnp.dot(placed[1], sent[1], preferred_element_type=jnp.float32)
    out_ref[...] = out.astype(out_ref.dtype)


def event_messages(
    slot_ids, slot_cols, fetched, edge_part, event_time, time_freq, time_phase, w_msg_in, w_msg_out
):
    slot_total = fetched.shape[0]
    msg_width = w_msg_out.shape[1]
    return pl.pallas_call(
        message_kernel,
        out_shape=jax.ShapeDtypeStruct((slot_total, msg_width), jnp.bfloat16),
    )(
        slot_cols,
        slot_ids,
        fetched,
        edge_part,
        event_time.reshape(-1, 1),
        time_freq.reshape(1, -1),
        time_phase.reshape(1, -1),
        w_msg_in,
        w_msg_out,
    )


def prologue_kernel(owner_ref, src_row_ref, dst_row_ref, time_ref, slot_ref, slot_t_ref, request_ref):
    events = owner_ref.shape[1]
    owners = 128
    capacity = 8
    slot_total = request_ref.shape[1]
    chunk = slot_total // owners
    upper = (
        lax.broadcasted_iota(jnp.int32, (events, events), 0)
        < lax.broadcasted_iota(jnp.int32, (events, events), 1)
    ).astype(jnp.bfloat16)
    owner_ids = lax.broadcasted_iota(jnp.int32, (owners, events), 0)
    slots = []
    for side in range(2):
        owner_row = owner_ref[side : side + 1, :]
        onehot = owner_ids == owner_row
        earlier = jnp.dot(onehot.astype(jnp.bfloat16), upper, preferred_element_type=jnp.float32)
        position = jnp.sum(jnp.where(onehot, earlier, 0.0), axis=0, keepdims=True)
        slots.append(owner_row * chunk + side * capacity + position.astype(jnp.int32))
    slot_all = jnp.concatenate(slots, axis=1)
    rows_all = jnp.concatenate([src_row_ref[...], dst_row_ref[...]], axis=1)
    times_all = jnp.concatenate([time_ref[...], time_ref[...]], axis=1)
    zero = jnp.zeros_like(rows_all)
    digits = jnp.concatenate(
        [rows_all // 64, rows_all % 64, times_all // 64, times_all % 64, zero + 1, zero, zero, zero],
        axis=0,
    ).astype(jnp.float32)
    stacked = jnp.concatenate([slot_all] + [jnp.zeros_like(slot_all)] * 7, axis=0)
    columns = jnp.transpose(stacked)
    slot_col = columns[:, 0:1]
    lanes = lax.broadcasted_iota(jnp.int32, (2 * events, slot_total), 1)
    placed = (lanes == slot_col).astype(jnp.bfloat16)
    got = jnp.dot(digits.astype(jnp.bfloat16), placed, preferred_element_type=jnp.float32)
    got = got.astype(jnp.int32)
    row_request = jnp.where(got[4:5] > 0, got[0:1] * 64 + got[1:2], -1)
    request_ref[...] = row_request
    slot_ref[...] = jnp.concatenate(slots, axis=0)
    slot_t_ref[...] = jnp.concatenate([columns[:events, 0:1], columns[events:, 0:1]], axis=1)


def build_requests(src_owner, src_row, dst_owner, dst_row, event_time, slot_total):
    events = src_row.shape[0]
    owner_pair = jnp.concatenate([src_owner, dst_owner], axis=1).T
    return pl.pallas_call(
        prologue_kernel,
        out_shape=[
            jax.ShapeDtypeStruct((2, events), jnp.int32),
            jax.ShapeDtypeStruct((events, 2), jnp.int32),
            jax.ShapeDtypeStruct((1, slot_total), jnp.int32),
        ],
    )(owner_pair, src_row.reshape(1, events), dst_row.reshape(1, events), event_time.reshape(1, events))


def slot_of(owner_ids, owner_count, capacity):
    events_here = owner_ids.shape[0]
    columns = jnp.arange(owner_count, dtype=jnp.int32)
    onehot = (owner_ids[:, None] == columns[None, :]).astype(jnp.bfloat16)
    order = jnp.arange(events_here, dtype=jnp.int32)
    lower = (order[None, :] < order[:, None]).astype(jnp.bfloat16)
    earlier = jnp.dot(lower, onehot, preferred_element_type=jnp.float32)
    position = jnp.sum(earlier * onehot.astype(jnp.float32), axis=1).astype(jnp.int32)
    return owner_ids * capacity + position


def owner_lookup(row_request, memory, last_update, time_width):
    rows_count, width = memory.shape
    row_range = jnp.arange(rows_count, dtype=jnp.int32)
    select = (row_request[:, None] == row_range[None, :]).astype(jnp.bfloat16)
    digit_cols = jnp.arange(time_width, dtype=jnp.int32)
    digits = jnp.where(
        digit_cols[None, :] == 0,
        last_update[:, None] // 64,
        jnp.where(digit_cols[None, :] == 1, last_update[:, None] % 64, 0),
    ).astype(jnp.bfloat16)
    table = jnp.concatenate([memory, digits], axis=1)
    return jnp.dot(select, table, preferred_element_type=jnp.float32).astype(jnp.bfloat16)


def local(
    src_owner,
    src_row,
    dst_owner,
    dst_row,
    event_time,
    edge_feat,
    memory,
    last_update,
    time_freq,
    time_phase,
    w_msg_in,
    b_msg,
    w_msg_out,
    w_gru_in,
    b_gru_in,
    w_gru_hid,
):
    devices_all = lax.axis_size(("ev", "node"))
    events_here = edge_feat.shape[0]
    capacity = max(2, 2 * events_here // devices_all)
    chunk = 2 * capacity
    width = memory.shape[1]
    time_width = time_freq.shape[0]
    slot_total = devices_all * chunk
    slot_ids, slot_cols, request = build_requests(
        src_owner, src_row, dst_owner, dst_row, event_time, slot_total
    )
    request = request.reshape(slot_total)
    edge_part = (
        jnp.dot(edge_feat, w_msg_in[2 * width + time_width :], preferred_element_type=jnp.float32)
        + b_msg
    )
    rows_held = lax.all_to_all(request, ("ev", "node"), split_axis=0, concat_axis=0, tiled=True)
    served = owner_lookup(rows_held, memory, last_update, time_width)
    returned = lax.all_to_all(served, ("ev", "node"), split_axis=0, concat_axis=0, tiled=True)
    outgoing = event_messages(
        slot_ids, slot_cols, returned, edge_part, event_time, time_freq, time_phase, w_msg_in, w_msg_out
    )
    arrived = lax.all_to_all(outgoing, ("ev", "node"), split_axis=0, concat_axis=0, tiled=True)
    return owner_update(rows_held, arrived, memory, w_gru_in, b_gru_in, w_gru_hid)


def solution(mesh):
    in_specs = (
        P(("ev", "node"), None),
        P(("ev", "node")),
        P(("ev", "node"), None),
        P(("ev", "node")),
        P(("ev", "node")),
        P(("ev", "node"), None),
        P(("ev", "node"), None),
        P(("ev", "node")),
        P(),
        P(),
        P(),
        P(),
        P(),
        P(),
        P(),
        P(),
    )
    out_specs = P(("ev", "node"), None)
    return jax.shard_map(local, mesh=mesh, in_specs=in_specs, out_specs=out_specs, check_vma=False)
```

```python
import jax
import jax.numpy as jnp
from jax import lax
from jax.experimental import pallas as pl
from jax.sharding import PartitionSpec as P


def encode(delta_int, time_freq, time_phase):
    delta = delta_int.astype(jnp.float32)
    return jnp.cos(delta[..., None] * time_freq + time_phase).astype(jnp.bfloat16)


def gru_update(mean_msg, state, w_gru_in, b_gru_in, w_gru_hid):
    width = state.shape[-1]
    input_part = jnp.dot(mean_msg, w_gru_in, preferred_element_type=jnp.float32) + b_gru_in
    state_part = jnp.dot(state, w_gru_hid, preferred_element_type=jnp.float32)
    reset = jax.nn.sigmoid(input_part[:, :width] + state_part[:, :width])
    update = jax.nn.sigmoid(input_part[:, width : 2 * width] + state_part[:, width : 2 * width])
    candid = jnp.tanh(input_part[:, 2 * width :] + reset * state_part[:, 2 * width :])
    return ((1.0 - update) * candid + update * state.astype(jnp.float32)).astype(jnp.bfloat16)


def gate(x):
    return 0.5 + 0.5 * jnp.tanh(0.5 * x)


def update_kernel(rows_ref, msg_ref, mem_ref, win_ref, bin_ref, whid_ref, out_ref):
    block = out_ref.shape[0]
    slots = rows_ref.shape[1]
    width = mem_ref.shape[1]
    ids = pl.program_id(0) * block + lax.broadcasted_iota(jnp.int32, (block, slots), 0)
    onehot = (ids == rows_ref[...]).astype(jnp.bfloat16)
    total = jnp.dot(onehot, msg_ref[...], preferred_element_type=jnp.float32)
    ones = jnp.ones((slots, 128), jnp.bfloat16)
    count = jnp.dot(onehot, ones, preferred_element_type=jnp.float32)[:, :1]
    mean_msg = (total / jnp.maximum(count, 1.0)).astype(jnp.bfloat16)
    state = mem_ref[...]
    input_part = jnp.dot(mean_msg, win_ref[...], preferred_element_type=jnp.float32) + bin_ref[...]
    state_part = jnp.dot(state, whid_ref[...], preferred_element_type=jnp.float32)
    reset = gate(input_part[:, :width] + state_part[:, :width])
    update = gate(input_part[:, width : 2 * width] + state_part[:, width : 2 * width])
    candid = jnp.tanh(input_part[:, 2 * width :] + reset * state_part[:, 2 * width :])
    fresh = (1.0 - update) * candid + update * state.astype(jnp.float32)
    out_ref[...] = jnp.where(count > 0, fresh, state.astype(jnp.float32)).astype(out_ref.dtype)


def owner_update(row_flat, msg_flat, memory, w_gru_in, b_gru_in, w_gru_hid):
    rows_count, width = memory.shape
    slots, msg_width = msg_flat.shape
    block = 2048
    gates = w_gru_in.shape[1]
    return pl.pallas_call(
        update_kernel,
        grid=(rows_count // block,),
        in_specs=[
            pl.BlockSpec((1, slots), lambda i: (0, 0)),
            pl.BlockSpec((slots, msg_width), lambda i: (0, 0)),
            pl.BlockSpec((block, width), lambda i: (i, 0)),
            pl.BlockSpec((msg_width, gates), lambda i: (0, 0)),
            pl.BlockSpec((1, gates), lambda i: (0, 0)),
            pl.BlockSpec((width, gates), lambda i: (0, 0)),
        ],
        out_specs=pl.BlockSpec((block, width), lambda i: (i, 0)),
        out_shape=jax.ShapeDtypeStruct(memory.shape, memory.dtype),
    )(row_flat.reshape(1, slots), msg_flat, memory, w_gru_in, b_gru_in.reshape(1, gates), w_gru_hid)


def message_kernel(
    col_ref, row_ref, fetched_ref, edge_ref, time_ref, freq_ref, phase_ref, w_in_ref, w_out_ref, out_ref
):
    events = edge_ref.shape[0]
    slot_total = fetched_ref.shape[0]
    width = out_ref.shape[1]
    time_width = fetched_ref.shape[1] - width
    lane_ids = lax.broadcasted_iota(jnp.int32, (events, slot_total), 1)
    picked = []
    for side in range(2):
        pick = (lane_ids == col_ref[:, side : side + 1]).astype(jnp.bfloat16)
        rows = jnp.dot(pick, fetched_ref[...], preferred_element_type=jnp.float32)
        stamp = rows[:, width : width + 1].astype(jnp.int32) * 64
        stamp = stamp + rows[:, width + 1 : width + 2].astype(jnp.int32)
        delta = (time_ref[...] - stamp).astype(jnp.float32)
        encoded = jnp.cos(delta * freq_ref[...] + phase_ref[...]).astype(jnp.bfloat16)
        picked.append((rows[:, :width].astype(jnp.bfloat16), encoded))
    mem_src, enc_src = picked[0]
    mem_dst, enc_dst = picked[1]
    w_self = w_in_ref[:width]
    w_other = w_in_ref[width : 2 * width]
    w_time = w_in_ref[2 * width : 2 * width + time_width]
    edge = edge_ref[...]

    def message(own, other, enc):
        hidden = (
            jnp.dot(own, w_self, preferred_element_type=jnp.float32)
            + jnp.dot(other, w_other, preferred_element_type=jnp.float32)
            + jnp.dot(enc, w_time, preferred_element_type=jnp.float32)
            + edge
        )
        hidden = jnp.maximum(hidden, 0.0).astype(jnp.bfloat16)
        return jnp.dot(hidden, w_out_ref[...], preferred_element_type=jnp.float32).astype(jnp.bfloat16)

    sent = (message(mem_src, mem_dst, enc_src), message(mem_dst, mem_src, enc_dst))
    sub_ids = lax.broadcasted_iota(jnp.int32, (slot_total, events), 0)
    placed = [(sub_ids == row_ref[side : side + 1, :]).astype(jnp.bfloat16) for side in range(2)]
    out = jnp.dot(placed[0], sent[0], preferred_element_type=jnp.float32)
    out = out + jnp.dot(placed[1], sent[1], preferred_element_type=jnp.float32)
    out_ref[...] = out.astype(out_ref.dtype)


def event_messages(
    slot_ids, slot_cols, fetched, edge_part, event_time, time_freq, time_phase, w_msg_in, w_msg_out
):
    slot_total = fetched.shape[0]
    msg_width = w_msg_out.shape[1]
    return pl.pallas_call(
        message_kernel,
        out_shape=jax.ShapeDtypeStruct((slot_total, msg_width), jnp.bfloat16),
    )(
        slot_cols,
        slot_ids,
        fetched,
        edge_part,
        event_time.reshape(-1, 1),
        time_freq.reshape(1, -1),
        time_phase.reshape(1, -1),
        w_msg_in,
        w_msg_out,
    )


def prologue_kernel(owner_ref, src_row_ref, dst_row_ref, time_ref, slot_ref, slot_t_ref, request_ref):
    events = owner_ref.shape[1]
    owners = 128
    capacity = 8
    slot_total = request_ref.shape[1]
    chunk = slot_total // owners
    upper = (
        lax.broadcasted_iota(jnp.int32, (events, events), 0)
        < lax.broadcasted_iota(jnp.int32, (events, events), 1)
    ).astype(jnp.bfloat16)
    owner_ids = lax.broadcasted_iota(jnp.int32, (owners, events), 0)
    slots = []
    for side in range(2):
        owner_row = owner_ref[side : side + 1, :]
        onehot = owner_ids == owner_row
        earlier = jnp.dot(onehot.astype(jnp.bfloat16), upper, preferred_element_type=jnp.float32)
        position = jnp.sum(jnp.where(onehot, earlier, 0.0), axis=0, keepdims=True)
        slots.append(owner_row * chunk + side * capacity + position.astype(jnp.int32))
    slot_all = jnp.concatenate(slots, axis=1)
    rows_all = jnp.concatenate([src_row_ref[...], dst_row_ref[...]], axis=1)
    times_all = jnp.concatenate([time_ref[...], time_ref[...]], axis=1)
    zero = jnp.zeros_like(rows_all)
    digits = jnp.concatenate(
        [rows_all // 64, rows_all % 64, times_all // 64, times_all % 64, zero + 1, zero, zero, zero],
        axis=0,
    ).astype(jnp.float32)
    stacked = jnp.concatenate([slot_all] + [jnp.zeros_like(slot_all)] * 7, axis=0)
    columns = jnp.transpose(stacked)
    slot_col = columns[:, 0:1]
    lanes = lax.broadcasted_iota(jnp.int32, (2 * events, slot_total), 1)
    placed = (lanes == slot_col).astype(jnp.bfloat16)
    got = jnp.dot(digits.astype(jnp.bfloat16), placed, preferred_element_type=jnp.float32)
    got = got.astype(jnp.int32)
    row_request = jnp.where(got[4:5] > 0, got[0:1] * 64 + got[1:2], -1)
    request_ref[...] = row_request
    slot_ref[...] = jnp.concatenate(slots, axis=0)
    slot_t_ref[...] = jnp.concatenate([columns[:events, 0:1], columns[events:, 0:1]], axis=1)


def build_requests(src_owner, src_row, dst_owner, dst_row, event_time, slot_total):
    events = src_row.shape[0]
    owner_pair = jnp.concatenate([src_owner, dst_owner], axis=1).T
    return pl.pallas_call(
        prologue_kernel,
        out_shape=[
            jax.ShapeDtypeStruct((2, events), jnp.int32),
            jax.ShapeDtypeStruct((events, 2), jnp.int32),
            jax.ShapeDtypeStruct((1, slot_total), jnp.int32),
        ],
    )(owner_pair, src_row.reshape(1, events), dst_row.reshape(1, events), event_time.reshape(1, events))


def slot_of(owner_ids, owner_count, capacity):
    events_here = owner_ids.shape[0]
    columns = jnp.arange(owner_count, dtype=jnp.int32)
    onehot = (owner_ids[:, None] == columns[None, :]).astype(jnp.bfloat16)
    order = jnp.arange(events_here, dtype=jnp.int32)
    lower = (order[None, :] < order[:, None]).astype(jnp.bfloat16)
    earlier = jnp.dot(lower, onehot, preferred_element_type=jnp.float32)
    position = jnp.sum(earlier * onehot.astype(jnp.float32), axis=1).astype(jnp.int32)
    return owner_ids * capacity + position


def owner_lookup(row_request, memory, last_update, time_width):
    rows_count, width = memory.shape
    row_range = jnp.arange(rows_count, dtype=jnp.int32)
    select = (row_request[:, None] == row_range[None, :]).astype(jnp.bfloat16)
    digit_cols = jnp.arange(time_width, dtype=jnp.int32)
    digits = jnp.where(
        digit_cols[None, :] == 0,
        last_update[:, None] // 64,
        jnp.where(digit_cols[None, :] == 1, last_update[:, None] % 64, 0),
    ).astype(jnp.bfloat16)
    table = jnp.concatenate([memory, digits], axis=1)
    return jnp.dot(select, table, preferred_element_type=jnp.float32).astype(jnp.bfloat16)


def local(
    src_owner,
    src_row,
    dst_owner,
    dst_row,
    event_time,
    edge_feat,
    memory,
    last_update,
    time_freq,
    time_phase,
    w_msg_in,
    b_msg,
    w_msg_out,
    w_gru_in,
    b_gru_in,
    w_gru_hid,
):
    devices_all = lax.axis_size(("ev", "node"))
    events_here = edge_feat.shape[0]
    capacity = max(2, 2 * events_here // devices_all)
    chunk = 2 * capacity
    width = memory.shape[1]
    time_width = time_freq.shape[0]
    slot_total = devices_all * chunk
    slot_ids, slot_cols, request = build_requests(
        src_owner, src_row, dst_owner, dst_row, event_time, slot_total
    )
    request = request.reshape(slot_total)
    edge_part = (
        jnp.dot(edge_feat, w_msg_in[2 * width + time_width :], preferred_element_type=jnp.float32)
        + b_msg
    )
    rows_held = lax.all_to_all(request, ("ev", "node"), split_axis=0, concat_axis=0, tiled=True)
    served = owner_lookup(rows_held, memory, last_update, time_width)
    returned = lax.all_to_all(served, ("ev", "node"), split_axis=0, concat_axis=0, tiled=True)
    outgoing = event_messages(
        slot_ids, slot_cols, returned, edge_part, event_time, time_freq, time_phase, w_msg_in, w_msg_out
    )
    arrived = lax.all_to_all(outgoing, ("ev", "node"), split_axis=0, concat_axis=0, tiled=True)
    return owner_update(rows_held, arrived, memory, w_gru_in, b_gru_in, w_gru_hid)


def solution(mesh):
    in_specs = (
        P(("ev", "node"), None),
        P(("ev", "node")),
        P(("ev", "node"), None),
        P(("ev", "node")),
        P(("ev", "node")),
        P(("ev", "node"), None),
        P(("ev", "node"), None),
        P(("ev", "node")),
        P(),
        P(),
        P(),
        P(),
        P(),
        P(),
        P(),
        P(),
    )
    out_specs = P(("ev", "node"), None)
    return jax.shard_map(local, mesh=mesh, in_specs=in_specs, out_specs=out_specs, check_vma=False)
```

```python
import jax
import jax.numpy as jnp
from jax import lax
from jax.experimental import pallas as pl
from jax.experimental.pallas import tpu as pltpu
from jax.sharding import PartitionSpec as P


def encode(delta_int, time_freq, time_phase):
    delta = delta_int.astype(jnp.float32)
    return jnp.cos(delta[..., None] * time_freq + time_phase).astype(jnp.bfloat16)


def gru_update(mean_msg, state, w_gru_in, b_gru_in, w_gru_hid):
    width = state.shape[-1]
    input_part = jnp.dot(mean_msg, w_gru_in, preferred_element_type=jnp.float32) + b_gru_in
    state_part = jnp.dot(state, w_gru_hid, preferred_element_type=jnp.float32)
    reset = jax.nn.sigmoid(input_part[:, :width] + state_part[:, :width])
    update = jax.nn.sigmoid(input_part[:, width : 2 * width] + state_part[:, width : 2 * width])
    candid = jnp.tanh(input_part[:, 2 * width :] + reset * state_part[:, 2 * width :])
    return ((1.0 - update) * candid + update * state.astype(jnp.float32)).astype(jnp.bfloat16)


def gate(x):
    return 0.5 + 0.5 * jnp.tanh(0.5 * x)


def update_kernel(rows_ref, msg_ref, mem_ref, win_ref, bin_ref, whid_ref, out_ref):
    block = out_ref.shape[0]
    slots = rows_ref.shape[1]
    width = mem_ref.shape[1]
    ids = pl.program_id(0) * block + lax.broadcasted_iota(jnp.int32, (block, slots), 0)
    onehot = (ids == rows_ref[...]).astype(jnp.bfloat16)
    total = jnp.dot(onehot, msg_ref[...], preferred_element_type=jnp.float32)
    ones = jnp.ones((slots, 128), jnp.bfloat16)
    count = jnp.dot(onehot, ones, preferred_element_type=jnp.float32)[:, :1]
    mean_msg = (total / jnp.maximum(count, 1.0)).astype(jnp.bfloat16)
    state = mem_ref[...]
    input_part = jnp.dot(mean_msg, win_ref[...], preferred_element_type=jnp.float32) + bin_ref[...]
    state_part = jnp.dot(state, whid_ref[...], preferred_element_type=jnp.float32)
    reset = gate(input_part[:, :width] + state_part[:, :width])
    update = gate(input_part[:, width : 2 * width] + state_part[:, width : 2 * width])
    candid = jnp.tanh(input_part[:, 2 * width :] + reset * state_part[:, 2 * width :])
    fresh = (1.0 - update) * candid + update * state.astype(jnp.float32)
    out_ref[...] = jnp.where(count > 0, fresh, state.astype(jnp.float32)).astype(out_ref.dtype)


def owner_update(row_flat, msg_flat, memory, w_gru_in, b_gru_in, w_gru_hid):
    rows_count, width = memory.shape
    slots, msg_width = msg_flat.shape
    block = 1024
    gates = w_gru_in.shape[1]
    return pl.pallas_call(
        update_kernel,
        grid=(rows_count // block,),
        in_specs=[
            pl.BlockSpec((1, slots), lambda i: (0, 0)),
            pl.BlockSpec((slots, msg_width), lambda i: (0, 0)),
            pl.BlockSpec((block, width), lambda i: (i, 0)),
            pl.BlockSpec((msg_width, gates), lambda i: (0, 0)),
            pl.BlockSpec((1, gates), lambda i: (0, 0)),
            pl.BlockSpec((width, gates), lambda i: (0, 0)),
        ],
        out_specs=pl.BlockSpec((block, width), lambda i: (i, 0)),
        out_shape=jax.ShapeDtypeStruct(memory.shape, memory.dtype),
    )(row_flat.reshape(1, slots), msg_flat, memory, w_gru_in, b_gru_in.reshape(1, gates), w_gru_hid)


def message_kernel(
    col_ref,
    row_ref,
    fetched_ref,
    edge_hbm,
    time_ref,
    freq_ref,
    phase_ref,
    w_in_hbm,
    w_out_hbm,
    out_ref,
    edge_ref,
    w_in_ref,
    w_out_ref,
    sems,
):
    copies = [
        pltpu.make_async_copy(edge_hbm, edge_ref, sems.at[0]),
        pltpu.make_async_copy(w_in_hbm, w_in_ref, sems.at[1]),
        pltpu.make_async_copy(w_out_hbm, w_out_ref, sems.at[2]),
    ]
    for copy in copies:
        copy.start()
    events = edge_ref.shape[0]
    slot_total = fetched_ref.shape[0]
    width = out_ref.shape[1]
    time_width = fetched_ref.shape[1] - width
    lane_ids = lax.broadcasted_iota(jnp.int32, (events, slot_total), 1)
    picked = []
    for side in range(2):
        pick = (lane_ids == col_ref[:, side : side + 1]).astype(jnp.bfloat16)
        rows = jnp.dot(pick, fetched_ref[...], preferred_element_type=jnp.float32)
        stamp = rows[:, width : width + 1].astype(jnp.int32) * 64
        stamp = stamp + rows[:, width + 1 : width + 2].astype(jnp.int32)
        delta = (time_ref[...] - stamp).astype(jnp.float32)
        encoded = jnp.cos(delta * freq_ref[...] + phase_ref[...]).astype(jnp.bfloat16)
        picked.append((rows[:, :width].astype(jnp.bfloat16), encoded))
    mem_src, enc_src = picked[0]
    mem_dst, enc_dst = picked[1]
    for copy in copies:
        copy.wait()
    w_self = w_in_ref[:width]
    w_other = w_in_ref[width : 2 * width]
    w_time = w_in_ref[2 * width : 2 * width + time_width]
    edge = edge_ref[...]

    def message(own, other, enc):
        hidden = (
            jnp.dot(own, w_self, preferred_element_type=jnp.float32)
            + jnp.dot(other, w_other, preferred_element_type=jnp.float32)
            + jnp.dot(enc, w_time, preferred_element_type=jnp.float32)
            + edge
        )
        hidden = jnp.maximum(hidden, 0.0).astype(jnp.bfloat16)
        return jnp.dot(hidden, w_out_ref[...], preferred_element_type=jnp.float32).astype(jnp.bfloat16)

    sent = (message(mem_src, mem_dst, enc_src), message(mem_dst, mem_src, enc_dst))
    sub_ids = lax.broadcasted_iota(jnp.int32, (slot_total, events), 0)
    placed = [(sub_ids == row_ref[side : side + 1, :]).astype(jnp.bfloat16) for side in range(2)]
    out = jnp.dot(placed[0], sent[0], preferred_element_type=jnp.float32)
    out = out + jnp.dot(placed[1], sent[1], preferred_element_type=jnp.float32)
    out_ref[...] = out.astype(out_ref.dtype)


def event_messages(
    slot_ids, slot_cols, fetched, edge_part, event_time, time_freq, time_phase, w_msg_in, w_msg_out
):
    slot_total = fetched.shape[0]
    msg_width = w_msg_out.shape[1]
    here = pl.BlockSpec(memory_space=pltpu.VMEM)
    away = pl.BlockSpec(memory_space=pl.ANY)
    return pl.pallas_call(
        message_kernel,
        in_specs=[here, here, here, away, here, here, here, away, away],
        out_specs=here,
        scratch_shapes=[
            pltpu.VMEM(edge_part.shape, edge_part.dtype),
            pltpu.VMEM(w_msg_in.shape, w_msg_in.dtype),
            pltpu.VMEM(w_msg_out.shape, w_msg_out.dtype),
            pltpu.SemaphoreType.DMA((3,)),
        ],
        out_shape=jax.ShapeDtypeStruct((slot_total, msg_width), jnp.bfloat16),
    )(
        slot_cols,
        slot_ids,
        fetched,
        edge_part,
        event_time.reshape(-1, 1),
        time_freq.reshape(1, -1),
        time_phase.reshape(1, -1),
        w_msg_in,
        w_msg_out,
    )


def prologue_kernel(owner_ref, src_row_ref, dst_row_ref, time_ref, slot_ref, slot_t_ref, request_ref):
    events = owner_ref.shape[1]
    owners = 128
    capacity = 8
    slot_total = request_ref.shape[1]
    chunk = slot_total // owners
    upper = (
        lax.broadcasted_iota(jnp.int32, (events, events), 0)
        < lax.broadcasted_iota(jnp.int32, (events, events), 1)
    ).astype(jnp.bfloat16)
    owner_ids = lax.broadcasted_iota(jnp.int32, (owners, events), 0)
    slots = []
    for side in range(2):
        owner_row = owner_ref[side : side + 1, :]
        onehot = owner_ids == owner_row
        earlier = jnp.dot(onehot.astype(jnp.bfloat16), upper, preferred_element_type=jnp.float32)
        position = jnp.sum(jnp.where(onehot, earlier, 0.0), axis=0, keepdims=True)
        slots.append(owner_row * chunk + side * capacity + position.astype(jnp.int32))
    slot_all = jnp.concatenate(slots, axis=1)
    rows_all = jnp.concatenate([src_row_ref[...], dst_row_ref[...]], axis=1)
    times_all = jnp.concatenate([time_ref[...], time_ref[...]], axis=1)
    zero = jnp.zeros_like(rows_all)
    digits = jnp.concatenate(
        [rows_all // 64, rows_all % 64, times_all // 64, times_all % 64, zero + 1, zero, zero, zero],
        axis=0,
    ).astype(jnp.float32)
    stacked = jnp.concatenate([slot_all] + [jnp.zeros_like(slot_all)] * 7, axis=0)
    columns = jnp.transpose(stacked)
    slot_col = columns[:, 0:1]
    lanes = lax.broadcasted_iota(jnp.int32, (2 * events, slot_total), 1)
    placed = (lanes == slot_col).astype(jnp.bfloat16)
    got = jnp.dot(digits.astype(jnp.bfloat16), placed, preferred_element_type=jnp.float32)
    got = got.astype(jnp.int32)
    row_request = jnp.where(got[4:5] > 0, got[0:1] * 64 + got[1:2], -1)
    request_ref[...] = row_request
    slot_ref[...] = jnp.concatenate(slots, axis=0)
    slot_t_ref[...] = jnp.concatenate([columns[:events, 0:1], columns[events:, 0:1]], axis=1)


def build_requests(src_owner, src_row, dst_owner, dst_row, event_time, slot_total):
    events = src_row.shape[0]
    owner_pair = jnp.concatenate([src_owner, dst_owner], axis=1).T
    return pl.pallas_call(
        prologue_kernel,
        out_shape=[
            jax.ShapeDtypeStruct((2, events), jnp.int32),
            jax.ShapeDtypeStruct((events, 2), jnp.int32),
            jax.ShapeDtypeStruct((1, slot_total), jnp.int32),
        ],
    )(owner_pair, src_row.reshape(1, events), dst_row.reshape(1, events), event_time.reshape(1, events))


def slot_of(owner_ids, owner_count, capacity):
    events_here = owner_ids.shape[0]
    columns = jnp.arange(owner_count, dtype=jnp.int32)
    onehot = (owner_ids[:, None] == columns[None, :]).astype(jnp.bfloat16)
    order = jnp.arange(events_here, dtype=jnp.int32)
    lower = (order[None, :] < order[:, None]).astype(jnp.bfloat16)
    earlier = jnp.dot(lower, onehot, preferred_element_type=jnp.float32)
    position = jnp.sum(earlier * onehot.astype(jnp.float32), axis=1).astype(jnp.int32)
    return owner_ids * capacity + position


def owner_lookup(row_request, memory, last_update, time_width):
    rows_count, width = memory.shape
    row_range = jnp.arange(rows_count, dtype=jnp.int32)
    select = (row_request[:, None] == row_range[None, :]).astype(jnp.bfloat16)
    digit_cols = jnp.arange(time_width, dtype=jnp.int32)
    digits = jnp.where(
        digit_cols[None, :] == 0,
        last_update[:, None] // 64,
        jnp.where(digit_cols[None, :] == 1, last_update[:, None] % 64, 0),
    ).astype(jnp.bfloat16)
    table = jnp.concatenate([memory, digits], axis=1)
    return jnp.dot(select, table, preferred_element_type=jnp.float32).astype(jnp.bfloat16)


def local(
    src_owner,
    src_row,
    dst_owner,
    dst_row,
    event_time,
    edge_feat,
    memory,
    last_update,
    time_freq,
    time_phase,
    w_msg_in,
    b_msg,
    w_msg_out,
    w_gru_in,
    b_gru_in,
    w_gru_hid,
):
    devices_all = lax.axis_size(("ev", "node"))
    events_here = edge_feat.shape[0]
    capacity = max(2, 2 * events_here // devices_all)
    chunk = 2 * capacity
    width = memory.shape[1]
    time_width = time_freq.shape[0]
    slot_total = devices_all * chunk
    slot_ids, slot_cols, request = build_requests(
        src_owner, src_row, dst_owner, dst_row, event_time, slot_total
    )
    request = request.reshape(slot_total)
    edge_part = (
        jnp.dot(edge_feat, w_msg_in[2 * width + time_width :], preferred_element_type=jnp.float32)
        + b_msg
    )
    rows_held = lax.all_to_all(request, ("ev", "node"), split_axis=0, concat_axis=0, tiled=True)
    served = owner_lookup(rows_held, memory, last_update, time_width)
    returned = lax.all_to_all(served, ("ev", "node"), split_axis=0, concat_axis=0, tiled=True)
    outgoing = event_messages(
        slot_ids, slot_cols, returned, edge_part, event_time, time_freq, time_phase, w_msg_in, w_msg_out
    )
    arrived = lax.all_to_all(outgoing, ("ev", "node"), split_axis=0, concat_axis=0, tiled=True)
    return owner_update(rows_held, arrived, memory, w_gru_in, b_gru_in, w_gru_hid)


def solution(mesh):
    in_specs = (
        P(("ev", "node"), None),
        P(("ev", "node")),
        P(("ev", "node"), None),
        P(("ev", "node")),
        P(("ev", "node")),
        P(("ev", "node"), None),
        P(("ev", "node"), None),
        P(("ev", "node")),
        P(),
        P(),
        P(),
        P(),
        P(),
        P(),
        P(),
        P(),
    )
    out_specs = P(("ev", "node"), None)
    return jax.shard_map(local, mesh=mesh, in_specs=in_specs, out_specs=out_specs, check_vma=False)
```

```python
import jax
import jax.numpy as jnp
from jax import lax
from jax.experimental import pallas as pl
from jax.sharding import PartitionSpec as P


def encode(delta_int, time_freq, time_phase):
    delta = delta_int.astype(jnp.float32)
    return jnp.cos(delta[..., None] * time_freq + time_phase).astype(jnp.bfloat16)


def gru_update(mean_msg, state, w_gru_in, b_gru_in, w_gru_hid):
    width = state.shape[-1]
    input_part = jnp.dot(mean_msg, w_gru_in, preferred_element_type=jnp.float32) + b_gru_in
    state_part = jnp.dot(state, w_gru_hid, preferred_element_type=jnp.float32)
    reset = jax.nn.sigmoid(input_part[:, :width] + state_part[:, :width])
    update = jax.nn.sigmoid(input_part[:, width : 2 * width] + state_part[:, width : 2 * width])
    candid = jnp.tanh(input_part[:, 2 * width :] + reset * state_part[:, 2 * width :])
    return ((1.0 - update) * candid + update * state.astype(jnp.float32)).astype(jnp.bfloat16)


def gate(x):
    return 0.5 + 0.5 * jnp.tanh(0.5 * x)


def update_kernel(rows_ref, msg_ref, mem_ref, win_ref, bin_ref, whid_ref, out_ref):
    block = out_ref.shape[0]
    slots = rows_ref.shape[1]
    width = mem_ref.shape[1]
    ids = pl.program_id(0) * block + lax.broadcasted_iota(jnp.int32, (block, slots), 0)
    onehot = (ids == rows_ref[...]).astype(jnp.bfloat16)
    total = jnp.dot(onehot, msg_ref[...], preferred_element_type=jnp.float32)
    ones = jnp.ones((slots, 128), jnp.bfloat16)
    count = jnp.dot(onehot, ones, preferred_element_type=jnp.float32)[:, :1]
    mean_msg = (total / jnp.maximum(count, 1.0)).astype(jnp.bfloat16)
    state = mem_ref[...]
    input_part = jnp.dot(mean_msg, win_ref[...], preferred_element_type=jnp.float32) + bin_ref[...]
    state_part = jnp.dot(state, whid_ref[...], preferred_element_type=jnp.float32)
    reset = gate(input_part[:, :width] + state_part[:, :width])
    update = gate(input_part[:, width : 2 * width] + state_part[:, width : 2 * width])
    candid = jnp.tanh(input_part[:, 2 * width :] + reset * state_part[:, 2 * width :])
    fresh = (1.0 - update) * candid + update * state.astype(jnp.float32)
    out_ref[...] = jnp.where(count > 0, fresh, state.astype(jnp.float32)).astype(out_ref.dtype)


def owner_update(row_flat, msg_flat, memory, w_gru_in, b_gru_in, w_gru_hid):
    rows_count, width = memory.shape
    slots, msg_width = msg_flat.shape
    block = 1024
    gates = w_gru_in.shape[1]
    return pl.pallas_call(
        update_kernel,
        grid=(rows_count // block,),
        in_specs=[
            pl.BlockSpec((1, slots), lambda i: (0, 0)),
            pl.BlockSpec((slots, msg_width), lambda i: (0, 0)),
            pl.BlockSpec((block, width), lambda i: (i, 0)),
            pl.BlockSpec((msg_width, gates), lambda i: (0, 0)),
            pl.BlockSpec((1, gates), lambda i: (0, 0)),
            pl.BlockSpec((width, gates), lambda i: (0, 0)),
        ],
        out_specs=pl.BlockSpec((block, width), lambda i: (i, 0)),
        out_shape=jax.ShapeDtypeStruct(memory.shape, memory.dtype),
    )(row_flat.reshape(1, slots), msg_flat, memory, w_gru_in, b_gru_in.reshape(1, gates), w_gru_hid)


def message_kernel(
    col_ref, row_ref, fetched_ref, edge_ref, time_ref, freq_ref, phase_ref, w_in_ref, w_out_ref, out_ref
):
    events = edge_ref.shape[0]
    slot_total = fetched_ref.shape[0]
    width = out_ref.shape[1]
    time_width = fetched_ref.shape[1] - width
    lane_ids = lax.broadcasted_iota(jnp.int32, (events, slot_total), 1)
    picked = []
    for side in range(2):
        pick = (lane_ids == col_ref[:, side : side + 1]).astype(jnp.bfloat16)
        rows = jnp.dot(pick, fetched_ref[...], preferred_element_type=jnp.float32)
        stamp = rows[:, width : width + 1].astype(jnp.int32) * 64
        stamp = stamp + rows[:, width + 1 : width + 2].astype(jnp.int32)
        delta = (time_ref[...] - stamp).astype(jnp.float32)
        encoded = jnp.cos(delta * freq_ref[...] + phase_ref[...]).astype(jnp.bfloat16)
        picked.append((rows[:, :width].astype(jnp.bfloat16), encoded))
    mem_src, enc_src = picked[0]
    mem_dst, enc_dst = picked[1]
    w_self = w_in_ref[:width]
    w_other = w_in_ref[width : 2 * width]
    w_time = w_in_ref[2 * width : 2 * width + time_width]
    edge = edge_ref[...]

    def message(own, other, enc):
        hidden = (
            jnp.dot(own, w_self, preferred_element_type=jnp.float32)
            + jnp.dot(other, w_other, preferred_element_type=jnp.float32)
            + jnp.dot(enc, w_time, preferred_element_type=jnp.float32)
            + edge
        )
        hidden = jnp.maximum(hidden, 0.0).astype(jnp.bfloat16)
        return jnp.dot(hidden, w_out_ref[...], preferred_element_type=jnp.float32).astype(jnp.bfloat16)

    sent = (message(mem_src, mem_dst, enc_src), message(mem_dst, mem_src, enc_dst))
    sub_ids = lax.broadcasted_iota(jnp.int32, (slot_total, events), 0)
    placed = [(sub_ids == row_ref[side : side + 1, :]).astype(jnp.bfloat16) for side in range(2)]
    out = jnp.dot(placed[0], sent[0], preferred_element_type=jnp.float32)
    out = out + jnp.dot(placed[1], sent[1], preferred_element_type=jnp.float32)
    out_ref[...] = out.astype(out_ref.dtype)


def event_messages(
    slot_ids, slot_cols, fetched, edge_part, event_time, time_freq, time_phase, w_msg_in, w_msg_out
):
    slot_total = fetched.shape[0]
    msg_width = w_msg_out.shape[1]
    return pl.pallas_call(
        message_kernel,
        out_shape=jax.ShapeDtypeStruct((slot_total, msg_width), jnp.bfloat16),
    )(
        slot_cols,
        slot_ids,
        fetched,
        edge_part,
        event_time.reshape(-1, 1),
        time_freq.reshape(1, -1),
        time_phase.reshape(1, -1),
        w_msg_in,
        w_msg_out,
    )


def prologue_kernel(owner_ref, src_row_ref, dst_row_ref, time_ref, slot_ref, slot_t_ref, request_ref):
    events = owner_ref.shape[1]
    owners = 128
    capacity = 8
    slot_total = request_ref.shape[-1]
    chunk = slot_total // owners
    upper = (
        lax.broadcasted_iota(jnp.int32, (events, events), 0)
        < lax.broadcasted_iota(jnp.int32, (events, events), 1)
    ).astype(jnp.bfloat16)
    owner_ids = lax.broadcasted_iota(jnp.int32, (owners, events), 0)
    slots = []
    for side in range(2):
        owner_row = owner_ref[side : side + 1, :]
        onehot = owner_ids == owner_row
        earlier = jnp.dot(onehot.astype(jnp.bfloat16), upper, preferred_element_type=jnp.float32)
        position = jnp.sum(jnp.where(onehot, earlier, 0.0), axis=0, keepdims=True)
        slots.append(owner_row * chunk + side * capacity + position.astype(jnp.int32))
    slot_all = jnp.concatenate(slots, axis=1)
    rows_all = jnp.concatenate([src_row_ref[...], dst_row_ref[...]], axis=1)
    times_all = jnp.concatenate([time_ref[...], time_ref[...]], axis=1)
    zero = jnp.zeros_like(rows_all)
    digits = jnp.concatenate(
        [rows_all // 64, rows_all % 64, times_all // 64, times_all % 64, zero + 1, zero, zero, zero],
        axis=0,
    ).astype(jnp.float32)
    stacked = jnp.concatenate([slot_all] + [jnp.zeros_like(slot_all)] * 7, axis=0)
    columns = jnp.transpose(stacked)
    slot_col = columns[:, 0:1]
    lanes = lax.broadcasted_iota(jnp.int32, (2 * events, slot_total), 1)
    placed = (lanes == slot_col).astype(jnp.bfloat16)
    got = jnp.dot(digits.astype(jnp.bfloat16), placed, preferred_element_type=jnp.float32)
    got = got.astype(jnp.int32)
    row_request = jnp.where(got[4:5] > 0, got[0:1] * 64 + got[1:2], -1)
    request_ref[...] = row_request.reshape(request_ref.shape)
    slot_ref[...] = jnp.concatenate(slots, axis=0)
    slot_t_ref[...] = jnp.concatenate([columns[:events, 0:1], columns[events:, 0:1]], axis=1)


def build_requests(src_owner, src_row, dst_owner, dst_row, event_time, slot_total):
    events = src_row.shape[0]
    owner_pair = jnp.concatenate([src_owner, dst_owner], axis=1).T
    return pl.pallas_call(
        prologue_kernel,
        out_shape=[
            jax.ShapeDtypeStruct((2, events), jnp.int32),
            jax.ShapeDtypeStruct((events, 2), jnp.int32),
            jax.ShapeDtypeStruct((slot_total,), jnp.int32),
        ],
    )(owner_pair, src_row.reshape(1, events), dst_row.reshape(1, events), event_time.reshape(1, events))


def slot_of(owner_ids, owner_count, capacity):
    events_here = owner_ids.shape[0]
    columns = jnp.arange(owner_count, dtype=jnp.int32)
    onehot = (owner_ids[:, None] == columns[None, :]).astype(jnp.bfloat16)
    order = jnp.arange(events_here, dtype=jnp.int32)
    lower = (order[None, :] < order[:, None]).astype(jnp.bfloat16)
    earlier = jnp.dot(lower, onehot, preferred_element_type=jnp.float32)
    position = jnp.sum(earlier * onehot.astype(jnp.float32), axis=1).astype(jnp.int32)
    return owner_ids * capacity + position


def owner_lookup(row_request, memory, last_update, time_width):
    rows_count, width = memory.shape
    row_range = jnp.arange(rows_count, dtype=jnp.int32)
    select = (row_request[:, None] == row_range[None, :]).astype(jnp.bfloat16)
    digit_cols = jnp.arange(time_width, dtype=jnp.int32)
    digits = jnp.where(
        digit_cols[None, :] == 0,
        last_update[:, None] // 64,
        jnp.where(digit_cols[None, :] == 1, last_update[:, None] % 64, 0),
    ).astype(jnp.bfloat16)
    table = jnp.concatenate([memory, digits], axis=1)
    return jnp.dot(select, table, preferred_element_type=jnp.float32).astype(jnp.bfloat16)


def local(
    src_owner,
    src_row,
    dst_owner,
    dst_row,
    event_time,
    edge_feat,
    memory,
    last_update,
    time_freq,
    time_phase,
    w_msg_in,
    b_msg,
    w_msg_out,
    w_gru_in,
    b_gru_in,
    w_gru_hid,
):
    devices_all = lax.axis_size(("ev", "node"))
    events_here = edge_feat.shape[0]
    capacity = max(2, 2 * events_here // devices_all)
    chunk = 2 * capacity
    width = memory.shape[1]
    time_width = time_freq.shape[0]
    slot_total = devices_all * chunk
    slot_ids, slot_cols, request = build_requests(
        src_owner, src_row, dst_owner, dst_row, event_time, slot_total
    )
    request = request.reshape(slot_total)
    edge_part = (
        jnp.dot(edge_feat, w_msg_in[2 * width + time_width :], preferred_element_type=jnp.float32)
        + b_msg
    )
    rows_held = lax.all_to_all(request, ("ev", "node"), split_axis=0, concat_axis=0, tiled=True)
    served = owner_lookup(rows_held, memory, last_update, time_width)
    returned = lax.all_to_all(served, ("ev", "node"), split_axis=0, concat_axis=0, tiled=True)
    outgoing = event_messages(
        slot_ids, slot_cols, returned, edge_part, event_time, time_freq, time_phase, w_msg_in, w_msg_out
    )
    arrived = lax.all_to_all(outgoing, ("ev", "node"), split_axis=0, concat_axis=0, tiled=True)
    return owner_update(rows_held, arrived, memory, w_gru_in, b_gru_in, w_gru_hid)


def solution(mesh):
    in_specs = (
        P(("ev", "node"), None),
        P(("ev", "node")),
        P(("ev", "node"), None),
        P(("ev", "node")),
        P(("ev", "node")),
        P(("ev", "node"), None),
        P(("ev", "node"), None),
        P(("ev", "node")),
        P(),
        P(),
        P(),
        P(),
        P(),
        P(),
        P(),
        P(),
    )
    out_specs = P(("ev", "node"), None)
    return jax.shard_map(local, mesh=mesh, in_specs=in_specs, out_specs=out_specs, check_vma=False)
```

```python
import jax
import jax.numpy as jnp
from jax import lax
from jax.experimental import pallas as pl
from jax.sharding import PartitionSpec as P


def encode(delta_int, time_freq, time_phase):
    delta = delta_int.astype(jnp.float32)
    return jnp.cos(delta[..., None] * time_freq + time_phase).astype(jnp.bfloat16)


def gru_update(mean_msg, state, w_gru_in, b_gru_in, w_gru_hid):
    width = state.shape[-1]
    input_part = jnp.dot(mean_msg, w_gru_in, preferred_element_type=jnp.float32) + b_gru_in
    state_part = jnp.dot(state, w_gru_hid, preferred_element_type=jnp.float32)
    reset = jax.nn.sigmoid(input_part[:, :width] + state_part[:, :width])
    update = jax.nn.sigmoid(input_part[:, width : 2 * width] + state_part[:, width : 2 * width])
    candid = jnp.tanh(input_part[:, 2 * width :] + reset * state_part[:, 2 * width :])
    return ((1.0 - update) * candid + update * state.astype(jnp.float32)).astype(jnp.bfloat16)


def gate(x):
    return 0.5 + 0.5 * jnp.tanh(0.5 * x)


def update_kernel(rows_ref, msg_ref, mem_ref, win_ref, bin_ref, whid_ref, out_ref):
    block = out_ref.shape[0]
    slots = rows_ref.shape[1]
    width = mem_ref.shape[1]
    ids = pl.program_id(0) * block + lax.broadcasted_iota(jnp.int32, (block, slots), 0)
    onehot = (ids == rows_ref[...]).astype(jnp.bfloat16)
    total = jnp.dot(onehot, msg_ref[...], preferred_element_type=jnp.float32)
    ones = jnp.ones((slots, 128), jnp.bfloat16)
    count = jnp.dot(onehot, ones, preferred_element_type=jnp.float32)[:, :1]
    mean_msg = (total / jnp.maximum(count, 1.0)).astype(jnp.bfloat16)
    state = mem_ref[...]
    input_part = jnp.dot(mean_msg, win_ref[...], preferred_element_type=jnp.float32) + bin_ref[...]
    state_part = jnp.dot(state, whid_ref[...], preferred_element_type=jnp.float32)
    reset = gate(input_part[:, :width] + state_part[:, :width])
    update = gate(input_part[:, width : 2 * width] + state_part[:, width : 2 * width])
    candid = jnp.tanh(input_part[:, 2 * width :] + reset * state_part[:, 2 * width :])
    fresh = (1.0 - update) * candid + update * state.astype(jnp.float32)
    out_ref[...] = jnp.where(count > 0, fresh, state.astype(jnp.float32)).astype(out_ref.dtype)


def owner_update(row_flat, msg_flat, memory, w_gru_in, b_gru_in, w_gru_hid):
    rows_count, width = memory.shape
    slots, msg_width = msg_flat.shape
    block = 1024
    gates = w_gru_in.shape[1]
    return pl.pallas_call(
        update_kernel,
        grid=(rows_count // block,),
        in_specs=[
            pl.BlockSpec((1, slots), lambda i: (0, 0)),
            pl.BlockSpec((slots, msg_width), lambda i: (0, 0)),
            pl.BlockSpec((block, width), lambda i: (i, 0)),
            pl.BlockSpec((msg_width, gates), lambda i: (0, 0)),
            pl.BlockSpec((1, gates), lambda i: (0, 0)),
            pl.BlockSpec((width, gates), lambda i: (0, 0)),
        ],
        out_specs=pl.BlockSpec((block, width), lambda i: (i, 0)),
        out_shape=jax.ShapeDtypeStruct(memory.shape, memory.dtype),
    )(row_flat.reshape(1, slots), msg_flat, memory, w_gru_in, b_gru_in.reshape(1, gates), w_gru_hid)


def message_kernel(
    col_ref, row_ref, fetched_ref, edge_ref, time_ref, freq_ref, phase_ref, w_in_ref, w_out_ref, out_ref
):
    events = edge_ref.shape[0]
    slot_total = fetched_ref.shape[0]
    width = out_ref.shape[1]
    time_width = fetched_ref.shape[1] - width
    lane_ids = lax.broadcasted_iota(jnp.int32, (events, slot_total), 1)
    picked = []
    for side in range(2):
        pick = (lane_ids == col_ref[:, side : side + 1]).astype(jnp.bfloat16)
        rows = jnp.dot(pick, fetched_ref[...], preferred_element_type=jnp.float32)
        stamp = rows[:, width : width + 1].astype(jnp.int32) * 64
        stamp = stamp + rows[:, width + 1 : width + 2].astype(jnp.int32)
        delta = (time_ref[...] - stamp).astype(jnp.float32)
        encoded = jnp.cos(delta * freq_ref[...] + phase_ref[...]).astype(jnp.bfloat16)
        picked.append((rows[:, :width].astype(jnp.bfloat16), encoded))
    mem_src, enc_src = picked[0]
    mem_dst, enc_dst = picked[1]
    w_self = w_in_ref[:width]
    w_other = w_in_ref[width : 2 * width]
    w_time = w_in_ref[2 * width : 2 * width + time_width]
    edge = edge_ref[...]

    def message(own, other, enc):
        hidden = (
            jnp.dot(own, w_self, preferred_element_type=jnp.float32)
            + jnp.dot(other, w_other, preferred_element_type=jnp.float32)
            + jnp.dot(enc, w_time, preferred_element_type=jnp.float32)
            + edge
        )
        hidden = jnp.maximum(hidden, 0.0).astype(jnp.bfloat16)
        return jnp.dot(hidden, w_out_ref[...], preferred_element_type=jnp.float32).astype(jnp.bfloat16)

    sent = (message(mem_src, mem_dst, enc_src), message(mem_dst, mem_src, enc_dst))
    sub_ids = lax.broadcasted_iota(jnp.int32, (slot_total, events), 0)
    placed = [(sub_ids == row_ref[side : side + 1, :]).astype(jnp.bfloat16) for side in range(2)]
    out = jnp.dot(placed[0], sent[0], preferred_element_type=jnp.float32)
    out = out + jnp.dot(placed[1], sent[1], preferred_element_type=jnp.float32)
    out_ref[...] = out.astype(out_ref.dtype)


def event_messages(
    slot_ids, slot_cols, fetched, edge_part, event_time, time_freq, time_phase, w_msg_in, w_msg_out
):
    slot_total = fetched.shape[0]
    msg_width = w_msg_out.shape[1]
    return pl.pallas_call(
        message_kernel,
        out_shape=jax.ShapeDtypeStruct((slot_total, msg_width), jnp.bfloat16),
    )(
        slot_cols,
        slot_ids,
        fetched,
        edge_part,
        event_time.reshape(-1, 1),
        time_freq.reshape(1, -1),
        time_phase.reshape(1, -1),
        w_msg_in,
        w_msg_out,
    )


def prologue_kernel(
    src_owner_ref, dst_owner_ref, src_row_ref, dst_row_ref, time_ref, slot_ref, slot_t_ref, request_ref
):
    events = src_owner_ref.shape[1]
    owners = 128
    capacity = 8
    slot_total = request_ref.shape[-1]
    chunk = slot_total // owners
    upper = (
        lax.broadcasted_iota(jnp.int32, (events, events), 0)
        < lax.broadcasted_iota(jnp.int32, (events, events), 1)
    ).astype(jnp.bfloat16)
    owner_ids = lax.broadcasted_iota(jnp.int32, (owners, events), 0)
    slots = []
    for side in range(2):
        owner_row = (src_owner_ref, dst_owner_ref)[side][...]
        onehot = owner_ids == owner_row
        earlier = jnp.dot(onehot.astype(jnp.bfloat16), upper, preferred_element_type=jnp.float32)
        position = jnp.sum(jnp.where(onehot, earlier, 0.0), axis=0, keepdims=True)
        slots.append(owner_row * chunk + side * capacity + position.astype(jnp.int32))
    slot_all = jnp.concatenate(slots, axis=1)
    rows_all = jnp.concatenate([src_row_ref[...], dst_row_ref[...]], axis=1)
    times_all = jnp.concatenate([time_ref[...], time_ref[...]], axis=1)
    zero = jnp.zeros_like(rows_all)
    digits = jnp.concatenate(
        [rows_all // 64, rows_all % 64, times_all // 64, times_all % 64, zero + 1, zero, zero, zero],
        axis=0,
    ).astype(jnp.float32)
    stacked = jnp.concatenate([slot_all] + [jnp.zeros_like(slot_all)] * 7, axis=0)
    columns = jnp.transpose(stacked)
    slot_col = columns[:, 0:1]
    lanes = lax.broadcasted_iota(jnp.int32, (2 * events, slot_total), 1)
    placed = (lanes == slot_col).astype(jnp.bfloat16)
    got = jnp.dot(digits.astype(jnp.bfloat16), placed, preferred_element_type=jnp.float32)
    got = got.astype(jnp.int32)
    row_request = jnp.where(got[4:5] > 0, got[0:1] * 64 + got[1:2], -1)
    request_ref[...] = row_request.reshape(request_ref.shape)
    slot_ref[...] = jnp.concatenate(slots, axis=0)
    slot_t_ref[...] = jnp.concatenate([columns[:events, 0:1], columns[events:, 0:1]], axis=1)


def build_requests(src_owner, src_row, dst_owner, dst_row, event_time, slot_total):
    events = src_row.shape[0]
    return pl.pallas_call(
        prologue_kernel,
        out_shape=[
            jax.ShapeDtypeStruct((2, events), jnp.int32),
            jax.ShapeDtypeStruct((events, 2), jnp.int32),
            jax.ShapeDtypeStruct((slot_total,), jnp.int32),
        ],
    )(
        src_owner.reshape(1, events),
        dst_owner.reshape(1, events),
        src_row.reshape(1, events), dst_row.reshape(1, events), event_time.reshape(1, events))


def slot_of(owner_ids, owner_count, capacity):
    events_here = owner_ids.shape[0]
    columns = jnp.arange(owner_count, dtype=jnp.int32)
    onehot = (owner_ids[:, None] == columns[None, :]).astype(jnp.bfloat16)
    order = jnp.arange(events_here, dtype=jnp.int32)
    lower = (order[None, :] < order[:, None]).astype(jnp.bfloat16)
    earlier = jnp.dot(lower, onehot, preferred_element_type=jnp.float32)
    position = jnp.sum(earlier * onehot.astype(jnp.float32), axis=1).astype(jnp.int32)
    return owner_ids * capacity + position


def owner_lookup(row_request, memory, last_update, time_width):
    rows_count, width = memory.shape
    row_range = jnp.arange(rows_count, dtype=jnp.int32)
    select = (row_request[:, None] == row_range[None, :]).astype(jnp.bfloat16)
    digit_cols = jnp.arange(time_width, dtype=jnp.int32)
    digits = jnp.where(
        digit_cols[None, :] == 0,
        last_update[:, None] // 64,
        jnp.where(digit_cols[None, :] == 1, last_update[:, None] % 64, 0),
    ).astype(jnp.bfloat16)
    table = jnp.concatenate([memory, digits], axis=1)
    return jnp.dot(select, table, preferred_element_type=jnp.float32).astype(jnp.bfloat16)


def local(
    src_owner,
    src_row,
    dst_owner,
    dst_row,
    event_time,
    edge_feat,
    memory,
    last_update,
    time_freq,
    time_phase,
    w_msg_in,
    b_msg,
    w_msg_out,
    w_gru_in,
    b_gru_in,
    w_gru_hid,
):
    devices_all = lax.axis_size(("ev", "node"))
    events_here = edge_feat.shape[0]
    capacity = max(2, 2 * events_here // devices_all)
    chunk = 2 * capacity
    width = memory.shape[1]
    time_width = time_freq.shape[0]
    slot_total = devices_all * chunk
    slot_ids, slot_cols, request = build_requests(
        src_owner, src_row, dst_owner, dst_row, event_time, slot_total
    )
    request = request.reshape(slot_total)
    edge_part = (
        jnp.dot(edge_feat, w_msg_in[2 * width + time_width :], preferred_element_type=jnp.float32)
        + b_msg
    )
    rows_held = lax.all_to_all(request, ("ev", "node"), split_axis=0, concat_axis=0, tiled=True)
    served = owner_lookup(rows_held, memory, last_update, time_width)
    returned = lax.all_to_all(served, ("ev", "node"), split_axis=0, concat_axis=0, tiled=True)
    outgoing = event_messages(
        slot_ids, slot_cols, returned, edge_part, event_time, time_freq, time_phase, w_msg_in, w_msg_out
    )
    arrived = lax.all_to_all(outgoing, ("ev", "node"), split_axis=0, concat_axis=0, tiled=True)
    return owner_update(rows_held, arrived, memory, w_gru_in, b_gru_in, w_gru_hid)


def solution(mesh):
    in_specs = (
        P(("ev", "node"), None),
        P(("ev", "node")),
        P(("ev", "node"), None),
        P(("ev", "node")),
        P(("ev", "node")),
        P(("ev", "node"), None),
        P(("ev", "node"), None),
        P(("ev", "node")),
        P(),
        P(),
        P(),
        P(),
        P(),
        P(),
        P(),
        P(),
    )
    out_specs = P(("ev", "node"), None)
    return jax.shard_map(local, mesh=mesh, in_specs=in_specs, out_specs=out_specs, check_vma=False)
```

```python
import jax
import jax.numpy as jnp
from jax import lax
from jax.experimental import pallas as pl
from jax.sharding import PartitionSpec as P


def encode(delta_int, time_freq, time_phase):
    delta = delta_int.astype(jnp.float32)
    return jnp.cos(delta[..., None] * time_freq + time_phase).astype(jnp.bfloat16)


def gru_update(mean_msg, state, w_gru_in, b_gru_in, w_gru_hid):
    width = state.shape[-1]
    input_part = jnp.dot(mean_msg, w_gru_in, preferred_element_type=jnp.float32) + b_gru_in
    state_part = jnp.dot(state, w_gru_hid, preferred_element_type=jnp.float32)
    reset = jax.nn.sigmoid(input_part[:, :width] + state_part[:, :width])
    update = jax.nn.sigmoid(input_part[:, width : 2 * width] + state_part[:, width : 2 * width])
    candid = jnp.tanh(input_part[:, 2 * width :] + reset * state_part[:, 2 * width :])
    return ((1.0 - update) * candid + update * state.astype(jnp.float32)).astype(jnp.bfloat16)


def gate(x):
    return 0.5 + 0.5 * jnp.tanh(0.5 * x)


def update_kernel(rows_ref, msg_ref, mem_ref, win_ref, bin_ref, whid_ref, out_ref):
    block = out_ref.shape[0]
    slots = rows_ref.shape[1]
    width = mem_ref.shape[1]
    ids = pl.program_id(0) * block + lax.broadcasted_iota(jnp.int32, (block, slots), 0)
    onehot = (ids == rows_ref[...]).astype(jnp.bfloat16)
    total = jnp.dot(onehot, msg_ref[...], preferred_element_type=jnp.float32)
    ones = jnp.ones((slots, 128), jnp.bfloat16)
    count = jnp.dot(onehot, ones, preferred_element_type=jnp.float32)[:, :1]
    mean_msg = (total / jnp.maximum(count, 1.0)).astype(jnp.bfloat16)
    state = mem_ref[...]
    input_part = jnp.dot(mean_msg, win_ref[...], preferred_element_type=jnp.float32) + bin_ref[...]
    state_part = jnp.dot(state, whid_ref[...], preferred_element_type=jnp.float32)
    reset = gate(input_part[:, :width] + state_part[:, :width])
    update = gate(input_part[:, width : 2 * width] + state_part[:, width : 2 * width])
    candid = jnp.tanh(input_part[:, 2 * width :] + reset * state_part[:, 2 * width :])
    fresh = (1.0 - update) * candid + update * state.astype(jnp.float32)
    out_ref[...] = jnp.where(count > 0, fresh, state.astype(jnp.float32)).astype(out_ref.dtype)


def owner_update(row_flat, msg_flat, memory, w_gru_in, b_gru_in, w_gru_hid):
    rows_count, width = memory.shape
    slots, msg_width = msg_flat.shape
    block = 1024
    gates = w_gru_in.shape[1]
    return pl.pallas_call(
        update_kernel,
        grid=(rows_count // block,),
        in_specs=[
            pl.BlockSpec((1, slots), lambda i: (0, 0)),
            pl.BlockSpec((slots, msg_width), lambda i: (0, 0)),
            pl.BlockSpec((block, width), lambda i: (i, 0)),
            pl.BlockSpec((msg_width, gates), lambda i: (0, 0)),
            pl.BlockSpec((1, gates), lambda i: (0, 0)),
            pl.BlockSpec((width, gates), lambda i: (0, 0)),
        ],
        out_specs=pl.BlockSpec((block, width), lambda i: (i, 0)),
        out_shape=jax.ShapeDtypeStruct(memory.shape, memory.dtype),
    )(row_flat.reshape(1, slots), msg_flat, memory, w_gru_in, b_gru_in.reshape(1, gates), w_gru_hid)


def message_kernel(
    col_ref, row_ref, fetched_ref, edge_ref, time_ref, freq_ref, phase_ref, w_in_ref, w_out_ref, out_ref
):
    events = edge_ref.shape[0]
    slot_total = fetched_ref.shape[0]
    width = out_ref.shape[1]
    time_width = fetched_ref.shape[1] - width
    lane_ids = lax.broadcasted_iota(jnp.int32, (events, slot_total), 1)
    picked = []
    for side in range(2):
        pick = (lane_ids == col_ref[:, side : side + 1]).astype(jnp.bfloat16)
        rows = jnp.dot(pick, fetched_ref[...], preferred_element_type=jnp.float32)
        stamp = rows[:, width : width + 1].astype(jnp.int32) * 64
        stamp = stamp + rows[:, width + 1 : width + 2].astype(jnp.int32)
        delta = (time_ref[...] - stamp).astype(jnp.float32)
        encoded = jnp.cos(delta * freq_ref[...] + phase_ref[...]).astype(jnp.bfloat16)
        picked.append((rows[:, :width].astype(jnp.bfloat16), encoded))
    mem_src, enc_src = picked[0]
    mem_dst, enc_dst = picked[1]
    w_self = w_in_ref[:width]
    w_other = w_in_ref[width : 2 * width]
    w_time = w_in_ref[2 * width : 2 * width + time_width]
    edge = edge_ref[...]

    def message(own, other, enc):
        hidden = (
            jnp.dot(own, w_self, preferred_element_type=jnp.float32)
            + jnp.dot(other, w_other, preferred_element_type=jnp.float32)
            + jnp.dot(enc, w_time, preferred_element_type=jnp.float32)
            + edge
        )
        hidden = jnp.maximum(hidden, 0.0).astype(jnp.bfloat16)
        return jnp.dot(hidden, w_out_ref[...], preferred_element_type=jnp.float32).astype(jnp.bfloat16)

    sent = (message(mem_src, mem_dst, enc_src), message(mem_dst, mem_src, enc_dst))
    sub_ids = lax.broadcasted_iota(jnp.int32, (slot_total, 2 * events), 0)
    slot_row = jnp.concatenate([row_ref[0:1, :], row_ref[1:2, :]], axis=1)
    placed = (sub_ids == slot_row).astype(jnp.bfloat16)
    both = jnp.concatenate(sent, axis=0)
    out = jnp.dot(placed, both, preferred_element_type=jnp.float32)
    out_ref[...] = out.astype(out_ref.dtype)


def event_messages(
    slot_ids, slot_cols, fetched, edge_part, event_time, time_freq, time_phase, w_msg_in, w_msg_out
):
    slot_total = fetched.shape[0]
    msg_width = w_msg_out.shape[1]
    return pl.pallas_call(
        message_kernel,
        out_shape=jax.ShapeDtypeStruct((slot_total, msg_width), jnp.bfloat16),
    )(
        slot_cols,
        slot_ids,
        fetched,
        edge_part,
        event_time.reshape(-1, 1),
        time_freq.reshape(1, -1),
        time_phase.reshape(1, -1),
        w_msg_in,
        w_msg_out,
    )


def prologue_kernel(
    src_owner_ref, dst_owner_ref, src_row_ref, dst_row_ref, time_ref, slot_ref, slot_t_ref, request_ref
):
    events = src_owner_ref.shape[1]
    owners = 128
    capacity = 8
    slot_total = request_ref.shape[-1]
    chunk = slot_total // owners
    upper = (
        lax.broadcasted_iota(jnp.int32, (events, events), 0)
        < lax.broadcasted_iota(jnp.int32, (events, events), 1)
    ).astype(jnp.bfloat16)
    owner_ids = lax.broadcasted_iota(jnp.int32, (owners, events), 0)
    slots = []
    for side in range(2):
        owner_row = (src_owner_ref, dst_owner_ref)[side][...]
        onehot = owner_ids == owner_row
        earlier = jnp.dot(onehot.astype(jnp.bfloat16), upper, preferred_element_type=jnp.float32)
        position = jnp.sum(jnp.where(onehot, earlier, 0.0), axis=0, keepdims=True)
        slots.append(owner_row * chunk + side * capacity + position.astype(jnp.int32))
    slot_all = jnp.concatenate(slots, axis=1)
    rows_all = jnp.concatenate([src_row_ref[...], dst_row_ref[...]], axis=1)
    times_all = jnp.concatenate([time_ref[...], time_ref[...]], axis=1)
    zero = jnp.zeros_like(rows_all)
    digits = jnp.concatenate(
        [rows_all // 64, rows_all % 64, times_all // 64, times_all % 64, zero + 1, zero, zero, zero],
        axis=0,
    ).astype(jnp.float32)
    stacked = jnp.concatenate([slot_all] + [jnp.zeros_like(slot_all)] * 7, axis=0)
    columns = jnp.transpose(stacked)
    slot_col = columns[:, 0:1]
    lanes = lax.broadcasted_iota(jnp.int32, (2 * events, slot_total), 1)
    placed = (lanes == slot_col).astype(jnp.bfloat16)
    got = jnp.dot(digits.astype(jnp.bfloat16), placed, preferred_element_type=jnp.float32)
    got = got.astype(jnp.int32)
    row_request = jnp.where(got[4:5] > 0, got[0:1] * 64 + got[1:2], -1)
    request_ref[...] = row_request.reshape(request_ref.shape)
    slot_ref[...] = jnp.concatenate(slots, axis=0)
    slot_t_ref[...] = jnp.concatenate([columns[:events, 0:1], columns[events:, 0:1]], axis=1)


def build_requests(src_owner, src_row, dst_owner, dst_row, event_time, slot_total):
    events = src_row.shape[0]
    return pl.pallas_call(
        prologue_kernel,
        out_shape=[
            jax.ShapeDtypeStruct((2, events), jnp.int32),
            jax.ShapeDtypeStruct((events, 2), jnp.int32),
            jax.ShapeDtypeStruct((slot_total,), jnp.int32),
        ],
    )(
        src_owner.reshape(1, events),
        dst_owner.reshape(1, events),
        src_row.reshape(1, events), dst_row.reshape(1, events), event_time.reshape(1, events))


def slot_of(owner_ids, owner_count, capacity):
    events_here = owner_ids.shape[0]
    columns = jnp.arange(owner_count, dtype=jnp.int32)
    onehot = (owner_ids[:, None] == columns[None, :]).astype(jnp.bfloat16)
    order = jnp.arange(events_here, dtype=jnp.int32)
    lower = (order[None, :] < order[:, None]).astype(jnp.bfloat16)
    earlier = jnp.dot(lower, onehot, preferred_element_type=jnp.float32)
    position = jnp.sum(earlier * onehot.astype(jnp.float32), axis=1).astype(jnp.int32)
    return owner_ids * capacity + position


def owner_lookup(row_request, memory, last_update, time_width):
    rows_count, width = memory.shape
    row_range = jnp.arange(rows_count, dtype=jnp.int32)
    select = (row_request[:, None] == row_range[None, :]).astype(jnp.bfloat16)
    digit_cols = jnp.arange(time_width, dtype=jnp.int32)
    digits = jnp.where(
        digit_cols[None, :] == 0,
        last_update[:, None] // 64,
        jnp.where(digit_cols[None, :] == 1, last_update[:, None] % 64, 0),
    ).astype(jnp.bfloat16)
    table = jnp.concatenate([memory, digits], axis=1)
    return jnp.dot(select, table, preferred_element_type=jnp.float32).astype(jnp.bfloat16)


def local(
    src_owner,
    src_row,
    dst_owner,
    dst_row,
    event_time,
    edge_feat,
    memory,
    last_update,
    time_freq,
    time_phase,
    w_msg_in,
    b_msg,
    w_msg_out,
    w_gru_in,
    b_gru_in,
    w_gru_hid,
):
    devices_all = lax.axis_size(("ev", "node"))
    events_here = edge_feat.shape[0]
    capacity = max(2, 2 * events_here // devices_all)
    chunk = 2 * capacity
    width = memory.shape[1]
    time_width = time_freq.shape[0]
    slot_total = devices_all * chunk
    slot_ids, slot_cols, request = build_requests(
        src_owner, src_row, dst_owner, dst_row, event_time, slot_total
    )
    request = request.reshape(slot_total)
    edge_part = (
        jnp.dot(edge_feat, w_msg_in[2 * width + time_width :], preferred_element_type=jnp.float32)
        + b_msg
    )
    rows_held = lax.all_to_all(request, ("ev", "node"), split_axis=0, concat_axis=0, tiled=True)
    served = owner_lookup(rows_held, memory, last_update, time_width)
    returned = lax.all_to_all(served, ("ev", "node"), split_axis=0, concat_axis=0, tiled=True)
    outgoing = event_messages(
        slot_ids, slot_cols, returned, edge_part, event_time, time_freq, time_phase, w_msg_in, w_msg_out
    )
    arrived = lax.all_to_all(outgoing, ("ev", "node"), split_axis=0, concat_axis=0, tiled=True)
    return owner_update(rows_held, arrived, memory, w_gru_in, b_gru_in, w_gru_hid)


def solution(mesh):
    in_specs = (
        P(("ev", "node"), None),
        P(("ev", "node")),
        P(("ev", "node"), None),
        P(("ev", "node")),
        P(("ev", "node")),
        P(("ev", "node"), None),
        P(("ev", "node"), None),
        P(("ev", "node")),
        P(),
        P(),
        P(),
        P(),
        P(),
        P(),
        P(),
        P(),
    )
    out_specs = P(("ev", "node"), None)
    return jax.shard_map(local, mesh=mesh, in_specs=in_specs, out_specs=out_specs, check_vma=False)
```

```python
import jax
import jax.numpy as jnp
from jax import lax
from jax.experimental import pallas as pl
from jax.sharding import PartitionSpec as P


def encode(delta_int, time_freq, time_phase):
    delta = delta_int.astype(jnp.float32)
    return jnp.cos(delta[..., None] * time_freq + time_phase).astype(jnp.bfloat16)


def gru_update(mean_msg, state, w_gru_in, b_gru_in, w_gru_hid):
    width = state.shape[-1]
    input_part = jnp.dot(mean_msg, w_gru_in, preferred_element_type=jnp.float32) + b_gru_in
    state_part = jnp.dot(state, w_gru_hid, preferred_element_type=jnp.float32)
    reset = jax.nn.sigmoid(input_part[:, :width] + state_part[:, :width])
    update = jax.nn.sigmoid(input_part[:, width : 2 * width] + state_part[:, width : 2 * width])
    candid = jnp.tanh(input_part[:, 2 * width :] + reset * state_part[:, 2 * width :])
    return ((1.0 - update) * candid + update * state.astype(jnp.float32)).astype(jnp.bfloat16)


def gate(x):
    return 0.5 + 0.5 * jnp.tanh(0.5 * x)


def update_kernel(rows_ref, msg_ref, mem_ref, win_ref, bin_ref, whid_ref, out_ref):
    block = out_ref.shape[0]
    slots = rows_ref.shape[1]
    width = mem_ref.shape[1]
    ids = lax.broadcasted_iota(jnp.int32, (block, slots), 0)
    onehot = (ids == rows_ref[...] - pl.program_id(0) * block).astype(jnp.bfloat16)
    total = jnp.dot(onehot, msg_ref[...], preferred_element_type=jnp.float32)
    ones = jnp.ones((slots, 128), jnp.bfloat16)
    count = jnp.dot(onehot, ones, preferred_element_type=jnp.float32)[:, :1]
    mean_msg = (total / jnp.maximum(count, 1.0)).astype(jnp.bfloat16)
    state = mem_ref[...]
    input_part = jnp.dot(mean_msg, win_ref[...], preferred_element_type=jnp.float32) + bin_ref[...]
    state_part = jnp.dot(state, whid_ref[...], preferred_element_type=jnp.float32)
    reset = gate(input_part[:, :width] + state_part[:, :width])
    update = gate(input_part[:, width : 2 * width] + state_part[:, width : 2 * width])
    candid = jnp.tanh(input_part[:, 2 * width :] + reset * state_part[:, 2 * width :])
    fresh = (1.0 - update) * candid + update * state.astype(jnp.float32)
    out_ref[...] = jnp.where(count > 0, fresh, state.astype(jnp.float32)).astype(out_ref.dtype)


def owner_update(row_flat, msg_flat, memory, w_gru_in, b_gru_in, w_gru_hid):
    rows_count, width = memory.shape
    slots, msg_width = msg_flat.shape
    block = 1024
    gates = w_gru_in.shape[1]
    return pl.pallas_call(
        update_kernel,
        grid=(rows_count // block,),
        in_specs=[
            pl.BlockSpec((1, slots), lambda i: (0, 0)),
            pl.BlockSpec((slots, msg_width), lambda i: (0, 0)),
            pl.BlockSpec((block, width), lambda i: (i, 0)),
            pl.BlockSpec((msg_width, gates), lambda i: (0, 0)),
            pl.BlockSpec((1, gates), lambda i: (0, 0)),
            pl.BlockSpec((width, gates), lambda i: (0, 0)),
        ],
        out_specs=pl.BlockSpec((block, width), lambda i: (i, 0)),
        out_shape=jax.ShapeDtypeStruct(memory.shape, memory.dtype),
    )(row_flat.reshape(1, slots), msg_flat, memory, w_gru_in, b_gru_in.reshape(1, gates), w_gru_hid)


def message_kernel(
    col_ref, row_ref, fetched_ref, edge_ref, time_ref, freq_ref, phase_ref, w_in_ref, w_out_ref, out_ref
):
    events = edge_ref.shape[0]
    slot_total = fetched_ref.shape[0]
    width = out_ref.shape[1]
    time_width = fetched_ref.shape[1] - width
    lane_ids = lax.broadcasted_iota(jnp.int32, (events, slot_total), 1)
    picked = []
    for side in range(2):
        pick = (lane_ids == col_ref[:, side : side + 1]).astype(jnp.bfloat16)
        rows = jnp.dot(pick, fetched_ref[...], preferred_element_type=jnp.float32)
        stamp = rows[:, width : width + 1].astype(jnp.int32) * 64
        stamp = stamp + rows[:, width + 1 : width + 2].astype(jnp.int32)
        delta = (time_ref[...] - stamp).astype(jnp.float32)
        encoded = jnp.cos(delta * freq_ref[...] + phase_ref[...]).astype(jnp.bfloat16)
        picked.append((rows[:, :width].astype(jnp.bfloat16), encoded))
    mem_src, enc_src = picked[0]
    mem_dst, enc_dst = picked[1]
    w_self = w_in_ref[:width]
    w_other = w_in_ref[width : 2 * width]
    w_time = w_in_ref[2 * width : 2 * width + time_width]
    edge = edge_ref[...]

    def message(own, other, enc):
        hidden = (
            jnp.dot(own, w_self, preferred_element_type=jnp.float32)
            + jnp.dot(other, w_other, preferred_element_type=jnp.float32)
            + jnp.dot(enc, w_time, preferred_element_type=jnp.float32)
            + edge
        )
        hidden = jnp.maximum(hidden, 0.0).astype(jnp.bfloat16)
        return jnp.dot(hidden, w_out_ref[...], preferred_element_type=jnp.float32).astype(jnp.bfloat16)

    sent = (message(mem_src, mem_dst, enc_src), message(mem_dst, mem_src, enc_dst))
    sub_ids = lax.broadcasted_iota(jnp.int32, (slot_total, events), 0)
    placed = [(sub_ids == row_ref[side : side + 1, :]).astype(jnp.bfloat16) for side in range(2)]
    out = jnp.dot(placed[0], sent[0], preferred_element_type=jnp.float32)
    out = out + jnp.dot(placed[1], sent[1], preferred_element_type=jnp.float32)
    out_ref[...] = out.astype(out_ref.dtype)


def event_messages(
    slot_ids, slot_cols, fetched, edge_part, event_time, time_freq, time_phase, w_msg_in, w_msg_out
):
    slot_total = fetched.shape[0]
    msg_width = w_msg_out.shape[1]
    return pl.pallas_call(
        message_kernel,
        out_shape=jax.ShapeDtypeStruct((slot_total, msg_width), jnp.bfloat16),
    )(
        slot_cols,
        slot_ids,
        fetched,
        edge_part,
        event_time.reshape(-1, 1),
        time_freq.reshape(1, -1),
        time_phase.reshape(1, -1),
        w_msg_in,
        w_msg_out,
    )


def prologue_kernel(
    src_owner_ref, dst_owner_ref, src_row_ref, dst_row_ref, time_ref, slot_ref, slot_t_ref, request_ref
):
    events = src_owner_ref.shape[1]
    owners = 128
    capacity = 8
    slot_total = request_ref.shape[-1]
    chunk = slot_total // owners
    upper = (
        lax.broadcasted_iota(jnp.int32, (events, events), 0)
        < lax.broadcasted_iota(jnp.int32, (events, events), 1)
    ).astype(jnp.bfloat16)
    owner_ids = lax.broadcasted_iota(jnp.int32, (owners, events), 0)
    slots = []
    for side in range(2):
        owner_row = (src_owner_ref, dst_owner_ref)[side][...]
        onehot = owner_ids == owner_row
        earlier = jnp.dot(onehot.astype(jnp.bfloat16), upper, preferred_element_type=jnp.float32)
        position = jnp.sum(jnp.where(onehot, earlier, 0.0), axis=0, keepdims=True)
        slots.append(owner_row * chunk + side * capacity + position.astype(jnp.int32))
    slot_all = jnp.concatenate(slots, axis=1)
    rows_all = jnp.concatenate([src_row_ref[...], dst_row_ref[...]], axis=1)
    times_all = jnp.concatenate([time_ref[...], time_ref[...]], axis=1)
    zero = jnp.zeros_like(rows_all)
    digits = jnp.concatenate(
        [rows_all // 64, rows_all % 64, times_all // 64, times_all % 64, zero + 1, zero, zero, zero],
        axis=0,
    ).astype(jnp.float32)
    stacked = jnp.concatenate([slot_all] + [jnp.zeros_like(slot_all)] * 7, axis=0)
    columns = jnp.transpose(stacked)
    slot_col = columns[:, 0:1]
    lanes = lax.broadcasted_iota(jnp.int32, (2 * events, slot_total), 1)
    placed = (lanes == slot_col).astype(jnp.bfloat16)
    got = jnp.dot(digits.astype(jnp.bfloat16), placed, preferred_element_type=jnp.float32)
    got = got.astype(jnp.int32)
    row_request = jnp.where(got[4:5] > 0, got[0:1] * 64 + got[1:2], -1)
    request_ref[...] = row_request.reshape(request_ref.shape)
    slot_ref[...] = jnp.concatenate(slots, axis=0)
    slot_t_ref[...] = jnp.concatenate([columns[:events, 0:1], columns[events:, 0:1]], axis=1)


def build_requests(src_owner, src_row, dst_owner, dst_row, event_time, slot_total):
    events = src_row.shape[0]
    return pl.pallas_call(
        prologue_kernel,
        out_shape=[
            jax.ShapeDtypeStruct((2, events), jnp.int32),
            jax.ShapeDtypeStruct((events, 2), jnp.int32),
            jax.ShapeDtypeStruct((slot_total,), jnp.int32),
        ],
    )(
        src_owner.reshape(1, events),
        dst_owner.reshape(1, events),
        src_row.reshape(1, events), dst_row.reshape(1, events), event_time.reshape(1, events))


def slot_of(owner_ids, owner_count, capacity):
    events_here = owner_ids.shape[0]
    columns = jnp.arange(owner_count, dtype=jnp.int32)
    onehot = (owner_ids[:, None] == columns[None, :]).astype(jnp.bfloat16)
    order = jnp.arange(events_here, dtype=jnp.int32)
    lower = (order[None, :] < order[:, None]).astype(jnp.bfloat16)
    earlier = jnp.dot(lower, onehot, preferred_element_type=jnp.float32)
    position = jnp.sum(earlier * onehot.astype(jnp.float32), axis=1).astype(jnp.int32)
    return owner_ids * capacity + position


def owner_lookup(row_request, memory, last_update, time_width):
    rows_count, width = memory.shape
    row_range = jnp.arange(rows_count, dtype=jnp.int32)
    select = (row_request[:, None] == row_range[None, :]).astype(jnp.bfloat16)
    digit_cols = jnp.arange(time_width, dtype=jnp.int32)
    digits = jnp.where(
        digit_cols[None, :] == 0,
        last_update[:, None] // 64,
        jnp.where(digit_cols[None, :] == 1, last_update[:, None] % 64, 0),
    ).astype(jnp.bfloat16)
    table = jnp.concatenate([memory, digits], axis=1)
    return jnp.dot(select, table, preferred_element_type=jnp.float32).astype(jnp.bfloat16)


def local(
    src_owner,
    src_row,
    dst_owner,
    dst_row,
    event_time,
    edge_feat,
    memory,
    last_update,
    time_freq,
    time_phase,
    w_msg_in,
    b_msg,
    w_msg_out,
    w_gru_in,
    b_gru_in,
    w_gru_hid,
):
    devices_all = lax.axis_size(("ev", "node"))
    events_here = edge_feat.shape[0]
    capacity = max(2, 2 * events_here // devices_all)
    chunk = 2 * capacity
    width = memory.shape[1]
    time_width = time_freq.shape[0]
    slot_total = devices_all * chunk
    slot_ids, slot_cols, request = build_requests(
        src_owner, src_row, dst_owner, dst_row, event_time, slot_total
    )
    request = request.reshape(slot_total)
    edge_part = (
        jnp.dot(edge_feat, w_msg_in[2 * width + time_width :], preferred_element_type=jnp.float32)
        + b_msg
    )
    rows_held = lax.all_to_all(request, ("ev", "node"), split_axis=0, concat_axis=0, tiled=True)
    served = owner_lookup(rows_held, memory, last_update, time_width)
    returned = lax.all_to_all(served, ("ev", "node"), split_axis=0, concat_axis=0, tiled=True)
    outgoing = event_messages(
        slot_ids, slot_cols, returned, edge_part, event_time, time_freq, time_phase, w_msg_in, w_msg_out
    )
    arrived = lax.all_to_all(outgoing, ("ev", "node"), split_axis=0, concat_axis=0, tiled=True)
    return owner_update(rows_held, arrived, memory, w_gru_in, b_gru_in, w_gru_hid)


def solution(mesh):
    in_specs = (
        P(("ev", "node"), None),
        P(("ev", "node")),
        P(("ev", "node"), None),
        P(("ev", "node")),
        P(("ev", "node")),
        P(("ev", "node"), None),
        P(("ev", "node"), None),
        P(("ev", "node")),
        P(),
        P(),
        P(),
        P(),
        P(),
        P(),
        P(),
        P(),
    )
    out_specs = P(("ev", "node"), None)
    return jax.shard_map(local, mesh=mesh, in_specs=in_specs, out_specs=out_specs, check_vma=False)
```

```python
import jax
import jax.numpy as jnp
from jax import lax
from jax.experimental import pallas as pl
from jax.sharding import PartitionSpec as P


def encode(delta_int, time_freq, time_phase):
    delta = delta_int.astype(jnp.float32)
    return jnp.cos(delta[..., None] * time_freq + time_phase).astype(jnp.bfloat16)


def gru_update(mean_msg, state, w_gru_in, b_gru_in, w_gru_hid):
    width = state.shape[-1]
    input_part = jnp.dot(mean_msg, w_gru_in, preferred_element_type=jnp.float32) + b_gru_in
    state_part = jnp.dot(state, w_gru_hid, preferred_element_type=jnp.float32)
    reset = jax.nn.sigmoid(input_part[:, :width] + state_part[:, :width])
    update = jax.nn.sigmoid(input_part[:, width : 2 * width] + state_part[:, width : 2 * width])
    candid = jnp.tanh(input_part[:, 2 * width :] + reset * state_part[:, 2 * width :])
    return ((1.0 - update) * candid + update * state.astype(jnp.float32)).astype(jnp.bfloat16)


def gate(x):
    return 0.5 + 0.5 * jnp.tanh(0.5 * x)


def update_kernel(rows_ref, msg_ref, mem_ref, win_ref, bin_ref, whid_ref, out_ref):
    block = out_ref.shape[0]
    slots = rows_ref.shape[1]
    width = mem_ref.shape[1]
    ids = pl.program_id(0) * block + lax.broadcasted_iota(jnp.int32, (block, slots), 0)
    onehot = (ids == rows_ref[...]).astype(jnp.bfloat16)
    total = jnp.dot(onehot, msg_ref[...], preferred_element_type=jnp.float32)
    ones = jnp.ones((slots, 128), jnp.bfloat16)
    count = jnp.dot(onehot, ones, preferred_element_type=jnp.float32)[:, :1]
    mean_msg = (total / jnp.maximum(count, 1.0)).astype(jnp.bfloat16)
    state = mem_ref[...]
    input_part = jnp.dot(mean_msg, win_ref[...], preferred_element_type=jnp.float32) + bin_ref[...]
    state_part = jnp.dot(state, whid_ref[...], preferred_element_type=jnp.float32)
    reset = gate(input_part[:, :width] + state_part[:, :width])
    update = gate(input_part[:, width : 2 * width] + state_part[:, width : 2 * width])
    candid = jnp.tanh(input_part[:, 2 * width :] + reset * state_part[:, 2 * width :])
    fresh = (1.0 - update) * candid + update * state.astype(jnp.float32)
    out_ref[...] = jnp.where(count > 0, fresh, state.astype(jnp.float32)).astype(out_ref.dtype)


def owner_update(row_flat, msg_flat, memory, w_gru_in, b_gru_in, w_gru_hid):
    rows_count, width = memory.shape
    slots, msg_width = msg_flat.shape
    block = 1024
    gates = w_gru_in.shape[1]
    return pl.pallas_call(
        update_kernel,
        grid=(rows_count // block,),
        in_specs=[
            pl.BlockSpec((1, slots), lambda i: (0, 0)),
            pl.BlockSpec((slots, msg_width), lambda i: (0, 0)),
            pl.BlockSpec((block, width), lambda i: (i, 0)),
            pl.BlockSpec((msg_width, gates), lambda i: (0, 0)),
            pl.BlockSpec((1, gates), lambda i: (0, 0)),
            pl.BlockSpec((width, gates), lambda i: (0, 0)),
        ],
        out_specs=pl.BlockSpec((block, width), lambda i: (i, 0)),
        out_shape=jax.ShapeDtypeStruct(memory.shape, memory.dtype),
    )(row_flat.reshape(1, slots), msg_flat, memory, w_gru_in, b_gru_in.reshape(1, gates), w_gru_hid)


def message_kernel(
    col_ref, row_ref, fetched_ref, edge_ref, time_ref, freq_ref, phase_ref, w_in_ref, w_out_ref, out_ref
):
    events = edge_ref.shape[0]
    slot_total = fetched_ref.shape[0]
    width = out_ref.shape[1]
    time_width = fetched_ref.shape[1] - width
    lane_ids = lax.broadcasted_iota(jnp.int32, (2 * events, slot_total), 1)
    slot_col = jnp.concatenate([col_ref[:, 0:1], col_ref[:, 1:2]], axis=0)
    pick = (lane_ids == slot_col).astype(jnp.bfloat16)
    rows_both = jnp.dot(pick, fetched_ref[...], preferred_element_type=jnp.float32)
    picked = []
    for side in range(2):
        rows = rows_both[side * events : (side + 1) * events]
        stamp = rows[:, width : width + 1].astype(jnp.int32) * 64
        stamp = stamp + rows[:, width + 1 : width + 2].astype(jnp.int32)
        delta = (time_ref[...] - stamp).astype(jnp.float32)
        encoded = jnp.cos(delta * freq_ref[...] + phase_ref[...]).astype(jnp.bfloat16)
        picked.append((rows[:, :width].astype(jnp.bfloat16), encoded))
    mem_src, enc_src = picked[0]
    mem_dst, enc_dst = picked[1]
    w_self = w_in_ref[:width]
    w_other = w_in_ref[width : 2 * width]
    w_time = w_in_ref[2 * width : 2 * width + time_width]
    edge = edge_ref[...]

    def message(own, other, enc):
        hidden = (
            jnp.dot(own, w_self, preferred_element_type=jnp.float32)
            + jnp.dot(other, w_other, preferred_element_type=jnp.float32)
            + jnp.dot(enc, w_time, preferred_element_type=jnp.float32)
            + edge
        )
        hidden = jnp.maximum(hidden, 0.0).astype(jnp.bfloat16)
        return jnp.dot(hidden, w_out_ref[...], preferred_element_type=jnp.float32).astype(jnp.bfloat16)

    sent = (message(mem_src, mem_dst, enc_src), message(mem_dst, mem_src, enc_dst))
    sub_ids = lax.broadcasted_iota(jnp.int32, (slot_total, events), 0)
    placed = [(sub_ids == row_ref[side : side + 1, :]).astype(jnp.bfloat16) for side in range(2)]
    out = jnp.dot(placed[0], sent[0], preferred_element_type=jnp.float32)
    out = out + jnp.dot(placed[1], sent[1], preferred_element_type=jnp.float32)
    out_ref[...] = out.astype(out_ref.dtype)


def event_messages(
    slot_ids, slot_cols, fetched, edge_part, event_time, time_freq, time_phase, w_msg_in, w_msg_out
):
    slot_total = fetched.shape[0]
    msg_width = w_msg_out.shape[1]
    return pl.pallas_call(
        message_kernel,
        out_shape=jax.ShapeDtypeStruct((slot_total, msg_width), jnp.bfloat16),
    )(
        slot_cols,
        slot_ids,
        fetched,
        edge_part,
        event_time.reshape(-1, 1),
        time_freq.reshape(1, -1),
        time_phase.reshape(1, -1),
        w_msg_in,
        w_msg_out,
    )


def prologue_kernel(
    src_owner_ref, dst_owner_ref, src_row_ref, dst_row_ref, time_ref, slot_ref, slot_t_ref, request_ref
):
    events = src_owner_ref.shape[1]
    owners = 128
    capacity = 8
    slot_total = request_ref.shape[-1]
    chunk = slot_total // owners
    upper = (
        lax.broadcasted_iota(jnp.int32, (events, events), 0)
        < lax.broadcasted_iota(jnp.int32, (events, events), 1)
    ).astype(jnp.bfloat16)
    owner_ids = lax.broadcasted_iota(jnp.int32, (owners, events), 0)
    slots = []
    for side in range(2):
        owner_row = (src_owner_ref, dst_owner_ref)[side][...]
        onehot = owner_ids == owner_row
        earlier = jnp.dot(onehot.astype(jnp.bfloat16), upper, preferred_element_type=jnp.float32)
        position = jnp.sum(jnp.where(onehot, earlier, 0.0), axis=0, keepdims=True)
        slots.append(owner_row * chunk + side * capacity + position.astype(jnp.int32))
    slot_all = jnp.concatenate(slots, axis=1)
    rows_all = jnp.concatenate([src_row_ref[...], dst_row_ref[...]], axis=1)
    times_all = jnp.concatenate([time_ref[...], time_ref[...]], axis=1)
    zero = jnp.zeros_like(rows_all)
    digits = jnp.concatenate(
        [rows_all // 64, rows_all % 64, times_all // 64, times_all % 64, zero + 1, zero, zero, zero],
        axis=0,
    ).astype(jnp.float32)
    stacked = jnp.concatenate([slot_all] + [jnp.zeros_like(slot_all)] * 7, axis=0)
    columns = jnp.transpose(stacked)
    slot_col = columns[:, 0:1]
    lanes = lax.broadcasted_iota(jnp.int32, (2 * events, slot_total), 1)
    placed = (lanes == slot_col).astype(jnp.bfloat16)
    got = jnp.dot(digits.astype(jnp.bfloat16), placed, preferred_element_type=jnp.float32)
    got = got.astype(jnp.int32)
    row_request = jnp.where(got[4:5] > 0, got[0:1] * 64 + got[1:2], -1)
    request_ref[...] = row_request.reshape(request_ref.shape)
    slot_ref[...] = jnp.concatenate(slots, axis=0)
    slot_t_ref[...] = jnp.concatenate([columns[:events, 0:1], columns[events:, 0:1]], axis=1)


def build_requests(src_owner, src_row, dst_owner, dst_row, event_time, slot_total):
    events = src_row.shape[0]
    return pl.pallas_call(
        prologue_kernel,
        out_shape=[
            jax.ShapeDtypeStruct((2, events), jnp.int32),
            jax.ShapeDtypeStruct((events, 2), jnp.int32),
            jax.ShapeDtypeStruct((slot_total,), jnp.int32),
        ],
    )(
        src_owner.reshape(1, events),
        dst_owner.reshape(1, events),
        src_row.reshape(1, events), dst_row.reshape(1, events), event_time.reshape(1, events))


def slot_of(owner_ids, owner_count, capacity):
    events_here = owner_ids.shape[0]
    columns = jnp.arange(owner_count, dtype=jnp.int32)
    onehot = (owner_ids[:, None] == columns[None, :]).astype(jnp.bfloat16)
    order = jnp.arange(events_here, dtype=jnp.int32)
    lower = (order[None, :] < order[:, None]).astype(jnp.bfloat16)
    earlier = jnp.dot(lower, onehot, preferred_element_type=jnp.float32)
    position = jnp.sum(earlier * onehot.astype(jnp.float32), axis=1).astype(jnp.int32)
    return owner_ids * capacity + position


def owner_lookup(row_request, memory, last_update, time_width):
    rows_count, width = memory.shape
    row_range = jnp.arange(rows_count, dtype=jnp.int32)
    select = (row_request[:, None] == row_range[None, :]).astype(jnp.bfloat16)
    digit_cols = jnp.arange(time_width, dtype=jnp.int32)
    digits = jnp.where(
        digit_cols[None, :] == 0,
        last_update[:, None] // 64,
        jnp.where(digit_cols[None, :] == 1, last_update[:, None] % 64, 0),
    ).astype(jnp.bfloat16)
    table = jnp.concatenate([memory, digits], axis=1)
    return jnp.dot(select, table, preferred_element_type=jnp.float32).astype(jnp.bfloat16)


def local(
    src_owner,
    src_row,
    dst_owner,
    dst_row,
    event_time,
    edge_feat,
    memory,
    last_update,
    time_freq,
    time_phase,
    w_msg_in,
    b_msg,
    w_msg_out,
    w_gru_in,
    b_gru_in,
    w_gru_hid,
):
    devices_all = lax.axis_size(("ev", "node"))
    events_here = edge_feat.shape[0]
    capacity = max(2, 2 * events_here // devices_all)
    chunk = 2 * capacity
    width = memory.shape[1]
    time_width = time_freq.shape[0]
    slot_total = devices_all * chunk
    slot_ids, slot_cols, request = build_requests(
        src_owner, src_row, dst_owner, dst_row, event_time, slot_total
    )
    request = request.reshape(slot_total)
    edge_part = (
        jnp.dot(edge_feat, w_msg_in[2 * width + time_width :], preferred_element_type=jnp.float32)
        + b_msg
    )
    rows_held = lax.all_to_all(request, ("ev", "node"), split_axis=0, concat_axis=0, tiled=True)
    served = owner_lookup(rows_held, memory, last_update, time_width)
    returned = lax.all_to_all(served, ("ev", "node"), split_axis=0, concat_axis=0, tiled=True)
    outgoing = event_messages(
        slot_ids, slot_cols, returned, edge_part, event_time, time_freq, time_phase, w_msg_in, w_msg_out
    )
    arrived = lax.all_to_all(outgoing, ("ev", "node"), split_axis=0, concat_axis=0, tiled=True)
    return owner_update(rows_held, arrived, memory, w_gru_in, b_gru_in, w_gru_hid)


def solution(mesh):
    in_specs = (
        P(("ev", "node"), None),
        P(("ev", "node")),
        P(("ev", "node"), None),
        P(("ev", "node")),
        P(("ev", "node")),
        P(("ev", "node"), None),
        P(("ev", "node"), None),
        P(("ev", "node")),
        P(),
        P(),
        P(),
        P(),
        P(),
        P(),
        P(),
        P(),
    )
    out_specs = P(("ev", "node"), None)
    return jax.shard_map(local, mesh=mesh, in_specs=in_specs, out_specs=out_specs, check_vma=False)
```
